32 devices in a mesh: groups: 2 (over x), batch: 4 (over z), head: 4 (over y, core).
Axes of the slice: x: 2, y: 2, z: 4, core: 2. Of those that a mesh axis runs over, the one named last changes fastest.
Arguments:
- tier_feed_tensor: bfloat16 [4, 64, 4096], P(None, 'groups', 'batch'), parts along dimension 1, may hold values from -6 to 6
- preceding_feed_each_stream: bfloat16 [64, 4096], P('groups', 'batch'), parts along dimension 0, may hold values from -6 to 6
- stream_kept_tableaux: float32 [64, 64, 4096], P(('groups', 'batch'), 'head'), parts along dimension 0, may hold values from -6 to 6
- position_mapping_target: int32 [64], P('groups'), parts along dimension 0, may hold values from 0 to 31, as said below
- lagging_mixture_weights: float32 [6, 4096], P(None, 'batch'), may hold values from 0 to 1
- lagging_narrow_lowering: bfloat16 [4096, 320], P('batch'), may hold values from -0.09375 to 0.09375
- lagging_narrow_raising: bfloat16 [5, 64, 4096], P(None, None, 'batch'), may hold values from -0.75 to 0.75
- fourfold_linear_maps: bfloat16 [4, 4096, 4096], P(None, 'batch', 'head'), may hold values from -0.09375 to 0.09375
- attenuation_narrow_lowering: bfloat16 [4096, 128], P('batch'), may hold values from -0.09375 to 0.09375
- attenuation_narrow_raising: bfloat16 [128, 4096], P(None, 'head'), may hold values from -0.5 to 0.5
- attenuation_doublelog_anchor: float32 [4096], P('head'), may hold values from -6 to 1
- instant_premium: float32 [4096], P('head'), may hold values from -4 to 4
- norming_multiplier: float32 [4096], P('head'), may hold values from 0.5 to 1.5
- norming_intercept: float32 [4096], P('head'), may hold values from -3 to 3
- outgoing_linear_map: bfloat16 [4096, 4096], P('head', 'batch'), may hold values from -0.09375 to 0.09375
Outputs:
- y_first: bfloat16 [2, 64, 4096], P(None, ('groups', 'head'), 'batch'), parts along dimension 1
- y_second: bfloat16 [2, 64, 4096], P(None, ('groups', 'head'), 'batch'), parts along dimension 1
- final_state: float32 [256, 16, 4096], P(('groups', 'batch', 'head')), parts along dimension 0
The draws below stay inside these ranges and needn't reach their ends.
There are 2 independent parts, one for each index of `groups`. The reference program is written for one: setup_inputs(seed, part) draws one part's arguments, and reference() takes and returns one part's arrays. A program takes and returns all parts, laid end to end along the dimension named above; an argument that names none is the same for every part. Nothing has to cross between parts.
Inputs may be any that keep to these rules, and one draw needn't show every extreme that they name: position_mapping_target is a permutation of 0 to 31. For every aligned block of 8 sessions and every aligned block of 8 slots, the number of sessions of the former that have slots in the latter is exactly 2.
All inputs are finite; a program needn't handle non-finite values.
Results may differ from the reference program's by a relative error of at most 0.035.
Values may be sent and summed in bfloat16 or wider, within the bound.
No kernel may reach another device: no remote copies, remote signals or barrier semaphores. Data moves between devices by JAX's collectives and lax.ppermute only.
A program may use at most 128 MiB of HBM per device.

```python
import jax
import jax.numpy as jnp
from jax import lax

HIDDEN_BREADTH = 4096
HEADCOUNT_TOTALS = 64
SUBSPACE_EXTENT = 64
MIXR = 64
DECR = 128
R = 8
STEPS_A = 2
STEPS_B = 2
SUBS = 1
SB = 8
SESS = 32
FB = 1024
HQ = 4
HG = 16
FEATURE_BREADTH = 4096
OUT_ROWS = 128


def draw_position_mapping_target(key, part):
    block_count = SESS // SB
    per_pair = R // block_count
    first_key = jax.random.fold_in(key, 11)
    second_key = jax.random.fold_in(key, 12)
    within = jax.vmap(lambda sub_key: jax.random.permutation(sub_key, SB))(jax.random.split(first_key, block_count)).astype(jnp.int32)
    target = within // per_pair
    ranking = within % per_pair
    shuffle = jax.vmap(lambda sub_key: jax.random.permutation(sub_key, R))(jax.random.split(second_key, block_count * SUBS)).astype(jnp.int32)
    source = jnp.arange(block_count, dtype=jnp.int32)[:, None]
    column = source * per_pair + ranking
    slot_index = target * R + shuffle[target, column]
    return slot_index.reshape(SESS).astype(jnp.int32)


def levels(key, dims, shards, least, top_value):
    level, own = 1.0, jax.random.fold_in(key, 6)
    for position, parts in shards:
        steps = jnp.exp(jax.random.uniform(jax.random.fold_in(own, position), (parts,), jnp.float32, least / len(shards), top_value / len(shards)))
        level = level * jnp.repeat(steps, dims[position] // parts).reshape([-1 if axis == position else 1 for axis in range(len(dims))])
    return level


def scatter_about(key, extent, scale, most, cuts=(), held_as=jnp.bfloat16):
    level = levels(key, extent, cuts, -0.22, 0.18) if cuts else 1.0
    entries = jax.random.normal(key, extent, jnp.float32) * scale * level
    return jnp.minimum(jnp.maximum(entries, -most), most).astype(held_as)


def setup_inputs(seed: int = 0, part: int = 0) -> dict:
    splits = jax.random.split(jax.random.key(seed), 16)
    part_keys = jax.random.split(jax.random.fold_in(splits[15], part), 16)
    tier_feed_tensor = scatter_about(part_keys[0], (STEPS_A + STEPS_B, SESS, HIDDEN_BREADTH), 1.0, 6.0, ((2, 4),))
    preceding_feed_each_stream = scatter_about(part_keys[1], (SESS, HIDDEN_BREADTH), 1.0, 6.0, ((1, 4),))
    stream_kept_tableaux = scatter_about(part_keys[2], (SESS, HEADCOUNT_TOTALS, SUBSPACE_EXTENT * SUBSPACE_EXTENT), 1.0, 6.0, ((0, 4), (1, 4)), jnp.float32)
    position_mapping_target = draw_position_mapping_target(jax.random.fold_in(jax.random.fold_in(splits[15], part), 71), part)
    lagging_mixture_weights = jnp.clip(1.0 * jax.random.uniform(splits[4], (6, HIDDEN_BREADTH), jnp.float32) ** levels(splits[4], (6, HIDDEN_BREADTH), ((1, 4),), -0.2, 0.2), 0.0, 1.0)
    lagging_narrow_lowering = scatter_about(splits[5], (HIDDEN_BREADTH, 5 * MIXR), HIDDEN_BREADTH ** -0.5, 0.09375, ((0, 4),))
    lagging_narrow_raising = scatter_about(splits[6], (5, MIXR, HIDDEN_BREADTH), MIXR ** -0.5, 0.75, ((2, 4),))
    fourfold_linear_maps = scatter_about(splits[7], (4, HIDDEN_BREADTH, FEATURE_BREADTH), HIDDEN_BREADTH ** -0.5, 0.09375, ((1, 4), (2, 4)))
    attenuation_narrow_lowering = scatter_about(splits[8], (HIDDEN_BREADTH, DECR), HIDDEN_BREADTH ** -0.5, 0.09375, ((0, 4),))
    attenuation_narrow_raising = scatter_about(splits[9], (DECR, FEATURE_BREADTH), DECR ** -0.5, 0.5, ((1, 4),))
    attenuation_doublelog_anchor = jnp.clip(-6.0 + 7.0 * jax.random.uniform(splits[10], (FEATURE_BREADTH,), jnp.float32) ** levels(splits[10], (FEATURE_BREADTH,), ((0, 4),), -0.2, 0.2), -6.0, 1.0)
    instant_premium = scatter_about(splits[11], (FEATURE_BREADTH,), 1.0, 4.0, ((0, 4),), jnp.float32)
    norming_multiplier = jnp.clip(0.5 + 1.0 * jax.random.uniform(splits[12], (FEATURE_BREADTH,), jnp.float32) ** levels(splits[12], (FEATURE_BREADTH,), ((0, 4),), -0.2, 0.2), 0.5, 1.5)
    norming_intercept = scatter_about(splits[13], (FEATURE_BREADTH,), 0.5, 3.0, ((0, 4),), jnp.float32)
    outgoing_linear_map = scatter_about(splits[14], (FEATURE_BREADTH, HIDDEN_BREADTH), FEATURE_BREADTH ** -0.5, 0.09375, ((0, 4), (1, 4)))
    return {"tier_feed_tensor": tier_feed_tensor, "preceding_feed_each_stream": preceding_feed_each_stream, "stream_kept_tableaux": stream_kept_tableaux, "position_mapping_target": position_mapping_target, "lagging_mixture_weights": lagging_mixture_weights, "lagging_narrow_lowering": lagging_narrow_lowering, "lagging_narrow_raising": lagging_narrow_raising, "fourfold_linear_maps": fourfold_linear_maps, "attenuation_narrow_lowering": attenuation_narrow_lowering, "attenuation_narrow_raising": attenuation_narrow_raising, "attenuation_doublelog_anchor": attenuation_doublelog_anchor, "instant_premium": instant_premium, "norming_multiplier": norming_multiplier, "norming_intercept": norming_intercept, "outgoing_linear_map": outgoing_linear_map}


NORMALIZER_GUARD = 0.00064

def block_sums(inputs, weight):
    line_tally = inputs.shape[0]
    columns = weight.shape[1]
    block_terms = jnp.einsum('nbf,bfc->nbc', inputs.reshape(line_tally, HIDDEN_BREADTH // FB, FB).astype(jnp.float32), weight.reshape(HIDDEN_BREADTH // FB, FB, columns).astype(jnp.float32))
    rounded = lax.optimization_barrier(block_terms.astype(jnp.bfloat16))
    return lax.optimization_barrier(jnp.sum(rounded.astype(jnp.float32), axis=1))

def widen(value):
    return lax.optimization_barrier(value.astype(jnp.bfloat16)).astype(jnp.float32)

def infer_lone_position(position_pieces, preceding_feed, kept_outer_tableau, lagging_mixture_weights, lagging_narrow_lowering, lagging_narrow_raising, fourfold_linear_maps, attenuation_narrow_lowering, attenuation_narrow_raising, attenuation_doublelog_anchor, instant_premium, norming_multiplier, norming_intercept, outgoing_linear_map):
    line_tally = position_pieces.shape[0]
    x_float = position_pieces.astype(jnp.float32)
    shifted = preceding_feed.astype(jnp.float32) - x_float
    base_mix = (x_float + shifted * lagging_mixture_weights[0]).astype(jnp.bfloat16)
    hidden = jnp.tanh(jnp.dot(base_mix, lagging_narrow_lowering, preferred_element_type=jnp.float32)).astype(jnp.bfloat16)
    hidden = hidden.reshape(line_tally, 5, MIXR)
    offsets = jnp.einsum('nim,imd->ind', hidden.astype(jnp.float32), lagging_narrow_raising.astype(jnp.float32))
    mixed = (x_float[None] + shifted[None] * (lagging_mixture_weights[1:, None, :] + offsets)).astype(jnp.bfloat16)
    accept_entries = widen(block_sums(mixed[0], fourfold_linear_maps[0])).reshape(line_tally, HEADCOUNT_TOTALS, SUBSPACE_EXTENT)
    lookup_entries = widen(block_sums(mixed[1], fourfold_linear_maps[1])).reshape(line_tally, HEADCOUNT_TOTALS, SUBSPACE_EXTENT)
    payload_scaled = widen(block_sums(mixed[2], fourfold_linear_maps[2])).reshape(line_tally, HEADCOUNT_TOTALS, SUBSPACE_EXTENT)
    valve_signal = jax.nn.silu(block_sums(mixed[3], fourfold_linear_maps[3]))
    low_rank = jnp.tanh(block_sums(mixed[4], attenuation_narrow_lowering)).astype(jnp.bfloat16)
    per_channel_decay = jnp.exp(-jnp.exp(attenuation_doublelog_anchor + jnp.dot(low_rank, attenuation_narrow_raising, preferred_element_type=jnp.float32)))
    per_channel_decay = per_channel_decay.reshape(line_tally, HEADCOUNT_TOTALS, SUBSPACE_EXTENT)
    present_reward_factor = lax.optimization_barrier(jnp.sum(accept_entries * instant_premium.reshape(HEADCOUNT_TOTALS, SUBSPACE_EXTENT) * lookup_entries, axis=-1))
    retained_query = present_reward_factor[..., None] * payload_scaled + jnp.einsum('rbm,rbmw->rbw', accept_entries, kept_outer_tableau, precision=lax.Precision.HIGHEST)
    updated_state = per_channel_decay[..., None] * kept_outer_tableau + lookup_entries[..., :, None] * payload_scaled[..., None, :]
    average = lax.optimization_barrier(jnp.mean(retained_query, axis=-1, keepdims=True))
    demeaned = retained_query - average
    spread_squared = lax.optimization_barrier(jnp.mean(demeaned * demeaned, axis=-1, keepdims=True))
    standardized = (demeaned * lax.rsqrt(spread_squared + NORMALIZER_GUARD)).reshape(line_tally, HEADCOUNT_TOTALS * SUBSPACE_EXTENT) * norming_multiplier + norming_intercept
    combined_response = (standardized * valve_signal).astype(jnp.bfloat16)
    produced_response = jnp.dot(combined_response, outgoing_linear_map, preferred_element_type=jnp.float32).astype(jnp.bfloat16)
    return (produced_response, updated_state)

def reference(tier_feed_tensor, preceding_feed_each_stream, stream_kept_tableaux, position_mapping_target, lagging_mixture_weights, lagging_narrow_lowering, lagging_narrow_raising, fourfold_linear_maps, attenuation_narrow_lowering, attenuation_narrow_raising, attenuation_doublelog_anchor, instant_premium, norming_multiplier, norming_intercept, outgoing_linear_map):
    kept_outer_tableau = stream_kept_tableaux.reshape(SESS, HEADCOUNT_TOTALS, SUBSPACE_EXTENT, SUBSPACE_EXTENT)
    preceding_feed = preceding_feed_each_stream
    results = []
    for step_index in range(STEPS_A + STEPS_B):
        position_pieces = tier_feed_tensor[step_index]
        produced_response, kept_outer_tableau = infer_lone_position(position_pieces, preceding_feed, kept_outer_tableau, lagging_mixture_weights, lagging_narrow_lowering, lagging_narrow_raising, fourfold_linear_maps, attenuation_narrow_lowering, attenuation_narrow_raising, attenuation_doublelog_anchor, instant_premium, norming_multiplier, norming_intercept, outgoing_linear_map)
        results.append(produced_response)
        preceding_feed = position_pieces
    inverse = jnp.argsort(position_mapping_target).astype(jnp.int32)
    y_first = jnp.stack(results[:STEPS_A])
    y_second = jnp.take(jnp.stack(results[STEPS_A:]), inverse, axis=1)
    row_ids = jnp.arange(OUT_ROWS, dtype=jnp.int32)
    device_ids = row_ids // R
    batch_ids = device_ids // (4 * SUBS)
    head_ids = device_ids % (4 * SUBS)
    slot_ids = (batch_ids * SUBS + head_ids % SUBS) * R + row_ids % R
    sessions = jnp.take(inverse, slot_ids)
    column = jnp.arange(HG, dtype=jnp.int32)
    global_heads = column[None, :] // HQ * (4 * HQ) + (head_ids // SUBS)[:, None] * HQ + column[None, :] % HQ
    final_state = kept_outer_tableau[sessions[:, None], global_heads]
    return (y_first, y_second, final_state.reshape(OUT_ROWS, HG, SUBSPACE_EXTENT * SUBSPACE_EXTENT))
```

```python
import jax
import jax.numpy as jnp
from jax import lax
from jax.sharding import PartitionSpec as P

SUBSPACE_EXTENT = 64
STEPS_A = 2
MIX_MAPS = 5
NORMALIZER_GUARD = 0.00064


def route_to_slots(value, position_mapping_target, batch_index, head_index):
    batch_count = lax.axis_size("batch")
    head_count = lax.axis_size("head")
    local_rows, heads_here, width = value.shape
    cluster_number = head_count // 4
    slots_dev = local_rows // cluster_number
    per_pair = slots_dev // batch_count
    quarter = heads_here // 4
    own_map = lax.dynamic_slice_in_dim(
        position_mapping_target, batch_index * local_rows, local_rows
    )
    send_order = jnp.argsort(own_map // slots_dev, stable=True)
    packed = jnp.take(value, send_order, axis=0)
    packed = packed.reshape(batch_count, cluster_number, per_pair, 4, quarter, width)
    packed = packed.transpose(0, 3, 1, 2, 4, 5).reshape(
        batch_count * head_count, per_pair, quarter, width
    )
    arrived = lax.all_to_all(packed, ("batch", "head"), split_axis=0, concat_axis=0, tiled=True)
    arrived = arrived.reshape(batch_count, head_count, per_pair, quarter, width)
    arrived = arrived.transpose(0, 2, 1, 3, 4).reshape(slots_dev, head_count * quarter, width)
    target = batch_index * cluster_number + head_index % cluster_number
    arrivals = lax.dynamic_slice_in_dim(
        jnp.argsort(position_mapping_target // slots_dev, stable=True),
        target * slots_dev,
        slots_dev,
    )
    placing = jnp.argsort(jnp.take(position_mapping_target, arrivals) % slots_dev)
    return jnp.take(arrived, placing, axis=0)


def per_device(
    tier_feed_tensor,
    preceding_feed_each_stream,
    stream_kept_tableaux,
    position_mapping_target,
    lagging_mixture_weights,
    lagging_narrow_lowering,
    lagging_narrow_raising,
    fourfold_linear_maps,
    attenuation_narrow_lowering,
    attenuation_narrow_raising,
    attenuation_doublelog_anchor,
    instant_premium,
    norming_multiplier,
    norming_intercept,
    outgoing_linear_map,
):
    batch_count = lax.axis_size("batch")
    batch_index = lax.axis_index("batch")
    head_index = lax.axis_index("head")
    steps, sessions, feats = tier_feed_tensor.shape
    local_rows = sessions // batch_count
    heads_here = stream_kept_tableaux.shape[1]
    width = heads_here * SUBSPACE_EXTENT
    f32 = jnp.float32
    bf16 = jnp.bfloat16

    moved_state = route_to_slots(
        stream_kept_tableaux.astype(bf16), position_mapping_target, batch_index, head_index
    )

    previous = jnp.concatenate([preceding_feed_each_stream[None], tier_feed_tensor[:-1]], axis=0)

    def by_block(value):
        return value.reshape(steps, batch_count, local_rows, feats).transpose(1, 0, 2, 3).reshape(
            batch_count * steps * local_rows, feats
        )

    x_float = by_block(tier_feed_tensor).astype(f32)
    shifted = by_block(previous).astype(f32) - x_float
    rows = x_float.shape[0]
    base_mix = (x_float + shifted * lagging_mixture_weights[0]).astype(bf16)
    partial_value = jnp.dot(base_mix, lagging_narrow_lowering, preferred_element_type=f32)
    hidden = jnp.tanh(lax.psum(partial_value.astype(bf16), "batch").astype(f32)).astype(bf16)
    hidden = hidden.reshape(rows, MIX_MAPS, lagging_narrow_raising.shape[1])
    offsets = jnp.einsum(
        "nim,imd->ind", hidden, lagging_narrow_raising, preferred_element_type=f32
    )
    mixed = (
        x_float[None] + shifted[None] * (lagging_mixture_weights[1:, None, :] + offsets)
    ).astype(bf16)
    main_part = jnp.einsum(
        "inf,ifc->nic", mixed[:4], fourfold_linear_maps, preferred_element_type=f32
    )
    decay_part = jnp.dot(mixed[4], attenuation_narrow_lowering, preferred_element_type=f32)
    aggregated = lax.psum_scatter(
        jnp.concatenate([main_part.reshape(rows, -1), decay_part], axis=1).astype(bf16),
        "batch",
        scatter_dimension=0,
        tiled=True,
    ).astype(f32)
    aggregated = aggregated.reshape(steps, local_rows, -1)

    def heads_of(value):
        return value.reshape(steps, local_rows, heads_here, SUBSPACE_EXTENT)

    recept = heads_of(aggregated[..., :width])
    key_vec = heads_of(aggregated[..., width : 2 * width])
    valued = heads_of(aggregated[..., 2 * width : 3 * width])
    gate_act = jax.nn.silu(aggregated[..., 3 * width : 4 * width])
    low_rank = jnp.tanh(aggregated[..., 4 * width :]).astype(bf16)
    decay_rate = heads_of(
        jnp.exp(
            -jnp.exp(
                attenuation_doublelog_anchor
                + jnp.dot(low_rank, attenuation_narrow_raising, preferred_element_type=f32)
            )
        )
    )
    bonus_term = jnp.sum(
        recept * instant_premium.reshape(heads_here, SUBSPACE_EXTENT) * key_vec, axis=-1
    )

    prefix = [jnp.ones_like(decay_rate[0])]
    for t in range(steps):
        prefix.append(prefix[-1] * decay_rate[t])
    query = jnp.stack([recept[t] * prefix[t] for t in range(steps)])
    state = stream_kept_tableaux.reshape(
        local_rows, heads_here, SUBSPACE_EXTENT, SUBSPACE_EXTENT
    )
    from_state = jnp.einsum(
        "tnhi,nhij->tnhj", query, state, precision=lax.Precision.HIGHEST
    )
    outputs = []
    for t in range(steps):
        total = bonus_term[t][..., None] * valued[t] + from_state[t]
        for s in range(t):
            factor = key_vec[s]
            for u in range(s + 1, t):
                factor = factor * decay_rate[u]
            total = total + jnp.sum(recept[t] * factor, axis=-1, keepdims=True) * valued[s]
        outputs.append(total)
    wkv_out = jnp.stack(outputs)

    tails = []
    for s in range(steps):
        factor = key_vec[s]
        for u in range(s + 1, steps):
            factor = factor * decay_rate[u]
        tails.append(factor)
    payload = jnp.concatenate([prefix[steps]] + tails + [valued[s] for s in range(steps)], axis=-1)
    moved_terms = route_to_slots(
        payload.astype(bf16), position_mapping_target, batch_index, head_index
    ).astype(f32)
    slots_dev, columns, _ = moved_terms.shape
    moved_terms = moved_terms.reshape(slots_dev, columns, 1 + 2 * steps, SUBSPACE_EXTENT)
    final_state = moved_terms[:, :, 0, :, None] * moved_state.astype(f32).reshape(
        slots_dev, columns, SUBSPACE_EXTENT, SUBSPACE_EXTENT
    )
    for s in range(steps):
        final_state = (
            final_state
            + moved_terms[:, :, 1 + s, :, None] * moved_terms[:, :, 1 + steps + s, None, :]
        )
    final_state = final_state.reshape(slots_dev, columns, SUBSPACE_EXTENT * SUBSPACE_EXTENT)

    average = jnp.mean(wkv_out, axis=-1, keepdims=True)
    demeaned = wkv_out - average
    spread_squared = jnp.mean(demeaned * demeaned, axis=-1, keepdims=True)
    standardized = (demeaned * lax.rsqrt(spread_squared + NORMALIZER_GUARD)).reshape(
        steps, local_rows, width
    ) * norming_multiplier + norming_intercept
    combined_response = (standardized * gate_act).astype(bf16)

    gathered = lax.all_gather(combined_response, "batch", axis=1, tiled=True)
    inverse = jnp.argsort(position_mapping_target)
    arranged = jnp.concatenate(
        [gathered[:STEPS_A], jnp.take(gathered[STEPS_A:], inverse, axis=1)], axis=0
    )
    partial_y = jnp.einsum(
        "tnf,fo->tno", arranged, outgoing_linear_map, preferred_element_type=f32
    ).astype(bf16)
    produced = lax.psum_scatter(partial_y, "head", scatter_dimension=1, tiled=True)
    return (produced[:STEPS_A], produced[STEPS_A:], final_state)


def solution(mesh):
    in_specs = (
        P(None, "groups", "batch"),
        P("groups", "batch"),
        P(("groups", "batch"), "head", None),
        P("groups"),
        P(None, "batch"),
        P("batch", None),
        P(None, None, "batch"),
        P(None, "batch", "head"),
        P("batch", None),
        P(None, "head"),
        P("head"),
        P("head"),
        P("head"),
        P("head"),
        P("head", "batch"),
    )
    out_specs = (
        P(None, ("groups", "head"), "batch"),
        P(None, ("groups", "head"), "batch"),
        P(("groups", "batch", "head"), None, None),
    )
    return jax.shard_map(
        per_device, mesh=mesh, in_specs=in_specs, out_specs=out_specs, check_vma=False
    )
```

```python
import functools

import jax
import jax.numpy as jnp
from jax import lax
from jax.experimental import pallas as pl
from jax.experimental.pallas import tpu as pltpu
from jax.sharding import PartitionSpec as P

SUBSPACE_EXTENT = 64
STEPS_A = 2
MIX_MAPS = 5
NORMALIZER_GUARD = 0.00064


def route_to_slots(value, position_mapping_target, batch_index, head_index):
    batch_count = lax.axis_size("batch")
    head_count = lax.axis_size("head")
    local_rows, heads_here, width = value.shape
    cluster_number = head_count // 4
    slots_dev = local_rows // cluster_number
    per_pair = slots_dev // batch_count
    quarter = heads_here // 4
    own_map = lax.dynamic_slice_in_dim(
        position_mapping_target, batch_index * local_rows, local_rows
    )
    send_order = jnp.argsort(own_map // slots_dev, stable=True)
    packed = jnp.take(value, send_order, axis=0)
    packed = packed.reshape(batch_count, cluster_number, per_pair, 4, quarter, width)
    packed = packed.transpose(0, 3, 1, 2, 4, 5).reshape(
        batch_count * head_count, per_pair, quarter, width
    )
    arrived = lax.all_to_all(packed, ("batch", "head"), split_axis=0, concat_axis=0, tiled=True)
    arrived = arrived.reshape(batch_count, head_count, per_pair, quarter, width)
    arrived = arrived.transpose(0, 2, 1, 3, 4).reshape(slots_dev, head_count * quarter, width)
    target = batch_index * cluster_number + head_index % cluster_number
    arrivals = lax.dynamic_slice_in_dim(
        jnp.argsort(position_mapping_target // slots_dev, stable=True),
        target * slots_dev,
        slots_dev,
    )
    placing = jnp.argsort(jnp.take(position_mapping_target, arrivals) % slots_dev)
    return jnp.take(arrived, placing, axis=0)


def rebuild_kernel(steps, state_ref, terms_ref, out_ref, spread_ref, tile_ref):
    extent = SUBSPACE_EXTENT

    @pl.when(pl.program_id(0) == 0)
    def _():
        lane = lax.broadcasted_iota(jnp.int32, spread_ref.shape, 1)
        row = lax.broadcasted_iota(jnp.int32, spread_ref.shape, 0)
        spread_ref[...] = (lane // extent == row).astype(spread_ref.dtype)
        tile_ref[...] = (lane % extent == row).astype(tile_ref.dtype)

    spread = spread_ref[...]
    tile = tile_ref[...]
    total = jnp.dot(terms_ref[0], spread, preferred_element_type=jnp.float32) * state_ref[...].astype(
        jnp.float32
    )
    for s in range(steps):
        total = total + jnp.dot(
            terms_ref[1 + s], spread, preferred_element_type=jnp.float32
        ) * jnp.dot(terms_ref[1 + steps + s], tile, preferred_element_type=jnp.float32)
    out_ref[...] = total


def rebuild_state(moved_state, moved_terms, steps):
    slots_dev, columns, flat = moved_state.shape
    pieces = moved_terms.shape[1]
    extent = SUBSPACE_EXTENT
    return pl.pallas_call(
        functools.partial(rebuild_kernel, steps),
        grid=(slots_dev,),
        in_specs=[
            pl.BlockSpec((None, columns, flat), lambda n: (n, 0, 0)),
            pl.BlockSpec((None, pieces, columns, extent), lambda n: (n, 0, 0, 0)),
        ],
        out_specs=pl.BlockSpec((None, columns, flat), lambda n: (n, 0, 0)),
        out_shape=jax.ShapeDtypeStruct((slots_dev, columns, flat), jnp.float32),
        scratch_shapes=[
            pltpu.VMEM((extent, flat), jnp.bfloat16),
            pltpu.VMEM((extent, flat), jnp.bfloat16),
        ],
        cost_estimate=pl.CostEstimate(
            flops=2 * slots_dev * columns * extent * flat * (1 + 2 * steps),
            transcendentals=0,
            bytes_accessed=slots_dev * columns * (flat * 6 + pieces * extent * 2),
        ),
    )(moved_state, moved_terms)


def per_device(
    tier_feed_tensor,
    preceding_feed_each_stream,
    stream_kept_tableaux,
    position_mapping_target,
    lagging_mixture_weights,
    lagging_narrow_lowering,
    lagging_narrow_raising,
    fourfold_linear_maps,
    attenuation_narrow_lowering,
    attenuation_narrow_raising,
    attenuation_doublelog_anchor,
    instant_premium,
    norming_multiplier,
    norming_intercept,
    outgoing_linear_map,
):
    batch_count = lax.axis_size("batch")
    batch_index = lax.axis_index("batch")
    head_index = lax.axis_index("head")
    steps, sessions, feats = tier_feed_tensor.shape
    local_rows = sessions // batch_count
    heads_here = stream_kept_tableaux.shape[1]
    width = heads_here * SUBSPACE_EXTENT
    f32 = jnp.float32
    bf16 = jnp.bfloat16

    moved_state = route_to_slots(
        stream_kept_tableaux.astype(bf16), position_mapping_target, batch_index, head_index
    )

    previous = jnp.concatenate([preceding_feed_each_stream[None], tier_feed_tensor[:-1]], axis=0)

    def by_block(value):
        return value.reshape(steps, batch_count, local_rows, feats).transpose(1, 0, 2, 3).reshape(
            batch_count * steps * local_rows, feats
        )

    x_float = by_block(tier_feed_tensor).astype(f32)
    shifted = by_block(previous).astype(f32) - x_float
    rows = x_float.shape[0]
    base_mix = (x_float + shifted * lagging_mixture_weights[0]).astype(bf16)
    partial_value = jnp.dot(base_mix, lagging_narrow_lowering, preferred_element_type=f32)
    hidden = jnp.tanh(lax.psum(partial_value.astype(bf16), "batch").astype(f32)).astype(bf16)
    hidden = hidden.reshape(rows, MIX_MAPS, lagging_narrow_raising.shape[1])
    offsets = jnp.einsum(
        "nim,imd->ind", hidden, lagging_narrow_raising, preferred_element_type=f32
    )
    mixed = (
        x_float[None] + shifted[None] * (lagging_mixture_weights[1:, None, :] + offsets)
    ).astype(bf16)
    main_part = jnp.einsum(
        "inf,ifc->nic", mixed[:4], fourfold_linear_maps, preferred_element_type=f32
    )
    decay_part = jnp.dot(mixed[4], attenuation_narrow_lowering, preferred_element_type=f32)
    aggregated = lax.psum_scatter(
        jnp.concatenate([main_part.reshape(rows, -1), decay_part], axis=1).astype(bf16),
        "batch",
        scatter_dimension=0,
        tiled=True,
    ).astype(f32)
    aggregated = aggregated.reshape(steps, local_rows, -1)

    def heads_of(value):
        return value.reshape(steps, local_rows, heads_here, SUBSPACE_EXTENT)

    recept = heads_of(aggregated[..., :width])
    key_vec = heads_of(aggregated[..., width : 2 * width])
    valued = heads_of(aggregated[..., 2 * width : 3 * width])
    gate_act = jax.nn.silu(aggregated[..., 3 * width : 4 * width])
    low_rank = jnp.tanh(aggregated[..., 4 * width :]).astype(bf16)
    decay_rate = heads_of(
        jnp.exp(
            -jnp.exp(
                attenuation_doublelog_anchor
                + jnp.dot(low_rank, attenuation_narrow_raising, preferred_element_type=f32)
            )
        )
    )
    bonus_term = jnp.sum(
        recept * instant_premium.reshape(heads_here, SUBSPACE_EXTENT) * key_vec, axis=-1
    )

    prefix = [jnp.ones_like(decay_rate[0])]
    for t in range(steps):
        prefix.append(prefix[-1] * decay_rate[t])
    query = jnp.stack([recept[t] * prefix[t] for t in range(steps)])
    state = stream_kept_tableaux.reshape(
        local_rows, heads_here, SUBSPACE_EXTENT, SUBSPACE_EXTENT
    )
    from_state = jnp.einsum(
        "tnhi,nhij->tnhj", query, state, precision=lax.Precision.HIGHEST
    )
    outputs = []
    for t in range(steps):
        total = bonus_term[t][..., None] * valued[t] + from_state[t]
        for s in range(t):
            factor = key_vec[s]
            for u in range(s + 1, t):
                factor = factor * decay_rate[u]
            total = total + jnp.sum(recept[t] * factor, axis=-1, keepdims=True) * valued[s]
        outputs.append(total)
    wkv_out = jnp.stack(outputs)

    tails = []
    for s in range(steps):
        factor = key_vec[s]
        for u in range(s + 1, steps):
            factor = factor * decay_rate[u]
        tails.append(factor)
    payload = jnp.concatenate([prefix[steps]] + tails + [valued[s] for s in range(steps)], axis=-1)
    moved_terms = route_to_slots(
        payload.astype(bf16), position_mapping_target, batch_index, head_index
    )
    slots_dev, columns, _ = moved_terms.shape
    moved_terms = moved_terms.reshape(slots_dev, columns, 1 + 2 * steps, SUBSPACE_EXTENT).transpose(
        0, 2, 1, 3
    )
    final_state = rebuild_state(moved_state, moved_terms, steps)

    average = jnp.mean(wkv_out, axis=-1, keepdims=True)
    demeaned = wkv_out - average
    spread_squared = jnp.mean(demeaned * demeaned, axis=-1, keepdims=True)
    standardized = (demeaned * lax.rsqrt(spread_squared + NORMALIZER_GUARD)).reshape(
        steps, local_rows, width
    ) * norming_multiplier + norming_intercept
    combined_response = (standardized * gate_act).astype(bf16)

    gathered = lax.all_gather(combined_response, "batch", axis=1, tiled=True)
    inverse = jnp.argsort(position_mapping_target)
    arranged = jnp.concatenate(
        [gathered[:STEPS_A], jnp.take(gathered[STEPS_A:], inverse, axis=1)], axis=0
    )
    partial_y = jnp.einsum(
        "tnf,fo->tno", arranged, outgoing_linear_map, preferred_element_type=f32
    ).astype(bf16)
    produced = lax.psum_scatter(partial_y, "head", scatter_dimension=1, tiled=True)
    return (produced[:STEPS_A], produced[STEPS_A:], final_state)


def solution(mesh):
    in_specs = (
        P(None, "groups", "batch"),
        P("groups", "batch"),
        P(("groups", "batch"), "head", None),
        P("groups"),
        P(None, "batch"),
        P("batch", None),
        P(None, None, "batch"),
        P(None, "batch", "head"),
        P("batch", None),
        P(None, "head"),
        P("head"),
        P("head"),
        P("head"),
        P("head"),
        P("head", "batch"),
    )
    out_specs = (
        P(None, ("groups", "head"), "batch"),
        P(None, ("groups", "head"), "batch"),
        P(("groups", "batch", "head"), None, None),
    )
    return jax.shard_map(
        per_device, mesh=mesh, in_specs=in_specs, out_specs=out_specs, check_vma=False
    )
```

```python
import functools

import jax
import jax.numpy as jnp
from jax import lax
from jax.experimental import pallas as pl
from jax.experimental.pallas import tpu as pltpu
from jax.sharding import PartitionSpec as P

SUBSPACE_EXTENT = 64
STEPS_A = 2
MIX_MAPS = 5
NORMALIZER_GUARD = 0.00064


def route_to_slots(value, position_mapping_target, batch_index, head_index):
    batch_count = lax.axis_size("batch")
    head_count = lax.axis_size("head")
    local_rows, heads_here, width = value.shape
    cluster_number = head_count // 4
    slots_dev = local_rows // cluster_number
    per_pair = slots_dev // batch_count
    quarter = heads_here // 4
    own_map = lax.dynamic_slice_in_dim(
        position_mapping_target, batch_index * local_rows, local_rows
    )
    send_order = jnp.argsort(own_map // slots_dev, stable=True)
    packed = jnp.take(value, send_order, axis=0)
    packed = packed.reshape(batch_count, cluster_number, per_pair, 4, quarter, width)
    packed = packed.transpose(0, 3, 1, 2, 4, 5).reshape(
        batch_count * head_count, per_pair, quarter, width
    )
    arrived = lax.all_to_all(packed, ("batch", "head"), split_axis=0, concat_axis=0, tiled=True)
    arrived = arrived.reshape(batch_count, head_count, per_pair, quarter, width)
    arrived = arrived.transpose(0, 2, 1, 3, 4).reshape(slots_dev, head_count * quarter, width)
    target = batch_index * cluster_number + head_index % cluster_number
    arrivals = lax.dynamic_slice_in_dim(
        jnp.argsort(position_mapping_target // slots_dev, stable=True),
        target * slots_dev,
        slots_dev,
    )
    placing = jnp.argsort(jnp.take(position_mapping_target, arrivals) % slots_dev)
    return jnp.take(arrived, placing, axis=0)


def exchange_sum(pieces, axis_name):
    arrived = lax.all_to_all(pieces, axis_name, split_axis=0, concat_axis=0, tiled=True)
    return jnp.sum(arrived.astype(jnp.float32), axis=0)


def exchange_copies(value, axis_name):
    count = lax.axis_size(axis_name)
    copies = jnp.broadcast_to(value[None], (count,) + value.shape)
    return lax.all_to_all(copies, axis_name, split_axis=0, concat_axis=0, tiled=True)


def widen(value):
    return value.astype(jnp.bfloat16).astype(jnp.float32)


def rebuild_kernel(steps, state_ref, terms_ref, out_ref, spread_ref, tile_ref):
    extent = SUBSPACE_EXTENT

    @pl.when(pl.program_id(0) == 0)
    def _():
        lane = lax.broadcasted_iota(jnp.int32, spread_ref.shape, 1)
        row = lax.broadcasted_iota(jnp.int32, spread_ref.shape, 0)
        spread_ref[...] = (lane // extent == row).astype(spread_ref.dtype)
        tile_ref[...] = (lane % extent == row).astype(tile_ref.dtype)

    spread = spread_ref[...]
    tile = tile_ref[...]
    total = jnp.dot(terms_ref[0], spread, preferred_element_type=jnp.float32) * state_ref[...].astype(
        jnp.float32
    )
    for s in range(steps):
        total = total + jnp.dot(
            terms_ref[1 + s], spread, preferred_element_type=jnp.float32
        ) * jnp.dot(terms_ref[1 + steps + s], tile, preferred_element_type=jnp.float32)
    out_ref[...] = total


def rebuild_state(moved_state, moved_terms, steps):
    slots_dev, columns, flat = moved_state.shape
    pieces = moved_terms.shape[1]
    extent = SUBSPACE_EXTENT
    return pl.pallas_call(
        functools.partial(rebuild_kernel, steps),
        grid=(slots_dev,),
        in_specs=[
            pl.BlockSpec((None, columns, flat), lambda n: (n, 0, 0)),
            pl.BlockSpec((None, pieces, columns, extent), lambda n: (n, 0, 0, 0)),
        ],
        out_specs=pl.BlockSpec((None, columns, flat), lambda n: (n, 0, 0)),
        out_shape=jax.ShapeDtypeStruct((slots_dev, columns, flat), jnp.float32),
        scratch_shapes=[
            pltpu.VMEM((extent, flat), jnp.bfloat16),
            pltpu.VMEM((extent, flat), jnp.bfloat16),
        ],
        cost_estimate=pl.CostEstimate(
            flops=2 * slots_dev * columns * extent * flat * (1 + 2 * steps),
            transcendentals=0,
            bytes_accessed=slots_dev * columns * (flat * 6 + pieces * extent * 2),
        ),
    )(moved_state, moved_terms)


def per_device(
    tier_feed_tensor,
    preceding_feed_each_stream,
    stream_kept_tableaux,
    position_mapping_target,
    lagging_mixture_weights,
    lagging_narrow_lowering,
    lagging_narrow_raising,
    fourfold_linear_maps,
    attenuation_narrow_lowering,
    attenuation_narrow_raising,
    attenuation_doublelog_anchor,
    instant_premium,
    norming_multiplier,
    norming_intercept,
    outgoing_linear_map,
):
    batch_count = lax.axis_size("batch")
    batch_index = lax.axis_index("batch")
    head_index = lax.axis_index("head")
    steps, sessions, feats = tier_feed_tensor.shape
    local_rows = sessions // batch_count
    heads_here = stream_kept_tableaux.shape[1]
    width = heads_here * SUBSPACE_EXTENT
    f32 = jnp.float32
    bf16 = jnp.bfloat16

    moved_state = route_to_slots(
        stream_kept_tableaux.astype(bf16), position_mapping_target, batch_index, head_index
    )

    previous = jnp.concatenate([preceding_feed_each_stream[None], tier_feed_tensor[:-1]], axis=0)

    def by_block(value):
        return value.reshape(steps, batch_count, local_rows, feats).transpose(1, 0, 2, 3).reshape(
            batch_count * steps * local_rows, feats
        )

    x_float = by_block(tier_feed_tensor).astype(f32)
    shifted = by_block(previous).astype(f32) - x_float
    rows = x_float.shape[0]
    base_mix = (x_float + shifted * lagging_mixture_weights[0]).astype(bf16)
    partial_value = jnp.dot(base_mix, lagging_narrow_lowering, preferred_element_type=f32)
    hidden = jnp.tanh(
        jnp.sum(exchange_copies(partial_value.astype(bf16), "batch").astype(f32), axis=0)
    ).astype(bf16)
    hidden = hidden.reshape(rows, MIX_MAPS, lagging_narrow_raising.shape[1])
    offsets = jnp.einsum(
        "nim,imd->ind", hidden, lagging_narrow_raising, preferred_element_type=f32
    )
    mixed = (
        x_float[None] + shifted[None] * (lagging_mixture_weights[1:, None, :] + offsets)
    ).astype(bf16)
    main_part = jnp.einsum(
        "inf,ifc->nic", mixed[:4], fourfold_linear_maps, preferred_element_type=f32
    )
    decay_part = jnp.dot(mixed[4], attenuation_narrow_lowering, preferred_element_type=f32)
    aggregated = exchange_sum(
        jnp.concatenate([main_part.reshape(rows, -1), decay_part], axis=1)
        .astype(bf16)
        .reshape(batch_count, steps, local_rows, -1),
        "batch",
    )

    def heads_of(value):
        return value.reshape(steps, local_rows, heads_here, SUBSPACE_EXTENT)

    recept = heads_of(widen(aggregated[..., :width]))
    key_vec = heads_of(widen(aggregated[..., width : 2 * width]))
    valued = heads_of(widen(aggregated[..., 2 * width : 3 * width]))
    gate_act = jax.nn.silu(aggregated[..., 3 * width : 4 * width])
    low_rank = jnp.tanh(aggregated[..., 4 * width :]).astype(bf16)
    decay_rate = heads_of(
        jnp.exp(
            -jnp.exp(
                attenuation_doublelog_anchor
                + jnp.dot(low_rank, attenuation_narrow_raising, preferred_element_type=f32)
            )
        )
    )
    bonus_term = jnp.sum(
        recept * instant_premium.reshape(heads_here, SUBSPACE_EXTENT) * key_vec, axis=-1
    )

    prefix = [jnp.ones_like(decay_rate[0])]
    for t in range(steps):
        prefix.append(prefix[-1] * decay_rate[t])
    query = jnp.stack([recept[t] * prefix[t] for t in range(steps)])
    state = stream_kept_tableaux.reshape(
        local_rows, heads_here, SUBSPACE_EXTENT, SUBSPACE_EXTENT
    )
    from_state = jnp.einsum(
        "tnhi,nhij->tnhj", query, state, precision=lax.Precision.HIGHEST
    )
    outputs = []
    for t in range(steps):
        total = bonus_term[t][..., None] * valued[t] + from_state[t]
        for s in range(t):
            factor = key_vec[s]
            for u in range(s + 1, t):
                factor = factor * decay_rate[u]
            total = total + jnp.sum(recept[t] * factor, axis=-1, keepdims=True) * valued[s]
        outputs.append(total)
    wkv_out = jnp.stack(outputs)

    tails = []
    for s in range(steps):
        factor = key_vec[s]
        for u in range(s + 1, steps):
            factor = factor * decay_rate[u]
        tails.append(factor)
    payload = jnp.concatenate([prefix[steps]] + tails + [valued[s] for s in range(steps)], axis=-1)
    moved_terms = route_to_slots(
        payload.astype(bf16), position_mapping_target, batch_index, head_index
    )
    slots_dev, columns, _ = moved_terms.shape
    moved_terms = moved_terms.reshape(slots_dev, columns, 1 + 2 * steps, SUBSPACE_EXTENT).transpose(
        0, 2, 1, 3
    )
    final_state = rebuild_state(moved_state, moved_terms, steps)

    average = jnp.mean(wkv_out, axis=-1, keepdims=True)
    demeaned = wkv_out - average
    spread_squared = jnp.mean(demeaned * demeaned, axis=-1, keepdims=True)
    standardized = (demeaned * lax.rsqrt(spread_squared + NORMALIZER_GUARD)).reshape(
        steps, local_rows, width
    ) * norming_multiplier + norming_intercept
    combined_response = (standardized * gate_act).astype(bf16)

    gathered = exchange_copies(combined_response, "batch").transpose(1, 0, 2, 3)
    gathered = gathered.reshape(steps, sessions, width)
    inverse = jnp.argsort(position_mapping_target)
    arranged = jnp.concatenate(
        [gathered[:STEPS_A], jnp.take(gathered[STEPS_A:], inverse, axis=1)], axis=0
    )
    partial_y = jnp.einsum(
        "tnf,fo->tno", arranged, outgoing_linear_map, preferred_element_type=f32
    ).astype(bf16)
    head_count = lax.axis_size("head")
    produced = exchange_sum(
        partial_y.reshape(steps, head_count, sessions // head_count, -1).transpose(1, 0, 2, 3),
        "head",
    ).astype(bf16)
    return (produced[:STEPS_A], produced[STEPS_A:], final_state)


def solution(mesh):
    in_specs = (
        P(None, "groups", "batch"),
        P("groups", "batch"),
        P(("groups", "batch"), "head", None),
        P("groups"),
        P(None, "batch"),
        P("batch", None),
        P(None, None, "batch"),
        P(None, "batch", "head"),
        P("batch", None),
        P(None, "head"),
        P("head"),
        P("head"),
        P("head"),
        P("head"),
        P("head", "batch"),
    )
    out_specs = (
        P(None, ("groups", "head"), "batch"),
        P(None, ("groups", "head"), "batch"),
        P(("groups", "batch", "head"), None, None),
    )
    return jax.shard_map(
        per_device, mesh=mesh, in_specs=in_specs, out_specs=out_specs, check_vma=False
    )
```

```python
import functools

import jax
import jax.numpy as jnp
from jax import lax
from jax.experimental import pallas as pl
from jax.experimental.pallas import tpu as pltpu
from jax.sharding import PartitionSpec as P

SUBSPACE_EXTENT = 64
STEPS_A = 2
MIX_MAPS = 5
NORMALIZER_GUARD = 0.00064


def route_to_slots(value, position_mapping_target, batch_index, head_index):
    batch_count = lax.axis_size("batch")
    head_count = lax.axis_size("head")
    local_rows, heads_here, width = value.shape
    cluster_number = head_count // 4
    slots_dev = local_rows // cluster_number
    per_pair = slots_dev // batch_count
    quarter = heads_here // 4
    own_map = lax.dynamic_slice_in_dim(
        position_mapping_target, batch_index * local_rows, local_rows
    )
    send_order = jnp.argsort(own_map // slots_dev, stable=True)
    dest = jnp.arange(batch_count * head_count, dtype=jnp.int32)
    dest_block = (dest // head_count) * cluster_number + dest % cluster_number
    quad = (dest % head_count) // cluster_number
    pair = jnp.arange(per_pair, dtype=jnp.int32)
    within = jnp.arange(quarter, dtype=jnp.int32)
    sent_sessions = jnp.take(
        send_order, dest_block[:, None] * per_pair + pair[None, :], mode="clip"
    )
    sent_rows = (
        sent_sessions[:, :, None] * heads_here
        + (quad * quarter)[:, None, None]
        + within[None, None, :]
    )
    packed = jnp.take(
        value.reshape(local_rows * heads_here, width), sent_rows.reshape(-1), axis=0, mode="clip"
    ).reshape(batch_count * head_count, per_pair * quarter, width)
    arrived = lax.all_to_all(packed, ("batch", "head"), split_axis=0, concat_axis=0, tiled=True)
    target = batch_index * cluster_number + head_index % cluster_number
    arrivals = lax.dynamic_slice_in_dim(
        jnp.argsort(position_mapping_target // slots_dev, stable=True),
        target * slots_dev,
        slots_dev,
    )
    placing = jnp.argsort(jnp.take(position_mapping_target, arrivals, mode="clip") % slots_dev)
    source_head = jnp.arange(head_count, dtype=jnp.int32)
    kept_rows = (
        (
            (placing[:, None, None] // per_pair) * head_count + source_head[None, :, None]
        )
        * per_pair
        + placing[:, None, None] % per_pair
    ) * quarter + within[None, None, :]
    return jnp.take(
        arrived.reshape(-1, width), kept_rows.reshape(-1), axis=0, mode="clip"
    ).reshape(slots_dev, head_count * quarter, width)

def exchange_sum(pieces, axis_name):
    arrived = lax.all_to_all(pieces, axis_name, split_axis=0, concat_axis=0, tiled=True)
    return jnp.sum(arrived.astype(jnp.float32), axis=0)


def exchange_copies(value, axis_name):
    count = lax.axis_size(axis_name)
    copies = jnp.broadcast_to(value[None], (count,) + value.shape)
    return lax.all_to_all(copies, axis_name, split_axis=0, concat_axis=0, tiled=True)


def widen(value):
    return value.astype(jnp.bfloat16).astype(jnp.float32)


def rebuild_kernel(steps, state_ref, terms_ref, out_ref, spread_ref, tile_ref):
    extent = SUBSPACE_EXTENT

    @pl.when(pl.program_id(0) == 0)
    def _():
        lane = lax.broadcasted_iota(jnp.int32, spread_ref.shape, 1)
        row = lax.broadcasted_iota(jnp.int32, spread_ref.shape, 0)
        spread_ref[...] = (lane // extent == row).astype(spread_ref.dtype)
        tile_ref[...] = (lane % extent == row).astype(tile_ref.dtype)

    spread = spread_ref[...]
    tile = tile_ref[...]
    total = jnp.dot(terms_ref[0], spread, preferred_element_type=jnp.float32) * state_ref[...].astype(
        jnp.float32
    )
    for s in range(steps):
        total = total + jnp.dot(
            terms_ref[1 + s], spread, preferred_element_type=jnp.float32
        ) * jnp.dot(terms_ref[1 + steps + s], tile, preferred_element_type=jnp.float32)
    out_ref[...] = total


def rebuild_state(moved_state, moved_terms, steps):
    slots_dev, columns, flat = moved_state.shape
    pieces = moved_terms.shape[1]
    extent = SUBSPACE_EXTENT
    return pl.pallas_call(
        functools.partial(rebuild_kernel, steps),
        grid=(slots_dev,),
        in_specs=[
            pl.BlockSpec((None, columns, flat), lambda n: (n, 0, 0)),
            pl.BlockSpec((None, pieces, columns, extent), lambda n: (n, 0, 0, 0)),
        ],
        out_specs=pl.BlockSpec((None, columns, flat), lambda n: (n, 0, 0)),
        out_shape=jax.ShapeDtypeStruct((slots_dev, columns, flat), jnp.float32),
        scratch_shapes=[
            pltpu.VMEM((extent, flat), jnp.bfloat16),
            pltpu.VMEM((extent, flat), jnp.bfloat16),
        ],
        cost_estimate=pl.CostEstimate(
            flops=2 * slots_dev * columns * extent * flat * (1 + 2 * steps),
            transcendentals=0,
            bytes_accessed=slots_dev * columns * (flat * 6 + pieces * extent * 2),
        ),
    )(moved_state, moved_terms)


def per_device(
    tier_feed_tensor,
    preceding_feed_each_stream,
    stream_kept_tableaux,
    position_mapping_target,
    lagging_mixture_weights,
    lagging_narrow_lowering,
    lagging_narrow_raising,
    fourfold_linear_maps,
    attenuation_narrow_lowering,
    attenuation_narrow_raising,
    attenuation_doublelog_anchor,
    instant_premium,
    norming_multiplier,
    norming_intercept,
    outgoing_linear_map,
):
    batch_count = lax.axis_size("batch")
    batch_index = lax.axis_index("batch")
    head_index = lax.axis_index("head")
    steps, sessions, feats = tier_feed_tensor.shape
    local_rows = sessions // batch_count
    heads_here = stream_kept_tableaux.shape[1]
    width = heads_here * SUBSPACE_EXTENT
    f32 = jnp.float32
    bf16 = jnp.bfloat16

    moved_state = route_to_slots(
        stream_kept_tableaux.astype(bf16), position_mapping_target, batch_index, head_index
    )

    previous = jnp.concatenate([preceding_feed_each_stream[None], tier_feed_tensor[:-1]], axis=0)

    def by_block(value):
        return value.reshape(steps, batch_count, local_rows, feats).transpose(1, 0, 2, 3).reshape(
            batch_count * steps * local_rows, feats
        )

    x_float = by_block(tier_feed_tensor).astype(f32)
    shifted = by_block(previous).astype(f32) - x_float
    rows = x_float.shape[0]
    base_mix = (x_float + shifted * lagging_mixture_weights[0]).astype(bf16)
    partial_value = jnp.dot(base_mix, lagging_narrow_lowering, preferred_element_type=f32)
    hidden = jnp.tanh(
        jnp.sum(exchange_copies(partial_value.astype(bf16), "batch").astype(f32), axis=0)
    ).astype(bf16)
    hidden = hidden.reshape(rows, MIX_MAPS, lagging_narrow_raising.shape[1])
    offsets = jnp.einsum(
        "nim,imd->ind", hidden, lagging_narrow_raising, preferred_element_type=f32
    )
    mixed = (
        x_float[None] + shifted[None] * (lagging_mixture_weights[1:, None, :] + offsets)
    ).astype(bf16)
    main_part = jnp.einsum(
        "inf,ifc->nic", mixed[:4], fourfold_linear_maps, preferred_element_type=f32
    )
    decay_part = jnp.dot(mixed[4], attenuation_narrow_lowering, preferred_element_type=f32)
    aggregated = exchange_sum(
        jnp.concatenate([main_part.reshape(rows, -1), decay_part], axis=1)
        .astype(bf16)
        .reshape(batch_count, steps, local_rows, -1),
        "batch",
    )

    def heads_of(value):
        return value.reshape(steps, local_rows, heads_here, SUBSPACE_EXTENT)

    recept = heads_of(widen(aggregated[..., :width]))
    key_vec = heads_of(widen(aggregated[..., width : 2 * width]))
    valued = heads_of(widen(aggregated[..., 2 * width : 3 * width]))
    gate_act = jax.nn.silu(aggregated[..., 3 * width : 4 * width])
    low_rank = jnp.tanh(aggregated[..., 4 * width :]).astype(bf16)
    decay_rate = heads_of(
        jnp.exp(
            -jnp.exp(
                attenuation_doublelog_anchor
                + jnp.dot(low_rank, attenuation_narrow_raising, preferred_element_type=f32)
            )
        )
    )
    bonus_term = jnp.sum(
        recept * instant_premium.reshape(heads_here, SUBSPACE_EXTENT) * key_vec, axis=-1
    )

    prefix = [jnp.ones_like(decay_rate[0])]
    for t in range(steps):
        prefix.append(prefix[-1] * decay_rate[t])
    query = jnp.stack([recept[t] * prefix[t] for t in range(steps)])
    state = stream_kept_tableaux.reshape(
        local_rows, heads_here, SUBSPACE_EXTENT, SUBSPACE_EXTENT
    )
    from_state = jnp.einsum(
        "tnhi,nhij->tnhj", query, state, precision=lax.Precision.HIGHEST
    )
    outputs = []
    for t in range(steps):
        total = bonus_term[t][..., None] * valued[t] + from_state[t]
        for s in range(t):
            factor = key_vec[s]
            for u in range(s + 1, t):
                factor = factor * decay_rate[u]
            total = total + jnp.sum(recept[t] * factor, axis=-1, keepdims=True) * valued[s]
        outputs.append(total)
    wkv_out = jnp.stack(outputs)

    tails = []
    for s in range(steps):
        factor = key_vec[s]
        for u in range(s + 1, steps):
            factor = factor * decay_rate[u]
        tails.append(factor)
    payload = jnp.concatenate([prefix[steps]] + tails + [valued[s] for s in range(steps)], axis=-1)
    moved_terms = route_to_slots(
        payload.astype(bf16), position_mapping_target, batch_index, head_index
    )
    slots_dev, columns, _ = moved_terms.shape
    moved_terms = moved_terms.reshape(slots_dev, columns, 1 + 2 * steps, SUBSPACE_EXTENT).transpose(
        0, 2, 1, 3
    )
    final_state = rebuild_state(moved_state, moved_terms, steps)

    average = jnp.mean(wkv_out, axis=-1, keepdims=True)
    demeaned = wkv_out - average
    spread_squared = jnp.mean(demeaned * demeaned, axis=-1, keepdims=True)
    standardized = (demeaned * lax.rsqrt(spread_squared + NORMALIZER_GUARD)).reshape(
        steps, local_rows, width
    ) * norming_multiplier + norming_intercept
    combined_response = (standardized * gate_act).astype(bf16)

    gathered = exchange_copies(combined_response, "batch").transpose(1, 0, 2, 3)
    gathered = gathered.reshape(steps, sessions, width)
    inverse = jnp.argsort(position_mapping_target)
    arranged = jnp.concatenate(
        [gathered[:STEPS_A], jnp.take(gathered[STEPS_A:], inverse, axis=1, mode="clip")], axis=0
    )
    partial_y = jnp.einsum(
        "tnf,fo->tno", arranged, outgoing_linear_map, preferred_element_type=f32
    ).astype(bf16)
    head_count = lax.axis_size("head")
    produced = exchange_sum(
        partial_y.reshape(steps, head_count, sessions // head_count, -1).transpose(1, 0, 2, 3),
        "head",
    ).astype(bf16)
    return (produced[:STEPS_A], produced[STEPS_A:], final_state)


def solution(mesh):
    in_specs = (
        P(None, "groups", "batch"),
        P("groups", "batch"),
        P(("groups", "batch"), "head", None),
        P("groups"),
        P(None, "batch"),
        P("batch", None),
        P(None, None, "batch"),
        P(None, "batch", "head"),
        P("batch", None),
        P(None, "head"),
        P("head"),
        P("head"),
        P("head"),
        P("head"),
        P("head", "batch"),
    )
    out_specs = (
        P(None, ("groups", "head"), "batch"),
        P(None, ("groups", "head"), "batch"),
        P(("groups", "batch", "head"), None, None),
    )
    return jax.shard_map(
        per_device, mesh=mesh, in_specs=in_specs, out_specs=out_specs, check_vma=False
    )
```

```python
import functools

import jax
import jax.numpy as jnp
from jax import lax
from jax.experimental import pallas as pl
from jax.experimental.pallas import tpu as pltpu
from jax.sharding import PartitionSpec as P

SUBSPACE_EXTENT = 64
STEPS_A = 2
MIX_MAPS = 5
NORMALIZER_GUARD = 0.00064


def route_to_slots(value, position_mapping_target, batch_index, head_index):
    batch_count = lax.axis_size("batch")
    head_count = lax.axis_size("head")
    local_rows, heads_here, width = value.shape
    cluster_number = head_count // 4
    slots_dev = local_rows // cluster_number
    per_pair = slots_dev // batch_count
    quarter = heads_here // 4
    own_map = lax.dynamic_slice_in_dim(
        position_mapping_target, batch_index * local_rows, local_rows
    )
    send_order = jnp.argsort(own_map // slots_dev, stable=True)
    dest = jnp.arange(batch_count * head_count, dtype=jnp.int32)
    dest_block = (dest // head_count) * cluster_number + dest % cluster_number
    quad = (dest % head_count) // cluster_number
    pair = jnp.arange(per_pair, dtype=jnp.int32)
    within = jnp.arange(quarter, dtype=jnp.int32)
    sent_sessions = jnp.take(
        send_order, dest_block[:, None] * per_pair + pair[None, :], mode="clip"
    )
    sent_rows = (
        sent_sessions[:, :, None] * heads_here
        + (quad * quarter)[:, None, None]
        + within[None, None, :]
    )
    packed = jnp.take(
        value.reshape(local_rows * heads_here, width), sent_rows.reshape(-1), axis=0, mode="clip"
    ).reshape(batch_count * head_count, per_pair * quarter, width)
    arrived = lax.all_to_all(packed, ("batch", "head"), split_axis=0, concat_axis=0, tiled=True)
    target = batch_index * cluster_number + head_index % cluster_number
    arrivals = lax.dynamic_slice_in_dim(
        jnp.argsort(position_mapping_target // slots_dev, stable=True),
        target * slots_dev,
        slots_dev,
    )
    placing = jnp.argsort(jnp.take(position_mapping_target, arrivals, mode="clip") % slots_dev)
    source_head = jnp.arange(head_count, dtype=jnp.int32)
    kept_rows = (
        (
            (placing[:, None, None] // per_pair) * head_count + source_head[None, :, None]
        )
        * per_pair
        + placing[:, None, None] % per_pair
    ) * quarter + within[None, None, :]
    return jnp.take(
        arrived.reshape(-1, width), kept_rows.reshape(-1), axis=0, mode="clip"
    ).reshape(slots_dev, head_count * quarter, width)

def exchange_sum(pieces, axis_name):
    arrived = lax.all_to_all(pieces, axis_name, split_axis=0, concat_axis=0, tiled=True)
    return jnp.sum(arrived.astype(jnp.float32), axis=0)


def exchange_copies(value, axis_name):
    count = lax.axis_size(axis_name)
    copies = jnp.broadcast_to(value[None], (count,) + value.shape)
    return lax.all_to_all(copies, axis_name, split_axis=0, concat_axis=0, tiled=True)


def widen(value):
    return value.astype(jnp.bfloat16).astype(jnp.float32)


def rebuild_kernel(steps, state_ref, terms_ref, out_ref, spread_ref, tile_ref):
    extent = SUBSPACE_EXTENT

    @pl.when(pl.program_id(0) == 0)
    def _():
        lane = lax.broadcasted_iota(jnp.int32, spread_ref.shape, 1)
        row = lax.broadcasted_iota(jnp.int32, spread_ref.shape, 0)
        spread_ref[...] = (lane // extent == row).astype(spread_ref.dtype)
        tile_ref[...] = (lane % extent == row).astype(tile_ref.dtype)

    spread = spread_ref[...]
    tile = tile_ref[...]
    total = jnp.dot(terms_ref[0], spread, preferred_element_type=jnp.float32) * state_ref[...].astype(
        jnp.float32
    )
    for s in range(steps):
        total = total + jnp.dot(
            terms_ref[1 + s], spread, preferred_element_type=jnp.float32
        ) * jnp.dot(terms_ref[1 + steps + s], tile, preferred_element_type=jnp.float32)
    out_ref[...] = total


def rebuild_state(moved_state, moved_terms, steps):
    slots_dev, columns, flat = moved_state.shape
    pieces = moved_terms.shape[1]
    extent = SUBSPACE_EXTENT
    return pl.pallas_call(
        functools.partial(rebuild_kernel, steps),
        grid=(slots_dev,),
        in_specs=[
            pl.BlockSpec((None, columns, flat), lambda n: (n, 0, 0)),
            pl.BlockSpec((None, pieces, columns, extent), lambda n: (n, 0, 0, 0)),
        ],
        out_specs=pl.BlockSpec((None, columns, flat), lambda n: (n, 0, 0)),
        out_shape=jax.ShapeDtypeStruct((slots_dev, columns, flat), jnp.float32),
        scratch_shapes=[
            pltpu.VMEM((extent, flat), jnp.bfloat16),
            pltpu.VMEM((extent, flat), jnp.bfloat16),
        ],
        cost_estimate=pl.CostEstimate(
            flops=2 * slots_dev * columns * extent * flat * (1 + 2 * steps),
            transcendentals=0,
            bytes_accessed=slots_dev * columns * (flat * 6 + pieces * extent * 2),
        ),
    )(moved_state, moved_terms)


def recurrence_kernel(steps, proj_ref, params_ref, state_ref, mixed_ref, payload_ref, spread_ref):
    extent = SUBSPACE_EXTENT

    @pl.when(pl.program_id(0) == 0)
    def _():
        lane = lax.broadcasted_iota(jnp.int32, spread_ref.shape, 1)
        row = lax.broadcasted_iota(jnp.int32, spread_ref.shape, 0)
        spread_ref[...] = (lane // extent == row).astype(spread_ref.dtype)

    spread = spread_ref[...]
    state = state_ref[...]
    premium = params_ref[0]
    gain = params_ref[1]
    bias = params_ref[2]
    recept = [proj_ref[0, t] for t in range(steps)]
    key_vec = [proj_ref[1, t] for t in range(steps)]
    valued = [proj_ref[2, t] for t in range(steps)]
    decay_rate = [proj_ref[3, t] for t in range(steps)]
    flat = state.shape[-1]
    prefix = jnp.ones_like(recept[0])
    for t in range(steps):
        query = recept[t] * prefix
        high = query.astype(jnp.bfloat16)
        rest = query - high.astype(jnp.float32)
        middle = rest.astype(jnp.bfloat16)
        low = (rest - middle.astype(jnp.float32)).astype(jnp.bfloat16)
        spread_query = (
            jnp.dot(high, spread, preferred_element_type=jnp.float32)
            + jnp.dot(middle, spread, preferred_element_type=jnp.float32)
            + jnp.dot(low, spread, preferred_element_type=jnp.float32)
        )
        weighted = spread_query * state
        folded = weighted[:, 0:128]
        for c in range(1, flat // 128):
            folded = folded + weighted[:, 128 * c : 128 * (c + 1)]
        from_state = folded[:, :extent] + folded[:, extent:]
        bonus_term = jnp.sum(recept[t] * premium * key_vec[t], axis=-1, keepdims=True)
        total = bonus_term * valued[t] + from_state
        for s in range(t):
            factor = key_vec[s]
            for u in range(s + 1, t):
                factor = factor * decay_rate[u]
            total = total + jnp.sum(recept[t] * factor, axis=-1, keepdims=True) * valued[s]
        average = jnp.mean(total, axis=-1, keepdims=True)
        demeaned = total - average
        spread_squared = jnp.mean(demeaned * demeaned, axis=-1, keepdims=True)
        standardized = demeaned * lax.rsqrt(spread_squared + NORMALIZER_GUARD) * gain + bias
        mixed_ref[t] = (standardized * proj_ref[4, t]).astype(mixed_ref.dtype)
        prefix = prefix * decay_rate[t]
    payload_ref[0] = prefix.astype(payload_ref.dtype)
    for s in range(steps):
        factor = key_vec[s]
        for u in range(s + 1, steps):
            factor = factor * decay_rate[u]
        payload_ref[1 + s] = factor.astype(payload_ref.dtype)
        payload_ref[1 + steps + s] = valued[s].astype(payload_ref.dtype)


def run_recurrence(projected, params, state):
    pieces, steps, local_rows, heads_here, extent = projected.shape
    flat = state.shape[-1]
    return pl.pallas_call(
        functools.partial(recurrence_kernel, steps),
        grid=(local_rows,),
        in_specs=[
            pl.BlockSpec((pieces, steps, None, heads_here, extent), lambda n: (0, 0, n, 0, 0)),
            pl.BlockSpec((3, heads_here, extent), lambda n: (0, 0, 0)),
            pl.BlockSpec((None, heads_here, flat), lambda n: (n, 0, 0)),
        ],
        out_specs=[
            pl.BlockSpec((steps, None, heads_here, extent), lambda n: (0, n, 0, 0)),
            pl.BlockSpec((None, 1 + 2 * steps, heads_here, extent), lambda n: (n, 0, 0, 0)),
        ],
        out_shape=[
            jax.ShapeDtypeStruct((steps, local_rows, heads_here, extent), jnp.bfloat16),
            jax.ShapeDtypeStruct((local_rows, 1 + 2 * steps, heads_here, extent), jnp.bfloat16),
        ],
        scratch_shapes=[pltpu.VMEM((extent, flat), jnp.bfloat16)],
        cost_estimate=pl.CostEstimate(
            flops=2 * local_rows * heads_here * extent * flat * 3 * steps,
            transcendentals=steps * local_rows * heads_here,
            bytes_accessed=local_rows * heads_here * (flat * 4 + extent * (pieces * steps * 4 + steps * 2 + (1 + 2 * steps) * 2)),
        ),
    )(projected, params, state)


def per_device(
    tier_feed_tensor,
    preceding_feed_each_stream,
    stream_kept_tableaux,
    position_mapping_target,
    lagging_mixture_weights,
    lagging_narrow_lowering,
    lagging_narrow_raising,
    fourfold_linear_maps,
    attenuation_narrow_lowering,
    attenuation_narrow_raising,
    attenuation_doublelog_anchor,
    instant_premium,
    norming_multiplier,
    norming_intercept,
    outgoing_linear_map,
):
    batch_count = lax.axis_size("batch")
    batch_index = lax.axis_index("batch")
    head_index = lax.axis_index("head")
    steps, sessions, feats = tier_feed_tensor.shape
    local_rows = sessions // batch_count
    heads_here = stream_kept_tableaux.shape[1]
    width = heads_here * SUBSPACE_EXTENT
    f32 = jnp.float32
    bf16 = jnp.bfloat16

    moved_state = route_to_slots(
        stream_kept_tableaux.astype(bf16), position_mapping_target, batch_index, head_index
    )

    previous = jnp.concatenate([preceding_feed_each_stream[None], tier_feed_tensor[:-1]], axis=0)

    def by_block(value):
        return value.reshape(steps, batch_count, local_rows, feats).transpose(1, 0, 2, 3).reshape(
            batch_count * steps * local_rows, feats
        )

    x_float = by_block(tier_feed_tensor).astype(f32)
    shifted = by_block(previous).astype(f32) - x_float
    rows = x_float.shape[0]
    base_mix = (x_float + shifted * lagging_mixture_weights[0]).astype(bf16)
    partial_value = jnp.dot(base_mix, lagging_narrow_lowering, preferred_element_type=f32)
    hidden = jnp.tanh(
        jnp.sum(exchange_copies(partial_value.astype(bf16), "batch").astype(f32), axis=0)
    ).astype(bf16)
    hidden = hidden.reshape(rows, MIX_MAPS, lagging_narrow_raising.shape[1])
    offsets = jnp.einsum(
        "nim,imd->ind", hidden, lagging_narrow_raising, preferred_element_type=f32
    )
    mixed = (
        x_float[None] + shifted[None] * (lagging_mixture_weights[1:, None, :] + offsets)
    ).astype(bf16)
    main_part = jnp.einsum(
        "inf,ifc->nic", mixed[:4], fourfold_linear_maps, preferred_element_type=f32
    )
    decay_part = jnp.dot(mixed[4], attenuation_narrow_lowering, preferred_element_type=f32)
    aggregated = exchange_sum(
        jnp.concatenate([main_part.reshape(rows, -1), decay_part], axis=1)
        .astype(bf16)
        .reshape(batch_count, steps, local_rows, -1),
        "batch",
    )

    def heads_of(value):
        return value.reshape(steps, local_rows, heads_here, SUBSPACE_EXTENT)

    recept = heads_of(widen(aggregated[..., :width]))
    key_vec = heads_of(widen(aggregated[..., width : 2 * width]))
    valued = heads_of(widen(aggregated[..., 2 * width : 3 * width]))
    gate_act = jax.nn.silu(aggregated[..., 3 * width : 4 * width])
    low_rank = jnp.tanh(aggregated[..., 4 * width :]).astype(bf16)
    decay_rate = heads_of(
        jnp.exp(
            -jnp.exp(
                attenuation_doublelog_anchor
                + jnp.dot(low_rank, attenuation_narrow_raising, preferred_element_type=f32)
            )
        )
    )
    projected = jnp.stack([recept, key_vec, valued, decay_rate, heads_of(gate_act)])
    params = jnp.stack([instant_premium, norming_multiplier, norming_intercept]).reshape(
        3, heads_here, SUBSPACE_EXTENT
    )
    mixed_heads, payload = run_recurrence(projected, params, stream_kept_tableaux)
    combined_response = mixed_heads.reshape(steps, local_rows, width)
    pieces = payload.shape[1]
    moved_terms = route_to_slots(
        payload.transpose(0, 2, 1, 3).reshape(local_rows, heads_here, pieces * SUBSPACE_EXTENT),
        position_mapping_target,
        batch_index,
        head_index,
    )
    slots_dev, columns, _ = moved_terms.shape
    moved_terms = moved_terms.reshape(slots_dev, columns, pieces, SUBSPACE_EXTENT).transpose(
        0, 2, 1, 3
    )
    final_state = rebuild_state(moved_state, moved_terms, steps)

    gathered = exchange_copies(combined_response, "batch").transpose(1, 0, 2, 3)
    gathered = gathered.reshape(steps, sessions, width)
    inverse = jnp.argsort(position_mapping_target)
    arranged = jnp.concatenate(
        [gathered[:STEPS_A], jnp.take(gathered[STEPS_A:], inverse, axis=1, mode="clip")], axis=0
    )
    partial_y = jnp.einsum(
        "tnf,fo->tno", arranged, outgoing_linear_map, preferred_element_type=f32
    ).astype(bf16)
    head_count = lax.axis_size("head")
    produced = exchange_sum(
        partial_y.reshape(steps, head_count, sessions // head_count, -1).transpose(1, 0, 2, 3),
        "head",
    ).astype(bf16)
    return (produced[:STEPS_A], produced[STEPS_A:], final_state)


def solution(mesh):
    in_specs = (
        P(None, "groups", "batch"),
        P("groups", "batch"),
        P(("groups", "batch"), "head", None),
        P("groups"),
        P(None, "batch"),
        P("batch", None),
        P(None, None, "batch"),
        P(None, "batch", "head"),
        P("batch", None),
        P(None, "head"),
        P("head"),
        P("head"),
        P("head"),
        P("head"),
        P("head", "batch"),
    )
    out_specs = (
        P(None, ("groups", "head"), "batch"),
        P(None, ("groups", "head"), "batch"),
        P(("groups", "batch", "head"), None, None),
    )
    return jax.shard_map(
        per_device, mesh=mesh, in_specs=in_specs, out_specs=out_specs, check_vma=False
    )
```

```python
import functools

import jax
import jax.numpy as jnp
from jax import lax
from jax.experimental import pallas as pl
from jax.experimental.pallas import tpu as pltpu
from jax.sharding import PartitionSpec as P

SUBSPACE_EXTENT = 64
STEPS_A = 2
MIX_MAPS = 5
NORMALIZER_GUARD = 0.00064


def route_to_slots(value, position_mapping_target, batch_index, head_index):
    batch_count = lax.axis_size("batch")
    head_count = lax.axis_size("head")
    local_rows, heads_here, width = value.shape
    cluster_number = head_count // 4
    slots_dev = local_rows // cluster_number
    per_pair = slots_dev // batch_count
    quarter = heads_here // 4
    own_map = lax.dynamic_slice_in_dim(
        position_mapping_target, batch_index * local_rows, local_rows
    )
    send_order = jnp.argsort(own_map // slots_dev, stable=True)
    dest = jnp.arange(batch_count * head_count, dtype=jnp.int32)
    dest_block = (dest // head_count) * cluster_number + dest % cluster_number
    quad = (dest % head_count) // cluster_number
    pair = jnp.arange(per_pair, dtype=jnp.int32)
    within = jnp.arange(quarter, dtype=jnp.int32)
    sent_sessions = jnp.take(
        send_order, dest_block[:, None] * per_pair + pair[None, :], mode="clip"
    )
    sent_rows = (
        sent_sessions[:, :, None] * heads_here
        + (quad * quarter)[:, None, None]
        + within[None, None, :]
    )
    packed = jnp.take(
        value.reshape(local_rows * heads_here, width), sent_rows.reshape(-1), axis=0, mode="clip"
    ).reshape(batch_count * head_count, per_pair * quarter, width)
    arrived = lax.all_to_all(packed, ("batch", "head"), split_axis=0, concat_axis=0, tiled=True)
    target = batch_index * cluster_number + head_index % cluster_number
    arrivals = lax.dynamic_slice_in_dim(
        jnp.argsort(position_mapping_target // slots_dev, stable=True),
        target * slots_dev,
        slots_dev,
    )
    placing = jnp.argsort(jnp.take(position_mapping_target, arrivals, mode="clip") % slots_dev)
    source_head = jnp.arange(head_count, dtype=jnp.int32)
    kept_rows = (
        (
            (placing[:, None, None] // per_pair) * head_count + source_head[None, :, None]
        )
        * per_pair
        + placing[:, None, None] % per_pair
    ) * quarter + within[None, None, :]
    return jnp.take(
        arrived.reshape(-1, width), kept_rows.reshape(-1), axis=0, mode="clip"
    ).reshape(slots_dev, head_count * quarter, width)

def exchange_sum(pieces, axis_name):
    arrived = lax.all_to_all(pieces, axis_name, split_axis=0, concat_axis=0, tiled=True)
    return jnp.sum(arrived.astype(jnp.float32), axis=0)


def exchange_copies(value, axis_name):
    count = lax.axis_size(axis_name)
    copies = jnp.broadcast_to(value[None], (count,) + value.shape)
    return lax.all_to_all(copies, axis_name, split_axis=0, concat_axis=0, tiled=True)


def widen(value):
    return value.astype(jnp.bfloat16).astype(jnp.float32)


def rebuild_kernel(steps, state_ref, terms_ref, out_ref, spread_ref, tile_ref):
    extent = SUBSPACE_EXTENT

    @pl.when(pl.program_id(0) == 0)
    def _():
        lane = lax.broadcasted_iota(jnp.int32, spread_ref.shape, 1)
        row = lax.broadcasted_iota(jnp.int32, spread_ref.shape, 0)
        spread_ref[...] = (lane // extent == row).astype(spread_ref.dtype)
        tile_ref[...] = (lane % extent == row).astype(tile_ref.dtype)

    spread = spread_ref[...]
    tile = tile_ref[...]
    total = jnp.dot(terms_ref[0], spread, preferred_element_type=jnp.float32) * state_ref[...].astype(
        jnp.float32
    )
    for s in range(steps):
        total = total + jnp.dot(
            terms_ref[1 + s], spread, preferred_element_type=jnp.float32
        ) * jnp.dot(terms_ref[1 + steps + s], tile, preferred_element_type=jnp.float32)
    out_ref[...] = total


def rebuild_state(moved_state, moved_terms, steps):
    slots_dev, columns, flat = moved_state.shape
    pieces = moved_terms.shape[1]
    extent = SUBSPACE_EXTENT
    return pl.pallas_call(
        functools.partial(rebuild_kernel, steps),
        grid=(slots_dev,),
        in_specs=[
            pl.BlockSpec((None, columns, flat), lambda n: (n, 0, 0)),
            pl.BlockSpec((None, pieces, columns, extent), lambda n: (n, 0, 0, 0)),
        ],
        out_specs=pl.BlockSpec((None, columns, flat), lambda n: (n, 0, 0)),
        out_shape=jax.ShapeDtypeStruct((slots_dev, columns, flat), jnp.float32),
        scratch_shapes=[
            pltpu.VMEM((extent, flat), jnp.bfloat16),
            pltpu.VMEM((extent, flat), jnp.bfloat16),
        ],
        cost_estimate=pl.CostEstimate(
            flops=2 * slots_dev * columns * extent * flat * (1 + 2 * steps),
            transcendentals=0,
            bytes_accessed=slots_dev * columns * (flat * 6 + pieces * extent * 2),
        ),
    )(moved_state, moved_terms)


def recurrence_kernel(
    steps,
    recept_ref,
    key_ref,
    value_ref,
    decay_ref,
    gate_ref,
    params_ref,
    state_ref,
    mixed_ref,
    payload_ref,
    spread_ref,
):
    extent = SUBSPACE_EXTENT

    @pl.when(pl.program_id(0) == 0)
    def _():
        lane = lax.broadcasted_iota(jnp.int32, spread_ref.shape, 1)
        row = lax.broadcasted_iota(jnp.int32, spread_ref.shape, 0)
        spread_ref[...] = (lane // extent == row).astype(spread_ref.dtype)

    spread = spread_ref[...]
    state = state_ref[...]
    premium = params_ref[0]
    gain = params_ref[1]
    bias = params_ref[2]
    recept = [recept_ref[t] for t in range(steps)]
    key_vec = [key_ref[t] for t in range(steps)]
    valued = [value_ref[t] for t in range(steps)]
    decay_rate = [decay_ref[t] for t in range(steps)]
    flat = state.shape[-1]
    prefix = jnp.ones_like(recept[0])
    for t in range(steps):
        query = recept[t] * prefix
        high = query.astype(jnp.bfloat16)
        rest = query - high.astype(jnp.float32)
        middle = rest.astype(jnp.bfloat16)
        low = (rest - middle.astype(jnp.float32)).astype(jnp.bfloat16)
        spread_query = (
            jnp.dot(high, spread, preferred_element_type=jnp.float32)
            + jnp.dot(middle, spread, preferred_element_type=jnp.float32)
            + jnp.dot(low, spread, preferred_element_type=jnp.float32)
        )
        weighted = spread_query * state
        folded = weighted[:, 0:128]
        for c in range(1, flat // 128):
            folded = folded + weighted[:, 128 * c : 128 * (c + 1)]
        from_state = folded[:, :extent] + folded[:, extent:]
        bonus_term = jnp.sum(recept[t] * premium * key_vec[t], axis=-1, keepdims=True)
        total = bonus_term * valued[t] + from_state
        for s in range(t):
            factor = key_vec[s]
            for u in range(s + 1, t):
                factor = factor * decay_rate[u]
            total = total + jnp.sum(recept[t] * factor, axis=-1, keepdims=True) * valued[s]
        average = jnp.mean(total, axis=-1, keepdims=True)
        demeaned = total - average
        spread_squared = jnp.mean(demeaned * demeaned, axis=-1, keepdims=True)
        standardized = demeaned * lax.rsqrt(spread_squared + NORMALIZER_GUARD) * gain + bias
        mixed_ref[t] = (standardized * gate_ref[t]).astype(mixed_ref.dtype)
        prefix = prefix * decay_rate[t]
    payload_ref[0] = prefix.astype(payload_ref.dtype)
    for s in range(steps):
        factor = key_vec[s]
        for u in range(s + 1, steps):
            factor = factor * decay_rate[u]
        payload_ref[1 + s] = factor.astype(payload_ref.dtype)
        payload_ref[1 + steps + s] = valued[s].astype(payload_ref.dtype)


def run_recurrence(projected, params, state):
    pieces = len(projected)
    steps, local_rows, heads_here, extent = projected[0].shape
    flat = state.shape[-1]
    return pl.pallas_call(
        functools.partial(recurrence_kernel, steps),
        grid=(local_rows,),
        in_specs=[
            *[pl.BlockSpec((steps, None, heads_here, extent), lambda n: (0, n, 0, 0))] * pieces,
            pl.BlockSpec((3, heads_here, extent), lambda n: (0, 0, 0)),
            pl.BlockSpec((None, heads_here, flat), lambda n: (n, 0, 0)),
        ],
        out_specs=[
            pl.BlockSpec((steps, None, heads_here, extent), lambda n: (0, n, 0, 0)),
            pl.BlockSpec((None, 1 + 2 * steps, heads_here, extent), lambda n: (n, 0, 0, 0)),
        ],
        out_shape=[
            jax.ShapeDtypeStruct((steps, local_rows, heads_here, extent), jnp.bfloat16),
            jax.ShapeDtypeStruct((local_rows, 1 + 2 * steps, heads_here, extent), jnp.bfloat16),
        ],
        scratch_shapes=[pltpu.VMEM((extent, flat), jnp.bfloat16)],
        cost_estimate=pl.CostEstimate(
            flops=2 * local_rows * heads_here * extent * flat * 3 * steps,
            transcendentals=steps * local_rows * heads_here,
            bytes_accessed=local_rows * heads_here * (flat * 4 + extent * (pieces * steps * 4 + steps * 2 + (1 + 2 * steps) * 2)),
        ),
    )(*projected, params, state)


def per_device(
    tier_feed_tensor,
    preceding_feed_each_stream,
    stream_kept_tableaux,
    position_mapping_target,
    lagging_mixture_weights,
    lagging_narrow_lowering,
    lagging_narrow_raising,
    fourfold_linear_maps,
    attenuation_narrow_lowering,
    attenuation_narrow_raising,
    attenuation_doublelog_anchor,
    instant_premium,
    norming_multiplier,
    norming_intercept,
    outgoing_linear_map,
):
    batch_count = lax.axis_size("batch")
    batch_index = lax.axis_index("batch")
    head_index = lax.axis_index("head")
    steps, sessions, feats = tier_feed_tensor.shape
    local_rows = sessions // batch_count
    heads_here = stream_kept_tableaux.shape[1]
    width = heads_here * SUBSPACE_EXTENT
    f32 = jnp.float32
    bf16 = jnp.bfloat16

    moved_state = route_to_slots(
        stream_kept_tableaux.astype(bf16), position_mapping_target, batch_index, head_index
    )

    previous = jnp.concatenate([preceding_feed_each_stream[None], tier_feed_tensor[:-1]], axis=0)

    def by_block(value):
        return value.reshape(steps, batch_count, local_rows, feats).transpose(1, 0, 2, 3).reshape(
            batch_count * steps * local_rows, feats
        )

    x_float = by_block(tier_feed_tensor).astype(f32)
    shifted = by_block(previous).astype(f32) - x_float
    rows = x_float.shape[0]
    base_mix = (x_float + shifted * lagging_mixture_weights[0]).astype(bf16)
    partial_value = jnp.dot(base_mix, lagging_narrow_lowering, preferred_element_type=f32)
    hidden = jnp.tanh(
        jnp.sum(exchange_copies(partial_value.astype(bf16), "batch").astype(f32), axis=0)
    ).astype(bf16)
    hidden = hidden.reshape(rows, MIX_MAPS, lagging_narrow_raising.shape[1])
    offsets = jnp.einsum(
        "nim,imd->ind", hidden, lagging_narrow_raising, preferred_element_type=f32
    )
    mixed = (
        x_float[None] + shifted[None] * (lagging_mixture_weights[1:, None, :] + offsets)
    ).astype(bf16)
    main_part = jnp.einsum(
        "inf,ifc->nic", mixed[:4], fourfold_linear_maps, preferred_element_type=f32
    )
    decay_part = jnp.dot(mixed[4], attenuation_narrow_lowering, preferred_element_type=f32)
    aggregated = exchange_sum(
        jnp.concatenate([main_part.reshape(rows, -1), decay_part], axis=1)
        .astype(bf16)
        .reshape(batch_count, steps, local_rows, -1),
        "batch",
    )

    def heads_of(value):
        return value.reshape(steps, local_rows, heads_here, SUBSPACE_EXTENT)

    recept = heads_of(widen(aggregated[..., :width]))
    key_vec = heads_of(widen(aggregated[..., width : 2 * width]))
    valued = heads_of(widen(aggregated[..., 2 * width : 3 * width]))
    gate_act = jax.nn.silu(aggregated[..., 3 * width : 4 * width])
    low_rank = jnp.tanh(aggregated[..., 4 * width :]).astype(bf16)
    decay_rate = heads_of(
        jnp.exp(
            -jnp.exp(
                attenuation_doublelog_anchor
                + jnp.dot(low_rank, attenuation_narrow_raising, preferred_element_type=f32)
            )
        )
    )
    projected = (recept, key_vec, valued, decay_rate, heads_of(gate_act))
    params = jnp.stack([instant_premium, norming_multiplier, norming_intercept]).reshape(
        3, heads_here, SUBSPACE_EXTENT
    )
    mixed_heads, payload = run_recurrence(projected, params, stream_kept_tableaux)
    combined_response = mixed_heads.reshape(steps, local_rows, width)
    pieces = payload.shape[1]
    moved_terms = route_to_slots(
        payload.transpose(0, 2, 1, 3).reshape(local_rows, heads_here, pieces * SUBSPACE_EXTENT),
        position_mapping_target,
        batch_index,
        head_index,
    )
    slots_dev, columns, _ = moved_terms.shape
    moved_terms = moved_terms.reshape(slots_dev, columns, pieces, SUBSPACE_EXTENT).transpose(
        0, 2, 1, 3
    )
    final_state = rebuild_state(moved_state, moved_terms, steps)

    gathered = exchange_copies(combined_response, "batch").transpose(1, 0, 2, 3)
    gathered = gathered.reshape(steps, sessions, width)
    inverse = jnp.argsort(position_mapping_target)
    arranged = jnp.concatenate(
        [gathered[:STEPS_A], jnp.take(gathered[STEPS_A:], inverse, axis=1, mode="clip")], axis=0
    )
    partial_y = jnp.einsum(
        "tnf,fo->tno", arranged, outgoing_linear_map, preferred_element_type=f32
    ).astype(bf16)
    head_count = lax.axis_size("head")
    produced = exchange_sum(
        partial_y.reshape(steps, head_count, sessions // head_count, -1).transpose(1, 0, 2, 3),
        "head",
    ).astype(bf16)
    return (produced[:STEPS_A], produced[STEPS_A:], final_state)


def solution(mesh):
    in_specs = (
        P(None, "groups", "batch"),
        P("groups", "batch"),
        P(("groups", "batch"), "head", None),
        P("groups"),
        P(None, "batch"),
        P("batch", None),
        P(None, None, "batch"),
        P(None, "batch", "head"),
        P("batch", None),
        P(None, "head"),
        P("head"),
        P("head"),
        P("head"),
        P("head"),
        P("head", "batch"),
    )
    out_specs = (
        P(None, ("groups", "head"), "batch"),
        P(None, ("groups", "head"), "batch"),
        P(("groups", "batch", "head"), None, None),
    )
    return jax.shard_map(
        per_device, mesh=mesh, in_specs=in_specs, out_specs=out_specs, check_vma=False
    )
```

```python
import functools

import jax
import jax.numpy as jnp
from jax import lax
from jax.experimental import pallas as pl
from jax.experimental.pallas import tpu as pltpu
from jax.sharding import PartitionSpec as P

SUBSPACE_EXTENT = 64
STEPS_A = 2
MIX_MAPS = 5
NORMALIZER_GUARD = 0.00064


def route_to_slots(value, position_mapping_target, batch_index, head_index):
    batch_count = lax.axis_size("batch")
    head_count = lax.axis_size("head")
    local_rows, heads_here, width = value.shape
    cluster_number = head_count // 4
    slots_dev = local_rows // cluster_number
    per_pair = slots_dev // batch_count
    quarter = heads_here // 4
    own_map = lax.dynamic_slice_in_dim(
        position_mapping_target, batch_index * local_rows, local_rows
    )
    send_order = jnp.argsort(own_map // slots_dev, stable=True)
    dest = jnp.arange(batch_count * head_count, dtype=jnp.int32)
    dest_block = (dest // head_count) * cluster_number + dest % cluster_number
    quad = (dest % head_count) // cluster_number
    pair = jnp.arange(per_pair, dtype=jnp.int32)
    within = jnp.arange(quarter, dtype=jnp.int32)
    sent_sessions = jnp.take(
        send_order, dest_block[:, None] * per_pair + pair[None, :], mode="clip"
    )
    sent_rows = (
        sent_sessions[:, :, None] * heads_here
        + (quad * quarter)[:, None, None]
        + within[None, None, :]
    )
    packed = jnp.take(
        value.reshape(local_rows * heads_here, width), sent_rows.reshape(-1), axis=0, mode="clip"
    ).reshape(batch_count * head_count, per_pair * quarter, width)
    arrived = lax.all_to_all(packed, ("batch", "head"), split_axis=0, concat_axis=0, tiled=True)
    target = batch_index * cluster_number + head_index % cluster_number
    arrivals = lax.dynamic_slice_in_dim(
        jnp.argsort(position_mapping_target // slots_dev, stable=True),
        target * slots_dev,
        slots_dev,
    )
    placing = jnp.argsort(jnp.take(position_mapping_target, arrivals, mode="clip") % slots_dev)
    source_head = jnp.arange(head_count, dtype=jnp.int32)
    kept_rows = (
        (
            (placing[:, None, None] // per_pair) * head_count + source_head[None, :, None]
        )
        * per_pair
        + placing[:, None, None] % per_pair
    ) * quarter + within[None, None, :]
    return jnp.take(
        arrived.reshape(-1, width), kept_rows.reshape(-1), axis=0, mode="clip"
    ).reshape(slots_dev, head_count * quarter, width)

def exchange_sum(pieces, axis_name):
    arrived = lax.all_to_all(pieces, axis_name, split_axis=0, concat_axis=0, tiled=True)
    return jnp.sum(arrived.astype(jnp.float32), axis=0)


def exchange_copies(value, axis_name):
    count = lax.axis_size(axis_name)
    copies = jnp.broadcast_to(value[None], (count,) + value.shape)
    return lax.all_to_all(copies, axis_name, split_axis=0, concat_axis=0, tiled=True)


def widen(value):
    return value.astype(jnp.bfloat16).astype(jnp.float32)


def fill_tables(spread_ref, tile_ref=None):
    extent = SUBSPACE_EXTENT

    @pl.when(pl.program_id(0) == 0)
    def _():
        lane = lax.broadcasted_iota(jnp.int32, spread_ref.shape, 1)
        row = lax.broadcasted_iota(jnp.int32, spread_ref.shape, 0)
        spread_ref[...] = (lane // extent == row).astype(spread_ref.dtype)
        if tile_ref is not None:
            tile_ref[...] = (lane % extent == row).astype(tile_ref.dtype)


def recurrence_kernel(
    steps,
    recept_ref,
    key_ref,
    value_ref,
    decay_ref,
    gate_ref,
    params_ref,
    state_ref,
    mixed_ref,
    payload_ref,
    spread_ref,
):
    extent = SUBSPACE_EXTENT
    fill_tables(spread_ref)
    spread = spread_ref[...]
    state = state_ref[...]
    premium = params_ref[0]
    gain = params_ref[1]
    bias = params_ref[2]
    recept = [recept_ref[t] for t in range(steps)]
    key_vec = [key_ref[t] for t in range(steps)]
    valued = [value_ref[t] for t in range(steps)]
    decay_rate = [decay_ref[t] for t in range(steps)]
    flat = state.shape[-1]
    prefix = jnp.ones_like(recept[0])
    for t in range(steps):
        query = recept[t] * prefix
        high = query.astype(jnp.bfloat16)
        rest = query - high.astype(jnp.float32)
        middle = rest.astype(jnp.bfloat16)
        low = (rest - middle.astype(jnp.float32)).astype(jnp.bfloat16)
        spread_query = (
            jnp.dot(high, spread, preferred_element_type=jnp.float32)
            + jnp.dot(middle, spread, preferred_element_type=jnp.float32)
            + jnp.dot(low, spread, preferred_element_type=jnp.float32)
        )
        weighted = spread_query * state
        folded = weighted[:, 0:128]
        for c in range(1, flat // 128):
            folded = folded + weighted[:, 128 * c : 128 * (c + 1)]
        from_state = folded[:, :extent] + folded[:, extent:]
        bonus_term = jnp.sum(recept[t] * premium * key_vec[t], axis=-1, keepdims=True)
        total = bonus_term * valued[t] + from_state
        for s in range(t):
            factor = key_vec[s]
            for u in range(s + 1, t):
                factor = factor * decay_rate[u]
            total = total + jnp.sum(recept[t] * factor, axis=-1, keepdims=True) * valued[s]
        average = jnp.mean(total, axis=-1, keepdims=True)
        demeaned = total - average
        spread_squared = jnp.mean(demeaned * demeaned, axis=-1, keepdims=True)
        standardized = demeaned * lax.rsqrt(spread_squared + NORMALIZER_GUARD) * gain + bias
        mixed_ref[t] = (standardized * gate_ref[t]).astype(mixed_ref.dtype)
        prefix = prefix * decay_rate[t]
    payload_ref[0] = prefix.astype(payload_ref.dtype)
    for s in range(steps):
        factor = key_vec[s]
        for u in range(s + 1, steps):
            factor = factor * decay_rate[u]
        payload_ref[1 + s] = factor.astype(payload_ref.dtype)
        payload_ref[1 + steps + s] = valued[s].astype(payload_ref.dtype)


def row_block(rows):
    return 64 if rows % 64 == 0 else rows


def run_recurrence(projected, params, state):
    pieces = len(projected)
    steps, rows, extent = projected[0].shape
    flat = state.shape[-1]
    block = row_block(rows)
    return pl.pallas_call(
        functools.partial(recurrence_kernel, steps),
        grid=(rows // block,),
        in_specs=[
            *[pl.BlockSpec((steps, block, extent), lambda n: (0, n, 0))] * pieces,
            pl.BlockSpec((3, block, extent), lambda n: (0, n, 0)),
            pl.BlockSpec((block, flat), lambda n: (n, 0)),
        ],
        out_specs=[
            pl.BlockSpec((steps, block, extent), lambda n: (0, n, 0)),
            pl.BlockSpec((1 + 2 * steps, block, extent), lambda n: (0, n, 0)),
        ],
        out_shape=[
            jax.ShapeDtypeStruct((steps, rows, extent), jnp.bfloat16),
            jax.ShapeDtypeStruct((1 + 2 * steps, rows, extent), jnp.bfloat16),
        ],
        scratch_shapes=[pltpu.VMEM((extent, flat), jnp.bfloat16)],
        cost_estimate=pl.CostEstimate(
            flops=2 * rows * extent * flat * 3 * steps,
            transcendentals=steps * rows,
            bytes_accessed=rows * (flat * 4 + extent * (pieces * steps * 4 + 3 * 4 + steps * 2 + (1 + 2 * steps) * 2)),
        ),
    )(*projected, params, state)


def rebuild_kernel(steps, state_ref, terms_ref, out_ref, spread_ref, tile_ref):
    fill_tables(spread_ref, tile_ref)
    spread = spread_ref[...]
    tile = tile_ref[...]
    total = jnp.dot(terms_ref[0], spread, preferred_element_type=jnp.float32) * state_ref[...].astype(
        jnp.float32
    )
    for s in range(steps):
        total = total + jnp.dot(
            terms_ref[1 + s], spread, preferred_element_type=jnp.float32
        ) * jnp.dot(terms_ref[1 + steps + s], tile, preferred_element_type=jnp.float32)
    out_ref[...] = total


def rebuild_state(moved_state, moved_terms, steps):
    rows, flat = moved_state.shape
    pieces = moved_terms.shape[0]
    extent = SUBSPACE_EXTENT
    block = row_block(rows)
    return pl.pallas_call(
        functools.partial(rebuild_kernel, steps),
        grid=(rows // block,),
        in_specs=[
            pl.BlockSpec((block, flat), lambda n: (n, 0)),
            pl.BlockSpec((pieces, block, extent), lambda n: (0, n, 0)),
        ],
        out_specs=pl.BlockSpec((block, flat), lambda n: (n, 0)),
        out_shape=jax.ShapeDtypeStruct((rows, flat), jnp.float32),
        scratch_shapes=[
            pltpu.VMEM((extent, flat), jnp.bfloat16),
            pltpu.VMEM((extent, flat), jnp.bfloat16),
        ],
        cost_estimate=pl.CostEstimate(
            flops=2 * rows * extent * flat * (1 + 2 * steps),
            transcendentals=0,
            bytes_accessed=rows * (flat * 6 + pieces * extent * 2),
        ),
    )(moved_state, moved_terms)


def per_device(
    tier_feed_tensor,
    preceding_feed_each_stream,
    stream_kept_tableaux,
    position_mapping_target,
    lagging_mixture_weights,
    lagging_narrow_lowering,
    lagging_narrow_raising,
    fourfold_linear_maps,
    attenuation_narrow_lowering,
    attenuation_narrow_raising,
    attenuation_doublelog_anchor,
    instant_premium,
    norming_multiplier,
    norming_intercept,
    outgoing_linear_map,
):
    batch_count = lax.axis_size("batch")
    batch_index = lax.axis_index("batch")
    head_index = lax.axis_index("head")
    steps, sessions, feats = tier_feed_tensor.shape
    local_rows = sessions // batch_count
    heads_here = stream_kept_tableaux.shape[1]
    width = heads_here * SUBSPACE_EXTENT
    f32 = jnp.float32
    bf16 = jnp.bfloat16

    moved_state = route_to_slots(
        stream_kept_tableaux.astype(bf16), position_mapping_target, batch_index, head_index
    )

    previous = jnp.concatenate([preceding_feed_each_stream[None], tier_feed_tensor[:-1]], axis=0)

    def by_block(value):
        return value.reshape(steps, batch_count, local_rows, feats).transpose(1, 0, 2, 3).reshape(
            batch_count * steps * local_rows, feats
        )

    x_float = by_block(tier_feed_tensor).astype(f32)
    shifted = by_block(previous).astype(f32) - x_float
    rows = x_float.shape[0]
    base_mix = (x_float + shifted * lagging_mixture_weights[0]).astype(bf16)
    partial_value = jnp.dot(base_mix, lagging_narrow_lowering, preferred_element_type=f32)
    hidden = jnp.tanh(
        jnp.sum(exchange_copies(partial_value.astype(bf16), "batch").astype(f32), axis=0)
    ).astype(bf16)
    hidden = hidden.reshape(rows, MIX_MAPS, lagging_narrow_raising.shape[1])
    offsets = jnp.einsum(
        "nim,imd->ind", hidden, lagging_narrow_raising, preferred_element_type=f32
    )
    mixed = (
        x_float[None] + shifted[None] * (lagging_mixture_weights[1:, None, :] + offsets)
    ).astype(bf16)
    main_part = jnp.einsum(
        "inf,ifc->nic", mixed[:4], fourfold_linear_maps, preferred_element_type=f32
    )
    decay_part = jnp.dot(mixed[4], attenuation_narrow_lowering, preferred_element_type=f32)
    aggregated = exchange_sum(
        jnp.concatenate([main_part.reshape(rows, -1), decay_part], axis=1)
        .astype(bf16)
        .reshape(batch_count, steps, local_rows, -1),
        "batch",
    )

    def heads_of(value):
        return value.reshape(steps, local_rows, heads_here, SUBSPACE_EXTENT)

    recept = heads_of(widen(aggregated[..., :width]))
    key_vec = heads_of(widen(aggregated[..., width : 2 * width]))
    valued = heads_of(widen(aggregated[..., 2 * width : 3 * width]))
    gate_act = jax.nn.silu(aggregated[..., 3 * width : 4 * width])
    low_rank = jnp.tanh(aggregated[..., 4 * width :]).astype(bf16)
    decay_rate = heads_of(
        jnp.exp(
            -jnp.exp(
                attenuation_doublelog_anchor
                + jnp.dot(low_rank, attenuation_narrow_raising, preferred_element_type=f32)
            )
        )
    )
    rows_here = local_rows * heads_here

    def by_row(value):
        return value.reshape(steps, rows_here, SUBSPACE_EXTENT)

    projected = tuple(by_row(value) for value in (recept, key_vec, valued, decay_rate, gate_act))
    params = jnp.broadcast_to(
        jnp.stack([instant_premium, norming_multiplier, norming_intercept]).reshape(
            3, 1, heads_here, SUBSPACE_EXTENT
        ),
        (3, local_rows, heads_here, SUBSPACE_EXTENT),
    ).reshape(3, rows_here, SUBSPACE_EXTENT)
    mixed_rows, payload = run_recurrence(
        projected, params, stream_kept_tableaux.reshape(rows_here, -1)
    )
    combined_response = mixed_rows.reshape(steps, local_rows, width)
    pieces = payload.shape[0]
    moved_terms = route_to_slots(
        payload.reshape(pieces, local_rows, heads_here, SUBSPACE_EXTENT)
        .transpose(1, 2, 0, 3)
        .reshape(local_rows, heads_here, pieces * SUBSPACE_EXTENT),
        position_mapping_target,
        batch_index,
        head_index,
    )
    slots_dev, columns, _ = moved_terms.shape
    moved_terms = (
        moved_terms.reshape(slots_dev, columns, pieces, SUBSPACE_EXTENT)
        .transpose(2, 0, 1, 3)
        .reshape(pieces, slots_dev * columns, SUBSPACE_EXTENT)
    )
    final_state = rebuild_state(
        moved_state.reshape(slots_dev * columns, -1), moved_terms, steps
    ).reshape(slots_dev, columns, -1)

    gathered = exchange_copies(combined_response, "batch").transpose(1, 0, 2, 3)
    gathered = gathered.reshape(steps, sessions, width)
    inverse = jnp.argsort(position_mapping_target)
    arranged = jnp.concatenate(
        [gathered[:STEPS_A], jnp.take(gathered[STEPS_A:], inverse, axis=1, mode="clip")], axis=0
    )
    partial_y = jnp.einsum(
        "tnf,fo->tno", arranged, outgoing_linear_map, preferred_element_type=f32
    ).astype(bf16)
    head_count = lax.axis_size("head")
    produced = exchange_sum(
        partial_y.reshape(steps, head_count, sessions // head_count, -1).transpose(1, 0, 2, 3),
        "head",
    ).astype(bf16)
    return (produced[:STEPS_A], produced[STEPS_A:], final_state)


def solution(mesh):
    in_specs = (
        P(None, "groups", "batch"),
        P("groups", "batch"),
        P(("groups", "batch"), "head", None),
        P("groups"),
        P(None, "batch"),
        P("batch", None),
        P(None, None, "batch"),
        P(None, "batch", "head"),
        P("batch", None),
        P(None, "head"),
        P("head"),
        P("head"),
        P("head"),
        P("head"),
        P("head", "batch"),
    )
    out_specs = (
        P(None, ("groups", "head"), "batch"),
        P(None, ("groups", "head"), "batch"),
        P(("groups", "batch", "head"), None, None),
    )
    return jax.shard_map(
        per_device, mesh=mesh, in_specs=in_specs, out_specs=out_specs, check_vma=False
    )
```

```python
import functools

import jax
import jax.numpy as jnp
from jax import lax
from jax.experimental import pallas as pl
from jax.experimental.pallas import tpu as pltpu
from jax.sharding import PartitionSpec as P

SUBSPACE_EXTENT = 64
STEPS_A = 2
MIX_MAPS = 5
NORMALIZER_GUARD = 0.00064


def route_to_slots(value, position_mapping_target, batch_index, head_index):
    batch_count = lax.axis_size("batch")
    head_count = lax.axis_size("head")
    local_rows, heads_here, width = value.shape
    cluster_number = head_count // 4
    slots_dev = local_rows // cluster_number
    per_pair = slots_dev // batch_count
    quarter = heads_here // 4
    own_map = lax.dynamic_slice_in_dim(
        position_mapping_target, batch_index * local_rows, local_rows
    )
    send_order = jnp.argsort(own_map // slots_dev, stable=True)
    dest = jnp.arange(batch_count * head_count, dtype=jnp.int32)
    dest_block = (dest // head_count) * cluster_number + dest % cluster_number
    quad = (dest % head_count) // cluster_number
    pair = jnp.arange(per_pair, dtype=jnp.int32)
    within = jnp.arange(quarter, dtype=jnp.int32)
    sent_sessions = jnp.take(
        send_order, dest_block[:, None] * per_pair + pair[None, :], mode="clip"
    )
    sent_rows = (
        sent_sessions[:, :, None] * heads_here
        + (quad * quarter)[:, None, None]
        + within[None, None, :]
    )
    packed = jnp.take(
        value.reshape(local_rows * heads_here, width), sent_rows.reshape(-1), axis=0, mode="clip"
    ).reshape(batch_count * head_count, per_pair * quarter, width)
    arrived = lax.all_to_all(packed, ("batch", "head"), split_axis=0, concat_axis=0, tiled=True)
    target = batch_index * cluster_number + head_index % cluster_number
    arrivals = lax.dynamic_slice_in_dim(
        jnp.argsort(position_mapping_target // slots_dev, stable=True),
        target * slots_dev,
        slots_dev,
    )
    placing = jnp.argsort(jnp.take(position_mapping_target, arrivals, mode="clip") % slots_dev)
    source_head = jnp.arange(head_count, dtype=jnp.int32)
    kept_rows = (
        (
            (placing[:, None, None] // per_pair) * head_count + source_head[None, :, None]
        )
        * per_pair
        + placing[:, None, None] % per_pair
    ) * quarter + within[None, None, :]
    return jnp.take(
        arrived.reshape(-1, width), kept_rows.reshape(-1), axis=0, mode="clip"
    ).reshape(slots_dev, head_count * quarter, width)

def exchange_sum(pieces, axis_name):
    arrived = lax.all_to_all(pieces, axis_name, split_axis=0, concat_axis=0, tiled=True)
    return jnp.sum(arrived.astype(jnp.float32), axis=0)


def exchange_copies(value, axis_name):
    count = lax.axis_size(axis_name)
    copies = jnp.broadcast_to(value[None], (count,) + value.shape)
    return lax.all_to_all(copies, axis_name, split_axis=0, concat_axis=0, tiled=True)


def widen(value):
    return value.astype(jnp.bfloat16).astype(jnp.float32)


def fill_tables(spread_ref, tile_ref=None):
    extent = SUBSPACE_EXTENT

    @pl.when(pl.program_id(0) == 0)
    def _():
        lane = lax.broadcasted_iota(jnp.int32, spread_ref.shape, 1)
        row = lax.broadcasted_iota(jnp.int32, spread_ref.shape, 0)
        spread_ref[...] = (lane // extent == row).astype(spread_ref.dtype)
        if tile_ref is not None:
            tile_ref[...] = (lane % extent == row).astype(tile_ref.dtype)


def recurrence_kernel(
    steps,
    fourway_ref,
    decay_ref,
    params_ref,
    state_ref,
    mixed_ref,
    payload_ref,
    spread_ref,
):
    extent = SUBSPACE_EXTENT
    fill_tables(spread_ref)
    spread = spread_ref[...]
    state = state_ref[...]
    premium = params_ref[0]
    gain = params_ref[1]
    bias = params_ref[2]
    recept = [widen(fourway_ref[0, t]) for t in range(steps)]
    key_vec = [widen(fourway_ref[1, t]) for t in range(steps)]
    valued = [widen(fourway_ref[2, t]) for t in range(steps)]
    decay_rate = [decay_ref[t] for t in range(steps)]
    flat = state.shape[-1]
    prefix = jnp.ones_like(recept[0])
    for t in range(steps):
        query = recept[t] * prefix
        high = query.astype(jnp.bfloat16)
        rest = query - high.astype(jnp.float32)
        middle = rest.astype(jnp.bfloat16)
        low = (rest - middle.astype(jnp.float32)).astype(jnp.bfloat16)
        spread_query = (
            jnp.dot(high, spread, preferred_element_type=jnp.float32)
            + jnp.dot(middle, spread, preferred_element_type=jnp.float32)
            + jnp.dot(low, spread, preferred_element_type=jnp.float32)
        )
        weighted = spread_query * state
        folded = weighted[:, 0:128]
        for c in range(1, flat // 128):
            folded = folded + weighted[:, 128 * c : 128 * (c + 1)]
        from_state = folded[:, :extent] + folded[:, extent:]
        bonus_term = jnp.sum(recept[t] * premium * key_vec[t], axis=-1, keepdims=True)
        total = bonus_term * valued[t] + from_state
        for s in range(t):
            factor = key_vec[s]
            for u in range(s + 1, t):
                factor = factor * decay_rate[u]
            total = total + jnp.sum(recept[t] * factor, axis=-1, keepdims=True) * valued[s]
        average = jnp.mean(total, axis=-1, keepdims=True)
        demeaned = total - average
        spread_squared = jnp.mean(demeaned * demeaned, axis=-1, keepdims=True)
        standardized = demeaned * lax.rsqrt(spread_squared + NORMALIZER_GUARD) * gain + bias
        gate_value = fourway_ref[3, t]
        gate_act = gate_value / (1.0 + jnp.exp(-gate_value))
        mixed_ref[t] = (standardized * gate_act).astype(mixed_ref.dtype)
        prefix = prefix * decay_rate[t]
    payload_ref[0] = prefix.astype(payload_ref.dtype)
    for s in range(steps):
        factor = key_vec[s]
        for u in range(s + 1, steps):
            factor = factor * decay_rate[u]
        payload_ref[1 + s] = factor.astype(payload_ref.dtype)
        payload_ref[1 + steps + s] = valued[s].astype(payload_ref.dtype)


def row_block(rows):
    return 64 if rows % 64 == 0 else rows


def run_recurrence(fourway, decay_rate, params, state):
    pieces = fourway.shape[0] + 1
    steps, rows, extent = decay_rate.shape
    flat = state.shape[-1]
    block = row_block(rows)
    return pl.pallas_call(
        functools.partial(recurrence_kernel, steps),
        grid=(rows // block,),
        in_specs=[
            pl.BlockSpec((pieces - 1, steps, block, extent), lambda n: (0, 0, n, 0)),
            pl.BlockSpec((steps, block, extent), lambda n: (0, n, 0)),
            pl.BlockSpec((3, block, extent), lambda n: (0, n, 0)),
            pl.BlockSpec((block, flat), lambda n: (n, 0)),
        ],
        out_specs=[
            pl.BlockSpec((steps, block, extent), lambda n: (0, n, 0)),
            pl.BlockSpec((1 + 2 * steps, block, extent), lambda n: (0, n, 0)),
        ],
        out_shape=[
            jax.ShapeDtypeStruct((steps, rows, extent), jnp.bfloat16),
            jax.ShapeDtypeStruct((1 + 2 * steps, rows, extent), jnp.bfloat16),
        ],
        scratch_shapes=[pltpu.VMEM((extent, flat), jnp.bfloat16)],
        cost_estimate=pl.CostEstimate(
            flops=2 * rows * extent * flat * 3 * steps,
            transcendentals=steps * rows,
            bytes_accessed=rows * (flat * 4 + extent * (pieces * steps * 4 + 3 * 4 + steps * 2 + (1 + 2 * steps) * 2)),
        ),
    )(fourway, decay_rate, params, state)


def rebuild_kernel(steps, state_ref, terms_ref, out_ref, spread_ref, tile_ref):
    fill_tables(spread_ref, tile_ref)
    spread = spread_ref[...]
    tile = tile_ref[...]
    total = jnp.dot(terms_ref[0], spread, preferred_element_type=jnp.float32) * state_ref[...].astype(
        jnp.float32
    )
    for s in range(steps):
        total = total + jnp.dot(
            terms_ref[1 + s], spread, preferred_element_type=jnp.float32
        ) * jnp.dot(terms_ref[1 + steps + s], tile, preferred_element_type=jnp.float32)
    out_ref[...] = total


def rebuild_state(moved_state, moved_terms, steps):
    rows, flat = moved_state.shape
    pieces = moved_terms.shape[0]
    extent = SUBSPACE_EXTENT
    block = row_block(rows)
    return pl.pallas_call(
        functools.partial(rebuild_kernel, steps),
        grid=(rows // block,),
        in_specs=[
            pl.BlockSpec((block, flat), lambda n: (n, 0)),
            pl.BlockSpec((pieces, block, extent), lambda n: (0, n, 0)),
        ],
        out_specs=pl.BlockSpec((block, flat), lambda n: (n, 0)),
        out_shape=jax.ShapeDtypeStruct((rows, flat), jnp.float32),
        scratch_shapes=[
            pltpu.VMEM((extent, flat), jnp.bfloat16),
            pltpu.VMEM((extent, flat), jnp.bfloat16),
        ],
        cost_estimate=pl.CostEstimate(
            flops=2 * rows * extent * flat * (1 + 2 * steps),
            transcendentals=0,
            bytes_accessed=rows * (flat * 6 + pieces * extent * 2),
        ),
    )(moved_state, moved_terms)


def per_device(
    tier_feed_tensor,
    preceding_feed_each_stream,
    stream_kept_tableaux,
    position_mapping_target,
    lagging_mixture_weights,
    lagging_narrow_lowering,
    lagging_narrow_raising,
    fourfold_linear_maps,
    attenuation_narrow_lowering,
    attenuation_narrow_raising,
    attenuation_doublelog_anchor,
    instant_premium,
    norming_multiplier,
    norming_intercept,
    outgoing_linear_map,
):
    batch_count = lax.axis_size("batch")
    batch_index = lax.axis_index("batch")
    head_index = lax.axis_index("head")
    steps, sessions, feats = tier_feed_tensor.shape
    local_rows = sessions // batch_count
    heads_here = stream_kept_tableaux.shape[1]
    width = heads_here * SUBSPACE_EXTENT
    f32 = jnp.float32
    bf16 = jnp.bfloat16


    previous = jnp.concatenate([preceding_feed_each_stream[None], tier_feed_tensor[:-1]], axis=0)

    def by_block(value):
        return value.reshape(steps, batch_count, local_rows, feats).transpose(1, 0, 2, 3).reshape(
            batch_count * steps * local_rows, feats
        )

    x_float = by_block(tier_feed_tensor).astype(f32)
    shifted = by_block(previous).astype(f32) - x_float
    rows = x_float.shape[0]
    base_mix = (x_float + shifted * lagging_mixture_weights[0]).astype(bf16)
    partial_value = jnp.dot(base_mix, lagging_narrow_lowering, preferred_element_type=f32)
    hidden = jnp.tanh(
        jnp.sum(exchange_copies(partial_value.astype(bf16), "batch").astype(f32), axis=0)
    ).astype(bf16)
    hidden = hidden.reshape(rows, MIX_MAPS, lagging_narrow_raising.shape[1])
    offsets = jnp.einsum(
        "nim,imd->ind", hidden, lagging_narrow_raising, preferred_element_type=f32
    )
    mixed = (
        x_float[None] + shifted[None] * (lagging_mixture_weights[1:, None, :] + offsets)
    ).astype(bf16)
    main_part = jnp.einsum(
        "inf,ifc->nic", mixed[:4], fourfold_linear_maps, preferred_element_type=f32
    )
    decay_part = jnp.dot(mixed[4], attenuation_narrow_lowering, preferred_element_type=f32)
    aggregated = exchange_sum(
        jnp.concatenate([main_part.reshape(rows, -1), decay_part], axis=1)
        .astype(bf16)
        .reshape(batch_count, steps, local_rows, -1),
        "batch",
    )

    kept_for_move, aggregated = lax.optimization_barrier((stream_kept_tableaux, aggregated))
    moved_state = route_to_slots(
        kept_for_move.astype(bf16), position_mapping_target, batch_index, head_index
    )

    def heads_of(value):
        return value.reshape(steps, local_rows, heads_here, SUBSPACE_EXTENT)

    low_rank = jnp.tanh(aggregated[..., 4 * width :]).astype(bf16)
    decay_rate = heads_of(
        jnp.exp(
            -jnp.exp(
                attenuation_doublelog_anchor
                + jnp.dot(low_rank, attenuation_narrow_raising, preferred_element_type=f32)
            )
        )
    )
    rows_here = local_rows * heads_here

    def by_row(value):
        return value.reshape(steps, rows_here, SUBSPACE_EXTENT)

    fourway = (
        aggregated[..., : 4 * width]
        .reshape(steps, local_rows, 4, heads_here, SUBSPACE_EXTENT)
        .transpose(2, 0, 1, 3, 4)
        .reshape(4, steps, rows_here, SUBSPACE_EXTENT)
    )
    params = jnp.broadcast_to(
        jnp.stack([instant_premium, norming_multiplier, norming_intercept]).reshape(
            3, 1, heads_here, SUBSPACE_EXTENT
        ),
        (3, local_rows, heads_here, SUBSPACE_EXTENT),
    ).reshape(3, rows_here, SUBSPACE_EXTENT)
    mixed_rows, payload = run_recurrence(
        fourway, by_row(decay_rate), params, stream_kept_tableaux.reshape(rows_here, -1)
    )
    moved_state, mixed_rows, payload = lax.optimization_barrier((moved_state, mixed_rows, payload))
    combined_response = mixed_rows.reshape(steps, local_rows, width)
    pieces = payload.shape[0]
    moved_terms = route_to_slots(
        payload.reshape(pieces, local_rows, heads_here, SUBSPACE_EXTENT)
        .transpose(1, 2, 0, 3)
        .reshape(local_rows, heads_here, pieces * SUBSPACE_EXTENT),
        position_mapping_target,
        batch_index,
        head_index,
    )
    slots_dev, columns, _ = moved_terms.shape
    moved_terms = (
        moved_terms.reshape(slots_dev, columns, pieces, SUBSPACE_EXTENT)
        .transpose(2, 0, 1, 3)
        .reshape(pieces, slots_dev * columns, SUBSPACE_EXTENT)
    )
    combined_response, moved_terms = lax.optimization_barrier((combined_response, moved_terms))
    final_state = rebuild_state(
        moved_state.reshape(slots_dev * columns, -1), moved_terms, steps
    ).reshape(slots_dev, columns, -1)

    gathered = exchange_copies(combined_response, "batch").transpose(1, 0, 2, 3)
    gathered = gathered.reshape(steps, sessions, width)
    inverse = jnp.argsort(position_mapping_target)
    arranged = jnp.concatenate(
        [gathered[:STEPS_A], jnp.take(gathered[STEPS_A:], inverse, axis=1, mode="clip")], axis=0
    )
    partial_y = jnp.einsum(
        "tnf,fo->tno", arranged, outgoing_linear_map, preferred_element_type=f32
    ).astype(bf16)
    head_count = lax.axis_size("head")
    produced = exchange_sum(
        partial_y.reshape(steps, head_count, sessions // head_count, -1).transpose(1, 0, 2, 3),
        "head",
    ).astype(bf16)
    return (produced[:STEPS_A], produced[STEPS_A:], final_state)


def solution(mesh):
    in_specs = (
        P(None, "groups", "batch"),
        P("groups", "batch"),
        P(("groups", "batch"), "head", None),
        P("groups"),
        P(None, "batch"),
        P("batch", None),
        P(None, None, "batch"),
        P(None, "batch", "head"),
        P("batch", None),
        P(None, "head"),
        P("head"),
        P("head"),
        P("head"),
        P("head"),
        P("head", "batch"),
    )
    out_specs = (
        P(None, ("groups", "head"), "batch"),
        P(None, ("groups", "head"), "batch"),
        P(("groups", "batch", "head"), None, None),
    )
    return jax.shard_map(
        per_device, mesh=mesh, in_specs=in_specs, out_specs=out_specs, check_vma=False
    )
```

```python
import functools

import jax
import jax.numpy as jnp
from jax import lax
from jax.experimental import pallas as pl
from jax.experimental.pallas import tpu as pltpu
from jax.sharding import PartitionSpec as P

SUBSPACE_EXTENT = 64
STEPS_A = 2
MIX_MAPS = 5
NORMALIZER_GUARD = 0.00064


def route_to_slots(value, position_mapping_target, batch_index, head_index):
    batch_count = lax.axis_size("batch")
    head_count = lax.axis_size("head")
    local_rows, heads_here, width = value.shape
    cluster_number = head_count // 4
    slots_dev = local_rows // cluster_number
    per_pair = slots_dev // batch_count
    quarter = heads_here // 4
    own_map = lax.dynamic_slice_in_dim(
        position_mapping_target, batch_index * local_rows, local_rows
    )
    send_order = jnp.argsort(own_map // slots_dev, stable=True)
    dest = jnp.arange(batch_count * head_count, dtype=jnp.int32)
    dest_block = (dest // head_count) * cluster_number + dest % cluster_number
    quad = (dest % head_count) // cluster_number
    pair = jnp.arange(per_pair, dtype=jnp.int32)
    within = jnp.arange(quarter, dtype=jnp.int32)
    sent_sessions = jnp.take(
        send_order, dest_block[:, None] * per_pair + pair[None, :], mode="clip"
    )
    sent_rows = (
        sent_sessions[:, :, None] * heads_here
        + (quad * quarter)[:, None, None]
        + within[None, None, :]
    )
    packed = jnp.take(
        value.reshape(local_rows * heads_here, width), sent_rows.reshape(-1), axis=0, mode="clip"
    ).reshape(batch_count * head_count, per_pair * quarter, width)
    arrived = lax.all_to_all(packed, ("batch", "head"), split_axis=0, concat_axis=0, tiled=True)
    target = batch_index * cluster_number + head_index % cluster_number
    arrivals = lax.dynamic_slice_in_dim(
        jnp.argsort(position_mapping_target // slots_dev, stable=True),
        target * slots_dev,
        slots_dev,
    )
    placing = jnp.argsort(jnp.take(position_mapping_target, arrivals, mode="clip") % slots_dev)
    source_head = jnp.arange(head_count, dtype=jnp.int32)
    kept_rows = (
        (
            (placing[:, None, None] // per_pair) * head_count + source_head[None, :, None]
        )
        * per_pair
        + placing[:, None, None] % per_pair
    ) * quarter + within[None, None, :]
    return jnp.take(
        arrived.reshape(-1, width), kept_rows.reshape(-1), axis=0, mode="clip"
    ).reshape(slots_dev, head_count * quarter, width)

def exchange_sum(pieces, axis_name):
    count = lax.axis_size(axis_name)
    index = lax.axis_index(axis_name)
    total = lax.dynamic_index_in_dim(pieces, index, keepdims=False).astype(jnp.float32)
    for shift in range(1, count):
        sent = lax.dynamic_index_in_dim(pieces, (index + shift) % count, keepdims=False)
        total = total + lax.ppermute(
            sent, axis_name, [(i, (i + shift) % count) for i in range(count)]
        ).astype(jnp.float32)
    return total


def exchange_copies(value, axis_name):
    count = lax.axis_size(axis_name)
    index = lax.axis_index(axis_name)
    received = [value]
    for shift in range(1, count):
        received.append(
            lax.ppermute(value, axis_name, [(i, (i + shift) % count) for i in range(count)])
        )
    shifts = (index - jnp.arange(count, dtype=jnp.int32)) % count
    return jnp.take(jnp.stack(received), shifts, axis=0, mode="clip")

def widen(value):
    return value.astype(jnp.bfloat16).astype(jnp.float32)


def fill_tables(spread_ref, tile_ref=None):
    extent = SUBSPACE_EXTENT

    @pl.when(pl.program_id(0) == 0)
    def _():
        lane = lax.broadcasted_iota(jnp.int32, spread_ref.shape, 1)
        row = lax.broadcasted_iota(jnp.int32, spread_ref.shape, 0)
        spread_ref[...] = (lane // extent == row).astype(spread_ref.dtype)
        if tile_ref is not None:
            tile_ref[...] = (lane % extent == row).astype(tile_ref.dtype)


def recurrence_kernel(
    steps,
    recept_ref,
    key_ref,
    value_ref,
    decay_ref,
    gate_ref,
    params_ref,
    state_ref,
    mixed_ref,
    payload_ref,
    spread_ref,
):
    extent = SUBSPACE_EXTENT
    fill_tables(spread_ref)
    spread = spread_ref[...]
    state = state_ref[...]
    premium = params_ref[0]
    gain = params_ref[1]
    bias = params_ref[2]
    recept = [recept_ref[t] for t in range(steps)]
    key_vec = [key_ref[t] for t in range(steps)]
    valued = [value_ref[t] for t in range(steps)]
    decay_rate = [decay_ref[t] for t in range(steps)]
    flat = state.shape[-1]
    prefix = jnp.ones_like(recept[0])
    for t in range(steps):
        query = recept[t] * prefix
        high = query.astype(jnp.bfloat16)
        rest = query - high.astype(jnp.float32)
        middle = rest.astype(jnp.bfloat16)
        low = (rest - middle.astype(jnp.float32)).astype(jnp.bfloat16)
        spread_query = (
            jnp.dot(high, spread, preferred_element_type=jnp.float32)
            + jnp.dot(middle, spread, preferred_element_type=jnp.float32)
            + jnp.dot(low, spread, preferred_element_type=jnp.float32)
        )
        weighted = spread_query * state
        folded = weighted[:, 0:128]
        for c in range(1, flat // 128):
            folded = folded + weighted[:, 128 * c : 128 * (c + 1)]
        from_state = folded[:, :extent] + folded[:, extent:]
        bonus_term = jnp.sum(recept[t] * premium * key_vec[t], axis=-1, keepdims=True)
        total = bonus_term * valued[t] + from_state
        for s in range(t):
            factor = key_vec[s]
            for u in range(s + 1, t):
                factor = factor * decay_rate[u]
            total = total + jnp.sum(recept[t] * factor, axis=-1, keepdims=True) * valued[s]
        average = jnp.mean(total, axis=-1, keepdims=True)
        demeaned = total - average
        spread_squared = jnp.mean(demeaned * demeaned, axis=-1, keepdims=True)
        standardized = demeaned * lax.rsqrt(spread_squared + NORMALIZER_GUARD) * gain + bias
        mixed_ref[t] = (standardized * gate_ref[t]).astype(mixed_ref.dtype)
        prefix = prefix * decay_rate[t]
    payload_ref[0] = prefix.astype(payload_ref.dtype)
    for s in range(steps):
        factor = key_vec[s]
        for u in range(s + 1, steps):
            factor = factor * decay_rate[u]
        payload_ref[1 + s] = factor.astype(payload_ref.dtype)
        payload_ref[1 + steps + s] = valued[s].astype(payload_ref.dtype)


def row_block(rows):
    return 64 if rows % 64 == 0 else rows


def run_recurrence(projected, params, state):
    pieces = len(projected)
    steps, rows, extent = projected[0].shape
    flat = state.shape[-1]
    block = row_block(rows)
    return pl.pallas_call(
        functools.partial(recurrence_kernel, steps),
        grid=(rows // block,),
        in_specs=[
            *[pl.BlockSpec((steps, block, extent), lambda n: (0, n, 0))] * pieces,
            pl.BlockSpec((3, block, extent), lambda n: (0, n, 0)),
            pl.BlockSpec((block, flat), lambda n: (n, 0)),
        ],
        out_specs=[
            pl.BlockSpec((steps, block, extent), lambda n: (0, n, 0)),
            pl.BlockSpec((1 + 2 * steps, block, extent), lambda n: (0, n, 0)),
        ],
        out_shape=[
            jax.ShapeDtypeStruct((steps, rows, extent), jnp.bfloat16),
            jax.ShapeDtypeStruct((1 + 2 * steps, rows, extent), jnp.bfloat16),
        ],
        scratch_shapes=[pltpu.VMEM((extent, flat), jnp.bfloat16)],
        cost_estimate=pl.CostEstimate(
            flops=2 * rows * extent * flat * 3 * steps,
            transcendentals=steps * rows,
            bytes_accessed=rows * (flat * 4 + extent * (pieces * steps * 4 + 3 * 4 + steps * 2 + (1 + 2 * steps) * 2)),
        ),
    )(*projected, params, state)


def rebuild_kernel(steps, state_ref, terms_ref, out_ref, spread_ref, tile_ref):
    fill_tables(spread_ref, tile_ref)
    spread = spread_ref[...]
    tile = tile_ref[...]
    total = jnp.dot(terms_ref[0], spread, preferred_element_type=jnp.float32) * state_ref[...].astype(
        jnp.float32
    )
    for s in range(steps):
        total = total + jnp.dot(
            terms_ref[1 + s], spread, preferred_element_type=jnp.float32
        ) * jnp.dot(terms_ref[1 + steps + s], tile, preferred_element_type=jnp.float32)
    out_ref[...] = total


def rebuild_state(moved_state, moved_terms, steps):
    rows, flat = moved_state.shape
    pieces = moved_terms.shape[0]
    extent = SUBSPACE_EXTENT
    block = row_block(rows)
    return pl.pallas_call(
        functools.partial(rebuild_kernel, steps),
        grid=(rows // block,),
        in_specs=[
            pl.BlockSpec((block, flat), lambda n: (n, 0)),
            pl.BlockSpec((pieces, block, extent), lambda n: (0, n, 0)),
        ],
        out_specs=pl.BlockSpec((block, flat), lambda n: (n, 0)),
        out_shape=jax.ShapeDtypeStruct((rows, flat), jnp.float32),
        scratch_shapes=[
            pltpu.VMEM((extent, flat), jnp.bfloat16),
            pltpu.VMEM((extent, flat), jnp.bfloat16),
        ],
        cost_estimate=pl.CostEstimate(
            flops=2 * rows * extent * flat * (1 + 2 * steps),
            transcendentals=0,
            bytes_accessed=rows * (flat * 6 + pieces * extent * 2),
        ),
    )(moved_state, moved_terms)


def per_device(
    tier_feed_tensor,
    preceding_feed_each_stream,
    stream_kept_tableaux,
    position_mapping_target,
    lagging_mixture_weights,
    lagging_narrow_lowering,
    lagging_narrow_raising,
    fourfold_linear_maps,
    attenuation_narrow_lowering,
    attenuation_narrow_raising,
    attenuation_doublelog_anchor,
    instant_premium,
    norming_multiplier,
    norming_intercept,
    outgoing_linear_map,
):
    batch_count = lax.axis_size("batch")
    batch_index = lax.axis_index("batch")
    head_index = lax.axis_index("head")
    steps, sessions, feats = tier_feed_tensor.shape
    local_rows = sessions // batch_count
    heads_here = stream_kept_tableaux.shape[1]
    width = heads_here * SUBSPACE_EXTENT
    f32 = jnp.float32
    bf16 = jnp.bfloat16

    moved_state = route_to_slots(
        stream_kept_tableaux.astype(bf16), position_mapping_target, batch_index, head_index
    )

    previous = jnp.concatenate([preceding_feed_each_stream[None], tier_feed_tensor[:-1]], axis=0)

    def by_block(value):
        return value.reshape(steps, batch_count, local_rows, feats).transpose(1, 0, 2, 3).reshape(
            batch_count * steps * local_rows, feats
        )

    x_float = by_block(tier_feed_tensor).astype(f32)
    shifted = by_block(previous).astype(f32) - x_float
    rows = x_float.shape[0]
    base_mix = (x_float + shifted * lagging_mixture_weights[0]).astype(bf16)
    partial_value = jnp.dot(base_mix, lagging_narrow_lowering, preferred_element_type=f32)
    hidden = jnp.tanh(
        jnp.sum(exchange_copies(partial_value.astype(bf16), "batch").astype(f32), axis=0)
    ).astype(bf16)
    hidden = hidden.reshape(rows, MIX_MAPS, lagging_narrow_raising.shape[1])
    offsets = jnp.einsum(
        "nim,imd->ind", hidden, lagging_narrow_raising, preferred_element_type=f32
    )
    mixed = (
        x_float[None] + shifted[None] * (lagging_mixture_weights[1:, None, :] + offsets)
    ).astype(bf16)
    main_part = jnp.einsum(
        "inf,ifc->nic", mixed[:4], fourfold_linear_maps, preferred_element_type=f32
    )
    decay_part = jnp.dot(mixed[4], attenuation_narrow_lowering, preferred_element_type=f32)
    aggregated = exchange_sum(
        jnp.concatenate([main_part.reshape(rows, -1), decay_part], axis=1)
        .astype(bf16)
        .reshape(batch_count, steps, local_rows, -1),
        "batch",
    )

    def heads_of(value):
        return value.reshape(steps, local_rows, heads_here, SUBSPACE_EXTENT)

    recept = heads_of(widen(aggregated[..., :width]))
    key_vec = heads_of(widen(aggregated[..., width : 2 * width]))
    valued = heads_of(widen(aggregated[..., 2 * width : 3 * width]))
    gate_act = jax.nn.silu(aggregated[..., 3 * width : 4 * width])
    low_rank = jnp.tanh(aggregated[..., 4 * width :]).astype(bf16)
    decay_rate = heads_of(
        jnp.exp(
            -jnp.exp(
                attenuation_doublelog_anchor
                + jnp.dot(low_rank, attenuation_narrow_raising, preferred_element_type=f32)
            )
        )
    )
    rows_here = local_rows * heads_here

    def by_row(value):
        return value.reshape(steps, rows_here, SUBSPACE_EXTENT)

    projected = tuple(by_row(value) for value in (recept, key_vec, valued, decay_rate, gate_act))
    params = jnp.broadcast_to(
        jnp.stack([instant_premium, norming_multiplier, norming_intercept]).reshape(
            3, 1, heads_here, SUBSPACE_EXTENT
        ),
        (3, local_rows, heads_here, SUBSPACE_EXTENT),
    ).reshape(3, rows_here, SUBSPACE_EXTENT)
    mixed_rows, payload = run_recurrence(
        projected, params, stream_kept_tableaux.reshape(rows_here, -1)
    )
    combined_response = mixed_rows.reshape(steps, local_rows, width)
    pieces = payload.shape[0]
    moved_terms = route_to_slots(
        payload.reshape(pieces, local_rows, heads_here, SUBSPACE_EXTENT)
        .transpose(1, 2, 0, 3)
        .reshape(local_rows, heads_here, pieces * SUBSPACE_EXTENT),
        position_mapping_target,
        batch_index,
        head_index,
    )
    slots_dev, columns, _ = moved_terms.shape
    moved_terms = (
        moved_terms.reshape(slots_dev, columns, pieces, SUBSPACE_EXTENT)
        .transpose(2, 0, 1, 3)
        .reshape(pieces, slots_dev * columns, SUBSPACE_EXTENT)
    )
    final_state = rebuild_state(
        moved_state.reshape(slots_dev * columns, -1), moved_terms, steps
    ).reshape(slots_dev, columns, -1)

    gathered = exchange_copies(combined_response, "batch").transpose(1, 0, 2, 3)
    gathered = gathered.reshape(steps, sessions, width)
    inverse = jnp.argsort(position_mapping_target)
    arranged = jnp.concatenate(
        [gathered[:STEPS_A], jnp.take(gathered[STEPS_A:], inverse, axis=1, mode="clip")], axis=0
    )
    partial_y = jnp.einsum(
        "tnf,fo->tno", arranged, outgoing_linear_map, preferred_element_type=f32
    ).astype(bf16)
    head_count = lax.axis_size("head")
    produced = exchange_sum(
        partial_y.reshape(steps, head_count, sessions // head_count, -1).transpose(1, 0, 2, 3),
        "head",
    ).astype(bf16)
    return (produced[:STEPS_A], produced[STEPS_A:], final_state)


def solution(mesh):
    in_specs = (
        P(None, "groups", "batch"),
        P("groups", "batch"),
        P(("groups", "batch"), "head", None),
        P("groups"),
        P(None, "batch"),
        P("batch", None),
        P(None, None, "batch"),
        P(None, "batch", "head"),
        P("batch", None),
        P(None, "head"),
        P("head"),
        P("head"),
        P("head"),
        P("head"),
        P("head", "batch"),
    )
    out_specs = (
        P(None, ("groups", "head"), "batch"),
        P(None, ("groups", "head"), "batch"),
        P(("groups", "batch", "head"), None, None),
    )
    return jax.shard_map(
        per_device, mesh=mesh, in_specs=in_specs, out_specs=out_specs, check_vma=False
    )
```

```python
import functools

import jax
import jax.numpy as jnp
from jax import lax
from jax.experimental import pallas as pl
from jax.experimental.pallas import tpu as pltpu
from jax.sharding import PartitionSpec as P

SUBSPACE_EXTENT = 64
STEPS_A = 2
MIX_MAPS = 5
NORMALIZER_GUARD = 0.00064


def route_to_slots(value, position_mapping_target, batch_index, head_index):
    batch_count = lax.axis_size("batch")
    head_count = lax.axis_size("head")
    local_rows, heads_here, width = value.shape
    cluster_number = head_count // 4
    slots_dev = local_rows // cluster_number
    per_pair = slots_dev // batch_count
    quarter = heads_here // 4
    own_map = lax.dynamic_slice_in_dim(
        position_mapping_target, batch_index * local_rows, local_rows
    )
    send_order = jnp.argsort(own_map // slots_dev, stable=True)
    dest = jnp.arange(batch_count * head_count, dtype=jnp.int32)
    dest_block = (dest // head_count) * cluster_number + dest % cluster_number
    quad = (dest % head_count) // cluster_number
    pair = jnp.arange(per_pair, dtype=jnp.int32)
    within = jnp.arange(quarter, dtype=jnp.int32)
    sent_sessions = jnp.take(
        send_order, dest_block[:, None] * per_pair + pair[None, :], mode="clip"
    )
    sent_rows = (
        sent_sessions[:, :, None] * heads_here
        + (quad * quarter)[:, None, None]
        + within[None, None, :]
    )
    packed = jnp.take(
        value.reshape(local_rows * heads_here, width), sent_rows.reshape(-1), axis=0, mode="clip"
    ).reshape(batch_count * head_count, per_pair * quarter, width)
    arrived = lax.all_to_all(packed, ("batch", "head"), split_axis=0, concat_axis=0, tiled=True)
    target = batch_index * cluster_number + head_index % cluster_number
    arrivals = lax.dynamic_slice_in_dim(
        jnp.argsort(position_mapping_target // slots_dev, stable=True),
        target * slots_dev,
        slots_dev,
    )
    placing = jnp.argsort(jnp.take(position_mapping_target, arrivals, mode="clip") % slots_dev)
    source_head = jnp.arange(head_count, dtype=jnp.int32)
    kept_rows = (
        (
            (placing[:, None, None] // per_pair) * head_count + source_head[None, :, None]
        )
        * per_pair
        + placing[:, None, None] % per_pair
    ) * quarter + within[None, None, :]
    return jnp.take(
        arrived.reshape(-1, width), kept_rows.reshape(-1), axis=0, mode="clip"
    ).reshape(slots_dev, head_count * quarter, width)

def exchange_sum(pieces, axis_name):
    count = lax.axis_size(axis_name)
    index = lax.axis_index(axis_name)
    total = lax.dynamic_index_in_dim(pieces, index, keepdims=False).astype(jnp.float32)
    for shift in range(1, count):
        sent = lax.dynamic_index_in_dim(pieces, (index + shift) % count, keepdims=False)
        total = total + lax.ppermute(
            sent, axis_name, [(i, (i + shift) % count) for i in range(count)]
        ).astype(jnp.float32)
    return total


def exchange_copies(value, axis_name):
    count = lax.axis_size(axis_name)
    index = lax.axis_index(axis_name)
    received = [value]
    for shift in range(1, count):
        received.append(
            lax.ppermute(value, axis_name, [(i, (i + shift) % count) for i in range(count)])
        )
    shifts = (index - jnp.arange(count, dtype=jnp.int32)) % count
    return jnp.take(jnp.stack(received), shifts, axis=0, mode="clip")

def widen(value):
    return value.astype(jnp.bfloat16).astype(jnp.float32)


def fill_tables(spread_ref, tile_ref=None):
    extent = SUBSPACE_EXTENT

    @pl.when(pl.program_id(0) == 0)
    def _():
        lane = lax.broadcasted_iota(jnp.int32, spread_ref.shape, 1)
        row = lax.broadcasted_iota(jnp.int32, spread_ref.shape, 0)
        spread_ref[...] = (lane // extent == row).astype(spread_ref.dtype)
        if tile_ref is not None:
            tile_ref[...] = (lane % extent == row).astype(tile_ref.dtype)


def recurrence_kernel(
    steps,
    recept_ref,
    key_ref,
    value_ref,
    decay_ref,
    gate_ref,
    params_ref,
    state_ref,
    mixed_ref,
    payload_ref,
    spread_ref,
):
    extent = SUBSPACE_EXTENT
    fill_tables(spread_ref)
    spread = spread_ref[...]
    state = state_ref[...]
    premium = params_ref[0]
    gain = params_ref[1]
    bias = params_ref[2]
    recept = [recept_ref[t] for t in range(steps)]
    key_vec = [key_ref[t] for t in range(steps)]
    valued = [value_ref[t] for t in range(steps)]
    decay_rate = [decay_ref[t] for t in range(steps)]
    flat = state.shape[-1]
    prefix = jnp.ones_like(recept[0])
    for t in range(steps):
        query = recept[t] * prefix
        high = query.astype(jnp.bfloat16)
        rest = query - high.astype(jnp.float32)
        middle = rest.astype(jnp.bfloat16)
        low = (rest - middle.astype(jnp.float32)).astype(jnp.bfloat16)
        spread_query = (
            jnp.dot(high, spread, preferred_element_type=jnp.float32)
            + jnp.dot(middle, spread, preferred_element_type=jnp.float32)
            + jnp.dot(low, spread, preferred_element_type=jnp.float32)
        )
        weighted = spread_query * state
        folded = weighted[:, 0:128]
        for c in range(1, flat // 128):
            folded = folded + weighted[:, 128 * c : 128 * (c + 1)]
        from_state = folded[:, :extent] + folded[:, extent:]
        bonus_term = jnp.sum(recept[t] * premium * key_vec[t], axis=-1, keepdims=True)
        total = bonus_term * valued[t] + from_state
        for s in range(t):
            factor = key_vec[s]
            for u in range(s + 1, t):
                factor = factor * decay_rate[u]
            total = total + jnp.sum(recept[t] * factor, axis=-1, keepdims=True) * valued[s]
        average = jnp.mean(total, axis=-1, keepdims=True)
        demeaned = total - average
        spread_squared = jnp.mean(demeaned * demeaned, axis=-1, keepdims=True)
        standardized = demeaned * lax.rsqrt(spread_squared + NORMALIZER_GUARD) * gain + bias
        mixed_ref[t] = (standardized * gate_ref[t]).astype(mixed_ref.dtype)
        prefix = prefix * decay_rate[t]
    payload_ref[0] = prefix.astype(payload_ref.dtype)
    for s in range(steps):
        factor = key_vec[s]
        for u in range(s + 1, steps):
            factor = factor * decay_rate[u]
        payload_ref[1 + s] = factor.astype(payload_ref.dtype)
        payload_ref[1 + steps + s] = valued[s].astype(payload_ref.dtype)


def row_block(rows):
    return 64 if rows % 64 == 0 else rows


def run_recurrence(projected, params, state):
    pieces = len(projected)
    steps, rows, extent = projected[0].shape
    flat = state.shape[-1]
    block = row_block(rows)
    return pl.pallas_call(
        functools.partial(recurrence_kernel, steps),
        grid=(rows // block,),
        in_specs=[
            *[pl.BlockSpec((steps, block, extent), lambda n: (0, n, 0))] * pieces,
            pl.BlockSpec((3, block, extent), lambda n: (0, n, 0)),
            pl.BlockSpec((block, flat), lambda n: (n, 0)),
        ],
        out_specs=[
            pl.BlockSpec((steps, block, extent), lambda n: (0, n, 0)),
            pl.BlockSpec((1 + 2 * steps, block, extent), lambda n: (0, n, 0)),
        ],
        out_shape=[
            jax.ShapeDtypeStruct((steps, rows, extent), jnp.bfloat16),
            jax.ShapeDtypeStruct((1 + 2 * steps, rows, extent), jnp.bfloat16),
        ],
        scratch_shapes=[pltpu.VMEM((extent, flat), jnp.bfloat16)],
        cost_estimate=pl.CostEstimate(
            flops=2 * rows * extent * flat * 3 * steps,
            transcendentals=steps * rows,
            bytes_accessed=rows * (flat * 4 + extent * (pieces * steps * 4 + 3 * 4 + steps * 2 + (1 + 2 * steps) * 2)),
        ),
    )(*projected, params, state)


def rebuild_kernel(steps, state_ref, terms_ref, out_ref, spread_ref, tile_ref):
    fill_tables(spread_ref, tile_ref)
    spread = spread_ref[...]
    tile = tile_ref[...]
    total = jnp.dot(terms_ref[0], spread, preferred_element_type=jnp.float32) * state_ref[...].astype(
        jnp.float32
    )
    for s in range(steps):
        total = total + jnp.dot(
            terms_ref[1 + s], spread, preferred_element_type=jnp.float32
        ) * jnp.dot(terms_ref[1 + steps + s], tile, preferred_element_type=jnp.float32)
    out_ref[...] = total


def rebuild_state(moved_state, moved_terms, steps):
    rows, flat = moved_state.shape
    pieces = moved_terms.shape[0]
    extent = SUBSPACE_EXTENT
    block = row_block(rows)
    return pl.pallas_call(
        functools.partial(rebuild_kernel, steps),
        grid=(rows // block,),
        in_specs=[
            pl.BlockSpec((block, flat), lambda n: (n, 0)),
            pl.BlockSpec((pieces, block, extent), lambda n: (0, n, 0)),
        ],
        out_specs=pl.BlockSpec((block, flat), lambda n: (n, 0)),
        out_shape=jax.ShapeDtypeStruct((rows, flat), jnp.float32),
        scratch_shapes=[
            pltpu.VMEM((extent, flat), jnp.bfloat16),
            pltpu.VMEM((extent, flat), jnp.bfloat16),
        ],
        cost_estimate=pl.CostEstimate(
            flops=2 * rows * extent * flat * (1 + 2 * steps),
            transcendentals=0,
            bytes_accessed=rows * (flat * 6 + pieces * extent * 2),
        ),
    )(moved_state, moved_terms)


def per_device(
    tier_feed_tensor,
    preceding_feed_each_stream,
    stream_kept_tableaux,
    position_mapping_target,
    lagging_mixture_weights,
    lagging_narrow_lowering,
    lagging_narrow_raising,
    fourfold_linear_maps,
    attenuation_narrow_lowering,
    attenuation_narrow_raising,
    attenuation_doublelog_anchor,
    instant_premium,
    norming_multiplier,
    norming_intercept,
    outgoing_linear_map,
):
    batch_count = lax.axis_size("batch")
    batch_index = lax.axis_index("batch")
    head_index = lax.axis_index("head")
    steps, sessions, feats = tier_feed_tensor.shape
    local_rows = sessions // batch_count
    heads_here = stream_kept_tableaux.shape[1]
    width = heads_here * SUBSPACE_EXTENT
    f32 = jnp.float32
    bf16 = jnp.bfloat16

    moved_state = route_to_slots(
        stream_kept_tableaux.astype(bf16), position_mapping_target, batch_index, head_index
    )

    previous = jnp.concatenate([preceding_feed_each_stream[None], tier_feed_tensor[:-1]], axis=0)

    def by_block(value):
        return value.reshape(steps, batch_count, local_rows, feats).transpose(1, 0, 2, 3).reshape(
            batch_count * steps * local_rows, feats
        )

    x_float = by_block(tier_feed_tensor).astype(f32)
    shifted = by_block(previous).astype(f32) - x_float
    rows = x_float.shape[0]
    base_mix = (x_float + shifted * lagging_mixture_weights[0]).astype(bf16)
    partial_value = jnp.dot(base_mix, lagging_narrow_lowering, preferred_element_type=f32)
    hidden = jnp.tanh(
        jnp.sum(exchange_copies(partial_value.astype(bf16), "batch").astype(f32), axis=0)
    ).astype(bf16)
    hidden = hidden.reshape(rows, MIX_MAPS, lagging_narrow_raising.shape[1])
    offsets = jnp.einsum(
        "nim,imd->ind", hidden, lagging_narrow_raising, preferred_element_type=f32
    )
    mixed = (
        x_float[None] + shifted[None] * (lagging_mixture_weights[1:, None, :] + offsets)
    ).astype(bf16)
    moved_state, mixed = lax.optimization_barrier((moved_state, mixed))
    main_part = jnp.einsum(
        "inf,ifc->nic", mixed[:4], fourfold_linear_maps, preferred_element_type=f32
    )
    decay_part = jnp.dot(mixed[4], attenuation_narrow_lowering, preferred_element_type=f32)
    aggregated = exchange_sum(
        jnp.concatenate([main_part.reshape(rows, -1), decay_part], axis=1)
        .astype(bf16)
        .reshape(batch_count, steps, local_rows, -1),
        "batch",
    )

    def heads_of(value):
        return value.reshape(steps, local_rows, heads_here, SUBSPACE_EXTENT)

    recept = heads_of(widen(aggregated[..., :width]))
    key_vec = heads_of(widen(aggregated[..., width : 2 * width]))
    valued = heads_of(widen(aggregated[..., 2 * width : 3 * width]))
    gate_act = jax.nn.silu(aggregated[..., 3 * width : 4 * width])
    low_rank = jnp.tanh(aggregated[..., 4 * width :]).astype(bf16)
    decay_rate = heads_of(
        jnp.exp(
            -jnp.exp(
                attenuation_doublelog_anchor
                + jnp.dot(low_rank, attenuation_narrow_raising, preferred_element_type=f32)
            )
        )
    )
    rows_here = local_rows * heads_here

    def by_row(value):
        return value.reshape(steps, rows_here, SUBSPACE_EXTENT)

    projected = tuple(by_row(value) for value in (recept, key_vec, valued, decay_rate, gate_act))
    params = jnp.broadcast_to(
        jnp.stack([instant_premium, norming_multiplier, norming_intercept]).reshape(
            3, 1, heads_here, SUBSPACE_EXTENT
        ),
        (3, local_rows, heads_here, SUBSPACE_EXTENT),
    ).reshape(3, rows_here, SUBSPACE_EXTENT)
    mixed_rows, payload = run_recurrence(
        projected, params, stream_kept_tableaux.reshape(rows_here, -1)
    )
    combined_response = mixed_rows.reshape(steps, local_rows, width)
    pieces = payload.shape[0]
    moved_terms = route_to_slots(
        payload.reshape(pieces, local_rows, heads_here, SUBSPACE_EXTENT)
        .transpose(1, 2, 0, 3)
        .reshape(local_rows, heads_here, pieces * SUBSPACE_EXTENT),
        position_mapping_target,
        batch_index,
        head_index,
    )
    slots_dev, columns, _ = moved_terms.shape
    moved_terms = (
        moved_terms.reshape(slots_dev, columns, pieces, SUBSPACE_EXTENT)
        .transpose(2, 0, 1, 3)
        .reshape(pieces, slots_dev * columns, SUBSPACE_EXTENT)
    )
    final_state = rebuild_state(
        moved_state.reshape(slots_dev * columns, -1), moved_terms, steps
    ).reshape(slots_dev, columns, -1)

    gathered = exchange_copies(combined_response, "batch").transpose(1, 0, 2, 3)
    gathered = gathered.reshape(steps, sessions, width)
    inverse = jnp.argsort(position_mapping_target)
    arranged = jnp.concatenate(
        [gathered[:STEPS_A], jnp.take(gathered[STEPS_A:], inverse, axis=1, mode="clip")], axis=0
    )
    partial_y = jnp.einsum(
        "tnf,fo->tno", arranged, outgoing_linear_map, preferred_element_type=f32
    ).astype(bf16)
    head_count = lax.axis_size("head")
    produced = exchange_sum(
        partial_y.reshape(steps, head_count, sessions // head_count, -1).transpose(1, 0, 2, 3),
        "head",
    ).astype(bf16)
    return (produced[:STEPS_A], produced[STEPS_A:], final_state)


def solution(mesh):
    in_specs = (
        P(None, "groups", "batch"),
        P("groups", "batch"),
        P(("groups", "batch"), "head", None),
        P("groups"),
        P(None, "batch"),
        P("batch", None),
        P(None, None, "batch"),
        P(None, "batch", "head"),
        P("batch", None),
        P(None, "head"),
        P("head"),
        P("head"),
        P("head"),
        P("head"),
        P("head", "batch"),
    )
    out_specs = (
        P(None, ("groups", "head"), "batch"),
        P(None, ("groups", "head"), "batch"),
        P(("groups", "batch", "head"), None, None),
    )
    return jax.shard_map(
        per_device, mesh=mesh, in_specs=in_specs, out_specs=out_specs, check_vma=False
    )
```

```python
import functools

import jax
import jax.numpy as jnp
from jax import lax
from jax.experimental import pallas as pl
from jax.experimental.pallas import tpu as pltpu
from jax.sharding import PartitionSpec as P

SUBSPACE_EXTENT = 64
STEPS_A = 2
MIX_MAPS = 5
NORMALIZER_GUARD = 0.00064


def route_to_slots(value, position_mapping_target, batch_index, head_index):
    batch_count = lax.axis_size("batch")
    head_count = lax.axis_size("head")
    local_rows, heads_here, width = value.shape
    cluster_number = head_count // 4
    slots_dev = local_rows // cluster_number
    per_pair = slots_dev // batch_count
    quarter = heads_here // 4
    own_map = lax.dynamic_slice_in_dim(
        position_mapping_target, batch_index * local_rows, local_rows
    )
    send_order = jnp.argsort(own_map // slots_dev, stable=True)
    dest = jnp.arange(batch_count * head_count, dtype=jnp.int32)
    dest_block = (dest // head_count) * cluster_number + dest % cluster_number
    quad = (dest % head_count) // cluster_number
    pair = jnp.arange(per_pair, dtype=jnp.int32)
    within = jnp.arange(quarter, dtype=jnp.int32)
    sent_sessions = jnp.take(
        send_order, dest_block[:, None] * per_pair + pair[None, :], mode="clip"
    )
    sent_rows = (
        sent_sessions[:, :, None] * heads_here
        + (quad * quarter)[:, None, None]
        + within[None, None, :]
    )
    packed = jnp.take(
        value.reshape(local_rows * heads_here, width), sent_rows.reshape(-1), axis=0, mode="clip"
    ).reshape(batch_count * head_count, per_pair * quarter, width)
    arrived = lax.all_to_all(packed, ("batch", "head"), split_axis=0, concat_axis=0, tiled=True)
    target = batch_index * cluster_number + head_index % cluster_number
    arrivals = lax.dynamic_slice_in_dim(
        jnp.argsort(position_mapping_target // slots_dev, stable=True),
        target * slots_dev,
        slots_dev,
    )
    placing = jnp.argsort(jnp.take(position_mapping_target, arrivals, mode="clip") % slots_dev)
    source_head = jnp.arange(head_count, dtype=jnp.int32)
    kept_rows = (
        (
            (placing[:, None, None] // per_pair) * head_count + source_head[None, :, None]
        )
        * per_pair
        + placing[:, None, None] % per_pair
    ) * quarter + within[None, None, :]
    return jnp.take(
        arrived.reshape(-1, width), kept_rows.reshape(-1), axis=0, mode="clip"
    ).reshape(slots_dev, head_count * quarter, width)

def exchange_sum(pieces, axis_name):
    count = lax.axis_size(axis_name)
    index = lax.axis_index(axis_name)
    total = lax.dynamic_index_in_dim(pieces, index, keepdims=False).astype(jnp.float32)
    for shift in range(1, count):
        sent = lax.dynamic_index_in_dim(pieces, (index + shift) % count, keepdims=False)
        total = total + lax.ppermute(
            sent, axis_name, [(i, (i + shift) % count) for i in range(count)]
        ).astype(jnp.float32)
    return total


def exchange_copies(value, axis_name):
    count = lax.axis_size(axis_name)
    index = lax.axis_index(axis_name)
    received = [value]
    for shift in range(1, count):
        received.append(
            lax.ppermute(value, axis_name, [(i, (i + shift) % count) for i in range(count)])
        )
    shifts = (index - jnp.arange(count, dtype=jnp.int32)) % count
    return jnp.take(jnp.stack(received), shifts, axis=0, mode="clip")

def widen(value):
    return value.astype(jnp.bfloat16).astype(jnp.float32)


def fill_tables(spread_ref, tile_ref=None):
    extent = SUBSPACE_EXTENT

    @pl.when(pl.program_id(0) == 0)
    def _():
        lane = lax.broadcasted_iota(jnp.int32, spread_ref.shape, 1)
        row = lax.broadcasted_iota(jnp.int32, spread_ref.shape, 0)
        spread_ref[...] = (lane // extent == row).astype(spread_ref.dtype)
        if tile_ref is not None:
            tile_ref[...] = (lane % extent == row).astype(tile_ref.dtype)


def recurrence_kernel(
    steps,
    recept_ref,
    key_ref,
    value_ref,
    decay_ref,
    gate_ref,
    params_ref,
    state_ref,
    mixed_ref,
    payload_ref,
    spread_ref,
):
    extent = SUBSPACE_EXTENT
    fill_tables(spread_ref)
    spread = spread_ref[...]
    state = state_ref[...]
    premium = params_ref[0]
    gain = params_ref[1]
    bias = params_ref[2]
    recept = [recept_ref[t] for t in range(steps)]
    key_vec = [key_ref[t] for t in range(steps)]
    valued = [value_ref[t] for t in range(steps)]
    decay_rate = [decay_ref[t] for t in range(steps)]
    flat = state.shape[-1]
    prefix = jnp.ones_like(recept[0])
    for t in range(steps):
        query = recept[t] * prefix
        high = query.astype(jnp.bfloat16)
        rest = query - high.astype(jnp.float32)
        middle = rest.astype(jnp.bfloat16)
        low = (rest - middle.astype(jnp.float32)).astype(jnp.bfloat16)
        spread_query = (
            jnp.dot(high, spread, preferred_element_type=jnp.float32)
            + jnp.dot(middle, spread, preferred_element_type=jnp.float32)
            + jnp.dot(low, spread, preferred_element_type=jnp.float32)
        )
        weighted = spread_query * state
        folded = weighted[:, 0:128]
        for c in range(1, flat // 128):
            folded = folded + weighted[:, 128 * c : 128 * (c + 1)]
        from_state = folded[:, :extent] + folded[:, extent:]
        bonus_term = jnp.sum(recept[t] * premium * key_vec[t], axis=-1, keepdims=True)
        total = bonus_term * valued[t] + from_state
        for s in range(t):
            factor = key_vec[s]
            for u in range(s + 1, t):
                factor = factor * decay_rate[u]
            total = total + jnp.sum(recept[t] * factor, axis=-1, keepdims=True) * valued[s]
        average = jnp.mean(total, axis=-1, keepdims=True)
        demeaned = total - average
        spread_squared = jnp.mean(demeaned * demeaned, axis=-1, keepdims=True)
        standardized = demeaned * lax.rsqrt(spread_squared + NORMALIZER_GUARD) * gain + bias
        mixed_ref[t] = (standardized * gate_ref[t]).astype(mixed_ref.dtype)
        prefix = prefix * decay_rate[t]
    payload_ref[0] = prefix.astype(payload_ref.dtype)
    for s in range(steps):
        factor = key_vec[s]
        for u in range(s + 1, steps):
            factor = factor * decay_rate[u]
        payload_ref[1 + s] = factor.astype(payload_ref.dtype)
        payload_ref[1 + steps + s] = valued[s].astype(payload_ref.dtype)


def row_block(rows):
    return 64 if rows % 64 == 0 else rows


def run_recurrence(projected, params, state):
    pieces = len(projected)
    steps, rows, extent = projected[0].shape
    flat = state.shape[-1]
    block = row_block(rows)
    return pl.pallas_call(
        functools.partial(recurrence_kernel, steps),
        grid=(rows // block,),
        in_specs=[
            *[pl.BlockSpec((steps, block, extent), lambda n: (0, n, 0))] * pieces,
            pl.BlockSpec((3, block, extent), lambda n: (0, n, 0)),
            pl.BlockSpec((block, flat), lambda n: (n, 0)),
        ],
        out_specs=[
            pl.BlockSpec((steps, block, extent), lambda n: (0, n, 0)),
            pl.BlockSpec((1 + 2 * steps, block, extent), lambda n: (0, n, 0)),
        ],
        out_shape=[
            jax.ShapeDtypeStruct((steps, rows, extent), jnp.bfloat16),
            jax.ShapeDtypeStruct((1 + 2 * steps, rows, extent), jnp.bfloat16),
        ],
        scratch_shapes=[pltpu.VMEM((extent, flat), jnp.bfloat16)],
        cost_estimate=pl.CostEstimate(
            flops=2 * rows * extent * flat * 3 * steps,
            transcendentals=steps * rows,
            bytes_accessed=rows * (flat * 4 + extent * (pieces * steps * 4 + 3 * 4 + steps * 2 + (1 + 2 * steps) * 2)),
        ),
    )(*projected, params, state)


def rebuild_kernel(steps, state_ref, terms_ref, out_ref, spread_ref, tile_ref):
    fill_tables(spread_ref, tile_ref)
    spread = spread_ref[...]
    tile = tile_ref[...]
    total = jnp.dot(terms_ref[0], spread, preferred_element_type=jnp.float32) * state_ref[...].astype(
        jnp.float32
    )
    for s in range(steps):
        total = total + jnp.dot(
            terms_ref[1 + s], spread, preferred_element_type=jnp.float32
        ) * jnp.dot(terms_ref[1 + steps + s], tile, preferred_element_type=jnp.float32)
    out_ref[...] = total


def rebuild_state(moved_state, moved_terms, steps):
    rows, flat = moved_state.shape
    pieces = moved_terms.shape[0]
    extent = SUBSPACE_EXTENT
    block = row_block(rows)
    return pl.pallas_call(
        functools.partial(rebuild_kernel, steps),
        grid=(rows // block,),
        in_specs=[
            pl.BlockSpec((block, flat), lambda n: (n, 0)),
            pl.BlockSpec((pieces, block, extent), lambda n: (0, n, 0)),
        ],
        out_specs=pl.BlockSpec((block, flat), lambda n: (n, 0)),
        out_shape=jax.ShapeDtypeStruct((rows, flat), jnp.float32),
        scratch_shapes=[
            pltpu.VMEM((extent, flat), jnp.bfloat16),
            pltpu.VMEM((extent, flat), jnp.bfloat16),
        ],
        cost_estimate=pl.CostEstimate(
            flops=2 * rows * extent * flat * (1 + 2 * steps),
            transcendentals=0,
            bytes_accessed=rows * (flat * 6 + pieces * extent * 2),
        ),
    )(moved_state, moved_terms)


def per_device(
    tier_feed_tensor,
    preceding_feed_each_stream,
    stream_kept_tableaux,
    position_mapping_target,
    lagging_mixture_weights,
    lagging_narrow_lowering,
    lagging_narrow_raising,
    fourfold_linear_maps,
    attenuation_narrow_lowering,
    attenuation_narrow_raising,
    attenuation_doublelog_anchor,
    instant_premium,
    norming_multiplier,
    norming_intercept,
    outgoing_linear_map,
):
    batch_count = lax.axis_size("batch")
    batch_index = lax.axis_index("batch")
    head_index = lax.axis_index("head")
    steps, sessions, feats = tier_feed_tensor.shape
    local_rows = sessions // batch_count
    heads_here = stream_kept_tableaux.shape[1]
    width = heads_here * SUBSPACE_EXTENT
    f32 = jnp.float32
    bf16 = jnp.bfloat16


    previous = jnp.concatenate([preceding_feed_each_stream[None], tier_feed_tensor[:-1]], axis=0)

    def by_block(value):
        return value.reshape(steps, batch_count, local_rows, feats).transpose(1, 0, 2, 3).reshape(
            batch_count * steps * local_rows, feats
        )

    x_float = by_block(tier_feed_tensor).astype(f32)
    shifted = by_block(previous).astype(f32) - x_float
    rows = x_float.shape[0]
    base_mix = (x_float + shifted * lagging_mixture_weights[0]).astype(bf16)
    partial_value = jnp.dot(base_mix, lagging_narrow_lowering, preferred_element_type=f32)
    hidden = jnp.tanh(
        jnp.sum(exchange_copies(partial_value.astype(bf16), "batch").astype(f32), axis=0)
    ).astype(bf16)
    hidden = hidden.reshape(rows, MIX_MAPS, lagging_narrow_raising.shape[1])
    offsets = jnp.einsum(
        "nim,imd->ind", hidden, lagging_narrow_raising, preferred_element_type=f32
    )
    mixed = (
        x_float[None] + shifted[None] * (lagging_mixture_weights[1:, None, :] + offsets)
    ).astype(bf16)
    main_part = jnp.einsum(
        "inf,ifc->nic", mixed[:4], fourfold_linear_maps, preferred_element_type=f32
    )
    decay_part = jnp.dot(mixed[4], attenuation_narrow_lowering, preferred_element_type=f32)
    aggregated = exchange_sum(
        jnp.concatenate([main_part.reshape(rows, -1), decay_part], axis=1)
        .astype(bf16)
        .reshape(batch_count, steps, local_rows, -1),
        "batch",
    )

    kept_for_move, aggregated = lax.optimization_barrier((stream_kept_tableaux, aggregated))
    moved_state = route_to_slots(
        kept_for_move.astype(bf16), position_mapping_target, batch_index, head_index
    )

    def heads_of(value):
        return value.reshape(steps, local_rows, heads_here, SUBSPACE_EXTENT)

    recept = heads_of(widen(aggregated[..., :width]))
    key_vec = heads_of(widen(aggregated[..., width : 2 * width]))
    valued = heads_of(widen(aggregated[..., 2 * width : 3 * width]))
    gate_act = jax.nn.silu(aggregated[..., 3 * width : 4 * width])
    low_rank = jnp.tanh(aggregated[..., 4 * width :]).astype(bf16)
    decay_rate = heads_of(
        jnp.exp(
            -jnp.exp(
                attenuation_doublelog_anchor
                + jnp.dot(low_rank, attenuation_narrow_raising, preferred_element_type=f32)
            )
        )
    )
    rows_here = local_rows * heads_here

    def by_row(value):
        return value.reshape(steps, rows_here, SUBSPACE_EXTENT)

    projected = tuple(by_row(value) for value in (recept, key_vec, valued, decay_rate, gate_act))
    params = jnp.broadcast_to(
        jnp.stack([instant_premium, norming_multiplier, norming_intercept]).reshape(
            3, 1, heads_here, SUBSPACE_EXTENT
        ),
        (3, local_rows, heads_here, SUBSPACE_EXTENT),
    ).reshape(3, rows_here, SUBSPACE_EXTENT)
    mixed_rows, payload = run_recurrence(
        projected, params, stream_kept_tableaux.reshape(rows_here, -1)
    )
    moved_state, mixed_rows, payload = lax.optimization_barrier((moved_state, mixed_rows, payload))
    combined_response = mixed_rows.reshape(steps, local_rows, width)
    pieces = payload.shape[0]
    moved_terms = route_to_slots(
        payload.reshape(pieces, local_rows, heads_here, SUBSPACE_EXTENT)
        .transpose(1, 2, 0, 3)
        .reshape(local_rows, heads_here, pieces * SUBSPACE_EXTENT),
        position_mapping_target,
        batch_index,
        head_index,
    )
    slots_dev, columns, _ = moved_terms.shape
    moved_terms = (
        moved_terms.reshape(slots_dev, columns, pieces, SUBSPACE_EXTENT)
        .transpose(2, 0, 1, 3)
        .reshape(pieces, slots_dev * columns, SUBSPACE_EXTENT)
    )
    final_state = rebuild_state(
        moved_state.reshape(slots_dev * columns, -1), moved_terms, steps
    ).reshape(slots_dev, columns, -1)

    gathered = exchange_copies(combined_response, "batch").transpose(1, 0, 2, 3)
    gathered = gathered.reshape(steps, sessions, width)
    inverse = jnp.argsort(position_mapping_target)
    arranged = jnp.concatenate(
        [gathered[:STEPS_A], jnp.take(gathered[STEPS_A:], inverse, axis=1, mode="clip")], axis=0
    )
    partial_y = jnp.einsum(
        "tnf,fo->tno", arranged, outgoing_linear_map, preferred_element_type=f32
    ).astype(bf16)
    head_count = lax.axis_size("head")
    produced = exchange_sum(
        partial_y.reshape(steps, head_count, sessions // head_count, -1).transpose(1, 0, 2, 3),
        "head",
    ).astype(bf16)
    return (produced[:STEPS_A], produced[STEPS_A:], final_state)


def solution(mesh):
    in_specs = (
        P(None, "groups", "batch"),
        P("groups", "batch"),
        P(("groups", "batch"), "head", None),
        P("groups"),
        P(None, "batch"),
        P("batch", None),
        P(None, None, "batch"),
        P(None, "batch", "head"),
        P("batch", None),
        P(None, "head"),
        P("head"),
        P("head"),
        P("head"),
        P("head"),
        P("head", "batch"),
    )
    out_specs = (
        P(None, ("groups", "head"), "batch"),
        P(None, ("groups", "head"), "batch"),
        P(("groups", "batch", "head"), None, None),
    )
    return jax.shard_map(
        per_device, mesh=mesh, in_specs=in_specs, out_specs=out_specs, check_vma=False
    )
```

```python
import functools

import jax
import jax.numpy as jnp
from jax import lax
from jax.experimental import pallas as pl
from jax.experimental.pallas import tpu as pltpu
from jax.sharding import PartitionSpec as P

SUBSPACE_EXTENT = 64
STEPS_A = 2
MIX_MAPS = 5
NORMALIZER_GUARD = 0.00064


def index_of(values, count):
    positions = jnp.arange(values.shape[0], dtype=jnp.int32)
    wanted = jnp.arange(count, dtype=jnp.int32)
    return jnp.sum(jnp.where(values[None, :] == wanted[:, None], positions[None, :], 0), axis=1)


def route_to_slots(value, position_mapping_target, batch_index, head_index):
    batch_count = lax.axis_size("batch")
    head_count = lax.axis_size("head")
    local_rows, heads_here, width = value.shape
    cluster_number = head_count // 4
    slots_dev = local_rows // cluster_number
    per_pair = slots_dev // batch_count
    quarter = heads_here // 4
    own_map = lax.dynamic_slice_in_dim(
        position_mapping_target, batch_index * local_rows, local_rows
    )
    dest_key = own_map // slots_dev
    positions = jnp.arange(local_rows, dtype=jnp.int32)
    ahead = (dest_key[None, :] < dest_key[:, None]) | (
        (dest_key[None, :] == dest_key[:, None]) & (positions[None, :] < positions[:, None])
    )
    send_order = index_of(jnp.sum(ahead.astype(jnp.int32), axis=1), local_rows)
    dest = jnp.arange(batch_count * head_count, dtype=jnp.int32)
    dest_block = (dest // head_count) * cluster_number + dest % cluster_number
    quad = (dest % head_count) // cluster_number
    pair = jnp.arange(per_pair, dtype=jnp.int32)
    within = jnp.arange(quarter, dtype=jnp.int32)
    sent_sessions = jnp.take(
        send_order, dest_block[:, None] * per_pair + pair[None, :], mode="clip"
    )
    sent_rows = (
        sent_sessions[:, :, None] * heads_here
        + (quad * quarter)[:, None, None]
        + within[None, None, :]
    )
    packed = jnp.take(
        value.reshape(local_rows * heads_here, width), sent_rows.reshape(-1), axis=0, mode="clip"
    ).reshape(batch_count * head_count, per_pair * quarter, width)
    arrived = lax.all_to_all(packed, ("batch", "head"), split_axis=0, concat_axis=0, tiled=True)
    target = batch_index * cluster_number + head_index % cluster_number
    sessions = position_mapping_target.shape[0]
    chosen = lax.dynamic_slice_in_dim(
        index_of(position_mapping_target, sessions), target * slots_dev, slots_dev
    )
    every = jnp.arange(sessions, dtype=jnp.int32)
    coming = (position_mapping_target // slots_dev) == target
    placing = jnp.sum(
        ((every[None, :] < chosen[:, None]) & coming[None, :]).astype(jnp.int32), axis=1
    )
    source_head = jnp.arange(head_count, dtype=jnp.int32)
    kept_rows = (
        (
            (placing[:, None, None] // per_pair) * head_count + source_head[None, :, None]
        )
        * per_pair
        + placing[:, None, None] % per_pair
    ) * quarter + within[None, None, :]
    return jnp.take(
        arrived.reshape(-1, width), kept_rows.reshape(-1), axis=0, mode="clip"
    ).reshape(slots_dev, head_count * quarter, width)

def exchange_sum(pieces, axis_name):
    count = lax.axis_size(axis_name)
    index = lax.axis_index(axis_name)

    def own(shift):
        return jax.tree.map(
            lambda value: lax.dynamic_index_in_dim(value, (index + shift) % count, keepdims=False),
            pieces,
        )

    total = jax.tree.map(lambda value: value.astype(jnp.float32), own(0))
    for shift in range(1, count):
        arrived = lax.ppermute(
            own(shift), axis_name, [(i, (i + shift) % count) for i in range(count)]
        )
        total = jax.tree.map(lambda acc, value: acc + value.astype(jnp.float32), total, arrived)
    return total

def exchange_copies(value, axis_name):
    count = lax.axis_size(axis_name)
    index = lax.axis_index(axis_name)
    received = [value]
    for shift in range(1, count):
        received.append(
            lax.ppermute(value, axis_name, [(i, (i + shift) % count) for i in range(count)])
        )
    shifts = (index - jnp.arange(count, dtype=jnp.int32)) % count
    return jnp.take(jnp.stack(received), shifts, axis=0, mode="clip")

def widen(value):
    return value.astype(jnp.bfloat16).astype(jnp.float32)


def fill_tables(spread_ref, tile_ref=None):
    extent = SUBSPACE_EXTENT

    @pl.when(pl.program_id(0) == 0)
    def _():
        lane = lax.broadcasted_iota(jnp.int32, spread_ref.shape, 1)
        row = lax.broadcasted_iota(jnp.int32, spread_ref.shape, 0)
        spread_ref[...] = (lane // extent == row).astype(spread_ref.dtype)
        if tile_ref is not None:
            tile_ref[...] = (lane % extent == row).astype(tile_ref.dtype)


def recurrence_kernel(
    steps,
    recept_ref,
    key_ref,
    value_ref,
    decay_ref,
    gate_ref,
    params_ref,
    state_ref,
    mixed_ref,
    payload_ref,
    spread_ref,
):
    extent = SUBSPACE_EXTENT
    fill_tables(spread_ref)
    spread = spread_ref[...]
    state = state_ref[...]
    premium = params_ref[0]
    gain = params_ref[1]
    bias = params_ref[2]
    recept = [recept_ref[t] for t in range(steps)]
    key_vec = [key_ref[t] for t in range(steps)]
    valued = [value_ref[t] for t in range(steps)]
    decay_rate = [decay_ref[t] for t in range(steps)]
    flat = state.shape[-1]
    prefix = jnp.ones_like(recept[0])
    for t in range(steps):
        query = recept[t] * prefix
        high = query.astype(jnp.bfloat16)
        rest = query - high.astype(jnp.float32)
        middle = rest.astype(jnp.bfloat16)
        low = (rest - middle.astype(jnp.float32)).astype(jnp.bfloat16)
        spread_query = (
            jnp.dot(high, spread, preferred_element_type=jnp.float32)
            + jnp.dot(middle, spread, preferred_element_type=jnp.float32)
            + jnp.dot(low, spread, preferred_element_type=jnp.float32)
        )
        weighted = spread_query * state
        folded = weighted[:, 0:128]
        for c in range(1, flat // 128):
            folded = folded + weighted[:, 128 * c : 128 * (c + 1)]
        from_state = folded[:, :extent] + folded[:, extent:]
        bonus_term = jnp.sum(recept[t] * premium * key_vec[t], axis=-1, keepdims=True)
        total = bonus_term * valued[t] + from_state
        for s in range(t):
            factor = key_vec[s]
            for u in range(s + 1, t):
                factor = factor * decay_rate[u]
            total = total + jnp.sum(recept[t] * factor, axis=-1, keepdims=True) * valued[s]
        average = jnp.mean(total, axis=-1, keepdims=True)
        demeaned = total - average
        spread_squared = jnp.mean(demeaned * demeaned, axis=-1, keepdims=True)
        standardized = demeaned * lax.rsqrt(spread_squared + NORMALIZER_GUARD) * gain + bias
        mixed_ref[t] = (standardized * gate_ref[t]).astype(mixed_ref.dtype)
        prefix = prefix * decay_rate[t]
    payload_ref[0] = prefix.astype(payload_ref.dtype)
    for s in range(steps):
        factor = key_vec[s]
        for u in range(s + 1, steps):
            factor = factor * decay_rate[u]
        payload_ref[1 + s] = factor.astype(payload_ref.dtype)
        payload_ref[1 + steps + s] = valued[s].astype(payload_ref.dtype)


def row_block(rows):
    return 64 if rows % 64 == 0 else rows


def run_recurrence(projected, params, state):
    pieces = len(projected)
    steps, rows, extent = projected[0].shape
    flat = state.shape[-1]
    block = row_block(rows)
    return pl.pallas_call(
        functools.partial(recurrence_kernel, steps),
        grid=(rows // block,),
        in_specs=[
            *[pl.BlockSpec((steps, block, extent), lambda n: (0, n, 0))] * pieces,
            pl.BlockSpec((3, block, extent), lambda n: (0, n, 0)),
            pl.BlockSpec((block, flat), lambda n: (n, 0)),
        ],
        out_specs=[
            pl.BlockSpec((steps, block, extent), lambda n: (0, n, 0)),
            pl.BlockSpec((1 + 2 * steps, block, extent), lambda n: (0, n, 0)),
        ],
        out_shape=[
            jax.ShapeDtypeStruct((steps, rows, extent), jnp.bfloat16),
            jax.ShapeDtypeStruct((1 + 2 * steps, rows, extent), jnp.bfloat16),
        ],
        scratch_shapes=[pltpu.VMEM((extent, flat), jnp.bfloat16)],
        cost_estimate=pl.CostEstimate(
            flops=2 * rows * extent * flat * 3 * steps,
            transcendentals=steps * rows,
            bytes_accessed=rows * (flat * 4 + extent * (pieces * steps * 4 + 3 * 4 + steps * 2 + (1 + 2 * steps) * 2)),
        ),
    )(*projected, params, state)


def rebuild_kernel(steps, state_ref, terms_ref, out_ref, spread_ref, tile_ref):
    fill_tables(spread_ref, tile_ref)
    spread = spread_ref[...]
    tile = tile_ref[...]
    total = jnp.dot(terms_ref[0], spread, preferred_element_type=jnp.float32) * state_ref[...].astype(
        jnp.float32
    )
    for s in range(steps):
        total = total + jnp.dot(
            terms_ref[1 + s], spread, preferred_element_type=jnp.float32
        ) * jnp.dot(terms_ref[1 + steps + s], tile, preferred_element_type=jnp.float32)
    out_ref[...] = total


def rebuild_state(moved_state, moved_terms, steps):
    rows, flat = moved_state.shape
    pieces = moved_terms.shape[0]
    extent = SUBSPACE_EXTENT
    block = row_block(rows)
    return pl.pallas_call(
        functools.partial(rebuild_kernel, steps),
        grid=(rows // block,),
        in_specs=[
            pl.BlockSpec((block, flat), lambda n: (n, 0)),
            pl.BlockSpec((pieces, block, extent), lambda n: (0, n, 0)),
        ],
        out_specs=pl.BlockSpec((block, flat), lambda n: (n, 0)),
        out_shape=jax.ShapeDtypeStruct((rows, flat), jnp.float32),
        scratch_shapes=[
            pltpu.VMEM((extent, flat), jnp.bfloat16),
            pltpu.VMEM((extent, flat), jnp.bfloat16),
        ],
        cost_estimate=pl.CostEstimate(
            flops=2 * rows * extent * flat * (1 + 2 * steps),
            transcendentals=0,
            bytes_accessed=rows * (flat * 6 + pieces * extent * 2),
        ),
    )(moved_state, moved_terms)


def per_device(
    tier_feed_tensor,
    preceding_feed_each_stream,
    stream_kept_tableaux,
    position_mapping_target,
    lagging_mixture_weights,
    lagging_narrow_lowering,
    lagging_narrow_raising,
    fourfold_linear_maps,
    attenuation_narrow_lowering,
    attenuation_narrow_raising,
    attenuation_doublelog_anchor,
    instant_premium,
    norming_multiplier,
    norming_intercept,
    outgoing_linear_map,
):
    batch_count = lax.axis_size("batch")
    batch_index = lax.axis_index("batch")
    head_index = lax.axis_index("head")
    steps, sessions, feats = tier_feed_tensor.shape
    local_rows = sessions // batch_count
    heads_here = stream_kept_tableaux.shape[1]
    width = heads_here * SUBSPACE_EXTENT
    f32 = jnp.float32
    bf16 = jnp.bfloat16


    previous = jnp.concatenate([preceding_feed_each_stream[None], tier_feed_tensor[:-1]], axis=0)

    def by_block(value):
        return value.reshape(steps, batch_count, local_rows, feats).transpose(1, 0, 2, 3).reshape(
            batch_count * steps * local_rows, feats
        )

    x_float = by_block(tier_feed_tensor).astype(f32)
    shifted = by_block(previous).astype(f32) - x_float
    rows = x_float.shape[0]
    base_mix = (x_float + shifted * lagging_mixture_weights[0]).astype(bf16)
    partial_value = jnp.dot(base_mix, lagging_narrow_lowering, preferred_element_type=f32)
    hidden = jnp.tanh(
        jnp.sum(exchange_copies(partial_value.astype(bf16), "batch").astype(f32), axis=0)
    ).astype(bf16)
    hidden = hidden.reshape(rows, MIX_MAPS, lagging_narrow_raising.shape[1])
    offsets = jnp.einsum(
        "nim,imd->ind", hidden, lagging_narrow_raising, preferred_element_type=f32
    )
    mixed = (
        x_float[None] + shifted[None] * (lagging_mixture_weights[1:, None, :] + offsets)
    ).astype(bf16)
    main_part = jnp.einsum(
        "inf,ifc->inc", mixed[:4], fourfold_linear_maps, preferred_element_type=f32
    )
    decay_part = jnp.dot(mixed[4], attenuation_narrow_lowering, preferred_element_type=f32)
    main_sum, decay_sum = exchange_sum(
        (
            main_part.astype(bf16)
            .reshape(4, batch_count, steps * local_rows, width)
            .transpose(1, 0, 2, 3),
            decay_part.astype(bf16).reshape(batch_count, steps * local_rows, -1),
        ),
        "batch",
    )

    kept_for_move, main_sum, decay_sum = lax.optimization_barrier(
        (stream_kept_tableaux, main_sum, decay_sum)
    )
    moved_state = route_to_slots(
        kept_for_move.astype(bf16), position_mapping_target, batch_index, head_index
    )

    def heads_of(value):
        return value.reshape(steps, local_rows, heads_here, SUBSPACE_EXTENT)

    main_sum = main_sum.reshape(4, steps, local_rows, width)
    recept = heads_of(widen(main_sum[0]))
    key_vec = heads_of(widen(main_sum[1]))
    valued = heads_of(widen(main_sum[2]))
    gate_act = jax.nn.silu(main_sum[3])
    low_rank = jnp.tanh(decay_sum.reshape(steps, local_rows, -1)).astype(bf16)
    decay_rate = heads_of(
        jnp.exp(
            -jnp.exp(
                attenuation_doublelog_anchor
                + jnp.dot(low_rank, attenuation_narrow_raising, preferred_element_type=f32)
            )
        )
    )
    rows_here = local_rows * heads_here

    def by_row(value):
        return value.reshape(steps, rows_here, SUBSPACE_EXTENT)

    projected = tuple(by_row(value) for value in (recept, key_vec, valued, decay_rate, gate_act))
    params = jnp.broadcast_to(
        jnp.stack([instant_premium, norming_multiplier, norming_intercept]).reshape(
            3, 1, heads_here, SUBSPACE_EXTENT
        ),
        (3, local_rows, heads_here, SUBSPACE_EXTENT),
    ).reshape(3, rows_here, SUBSPACE_EXTENT)
    mixed_rows, payload = run_recurrence(
        projected, params, stream_kept_tableaux.reshape(rows_here, -1)
    )
    moved_state, mixed_rows, payload = lax.optimization_barrier((moved_state, mixed_rows, payload))
    combined_response = mixed_rows.reshape(steps, local_rows, width)
    pieces = payload.shape[0]
    moved_terms = route_to_slots(
        payload.reshape(pieces, local_rows, heads_here, SUBSPACE_EXTENT)
        .transpose(1, 2, 0, 3)
        .reshape(local_rows, heads_here, pieces * SUBSPACE_EXTENT),
        position_mapping_target,
        batch_index,
        head_index,
    )
    slots_dev, columns, _ = moved_terms.shape
    moved_terms = (
        moved_terms.reshape(slots_dev, columns, pieces, SUBSPACE_EXTENT)
        .transpose(2, 0, 1, 3)
        .reshape(pieces, slots_dev * columns, SUBSPACE_EXTENT)
    )
    final_state = rebuild_state(
        moved_state.reshape(slots_dev * columns, -1), moved_terms, steps
    ).reshape(slots_dev, columns, -1)

    gathered = exchange_copies(combined_response, "batch").transpose(1, 0, 2, 3)
    gathered = gathered.reshape(steps, sessions, width)
    inverse = index_of(position_mapping_target, sessions)
    arranged = jnp.concatenate(
        [gathered[:STEPS_A], jnp.take(gathered[STEPS_A:], inverse, axis=1, mode="clip")], axis=0
    )
    partial_y = jnp.einsum(
        "tnf,fo->tno", arranged, outgoing_linear_map, preferred_element_type=f32
    ).astype(bf16)
    head_count = lax.axis_size("head")
    produced = exchange_sum(
        partial_y.reshape(steps, head_count, sessions // head_count, -1).transpose(1, 0, 2, 3),
        "head",
    ).astype(bf16)
    return (produced[:STEPS_A], produced[STEPS_A:], final_state)


def solution(mesh):
    in_specs = (
        P(None, "groups", "batch"),
        P("groups", "batch"),
        P(("groups", "batch"), "head", None),
        P("groups"),
        P(None, "batch"),
        P("batch", None),
        P(None, None, "batch"),
        P(None, "batch", "head"),
        P("batch", None),
        P(None, "head"),
        P("head"),
        P("head"),
        P("head"),
        P("head"),
        P("head", "batch"),
    )
    out_specs = (
        P(None, ("groups", "head"), "batch"),
        P(None, ("groups", "head"), "batch"),
        P(("groups", "batch", "head"), None, None),
    )
    return jax.shard_map(
        per_device, mesh=mesh, in_specs=in_specs, out_specs=out_specs, check_vma=False
    )
```

```python
import functools

import jax
import jax.numpy as jnp
from jax import lax
from jax.experimental import pallas as pl
from jax.experimental.pallas import tpu as pltpu
from jax.sharding import PartitionSpec as P

SUBSPACE_EXTENT = 64
STEPS_A = 2
MIX_MAPS = 5
NORMALIZER_GUARD = 0.00064


def index_of(values, count):
    positions = jnp.arange(values.shape[0], dtype=jnp.int32)
    wanted = jnp.arange(count, dtype=jnp.int32)
    return jnp.sum(jnp.where(values[None, :] == wanted[:, None], positions[None, :], 0), axis=1)


def route_to_slots(value, position_mapping_target, batch_index, head_index):
    batch_count = lax.axis_size("batch")
    head_count = lax.axis_size("head")
    local_rows, heads_here, width = value.shape
    cluster_number = head_count // 4
    slots_dev = local_rows // cluster_number
    per_pair = slots_dev // batch_count
    quarter = heads_here // 4
    own_map = lax.dynamic_slice_in_dim(
        position_mapping_target, batch_index * local_rows, local_rows
    )
    dest_key = own_map // slots_dev
    positions = jnp.arange(local_rows, dtype=jnp.int32)
    ahead = (dest_key[None, :] < dest_key[:, None]) | (
        (dest_key[None, :] == dest_key[:, None]) & (positions[None, :] < positions[:, None])
    )
    send_order = index_of(jnp.sum(ahead.astype(jnp.int32), axis=1), local_rows)
    dest = jnp.arange(batch_count * head_count, dtype=jnp.int32)
    dest_block = (dest // head_count) * cluster_number + dest % cluster_number
    quad = (dest % head_count) // cluster_number
    pair = jnp.arange(per_pair, dtype=jnp.int32)
    within = jnp.arange(quarter, dtype=jnp.int32)
    sent_sessions = jnp.take(
        send_order, dest_block[:, None] * per_pair + pair[None, :], mode="clip"
    )
    sent_rows = (
        sent_sessions[:, :, None] * heads_here
        + (quad * quarter)[:, None, None]
        + within[None, None, :]
    )
    packed = jnp.take(
        value.reshape(local_rows * heads_here, width), sent_rows.reshape(-1), axis=0, mode="clip"
    ).reshape(batch_count * head_count, per_pair * quarter, width)
    arrived = lax.all_to_all(packed, ("batch", "head"), split_axis=0, concat_axis=0, tiled=True)
    target = batch_index * cluster_number + head_index % cluster_number
    sessions = position_mapping_target.shape[0]
    chosen = lax.dynamic_slice_in_dim(
        index_of(position_mapping_target, sessions), target * slots_dev, slots_dev
    )
    every = jnp.arange(sessions, dtype=jnp.int32)
    coming = (position_mapping_target // slots_dev) == target
    placing = jnp.sum(
        ((every[None, :] < chosen[:, None]) & coming[None, :]).astype(jnp.int32), axis=1
    )
    source_head = jnp.arange(head_count, dtype=jnp.int32)
    kept_rows = (
        (
            (placing[:, None, None] // per_pair) * head_count + source_head[None, :, None]
        )
        * per_pair
        + placing[:, None, None] % per_pair
    ) * quarter + within[None, None, :]
    return jnp.take(
        arrived.reshape(-1, width), kept_rows.reshape(-1), axis=0, mode="clip"
    ).reshape(slots_dev, head_count * quarter, width)

def exchange_sum(pieces, axis_name):
    count = lax.axis_size(axis_name)
    index = lax.axis_index(axis_name)

    def own(shift):
        return jax.tree.map(
            lambda value: lax.dynamic_index_in_dim(value, (index + shift) % count, keepdims=False),
            pieces,
        )

    total = jax.tree.map(lambda value: value.astype(jnp.float32), own(0))
    for shift in range(1, count):
        arrived = lax.ppermute(
            own(shift), axis_name, [(i, (i + shift) % count) for i in range(count)]
        )
        total = jax.tree.map(lambda acc, value: acc + value.astype(jnp.float32), total, arrived)
    return total

def exchange_copies(value, axis_name):
    count = lax.axis_size(axis_name)
    index = lax.axis_index(axis_name)
    received = [value]
    for shift in range(1, count):
        received.append(
            lax.ppermute(value, axis_name, [(i, (i + shift) % count) for i in range(count)])
        )
    shifts = (index - jnp.arange(count, dtype=jnp.int32)) % count
    return jnp.take(jnp.stack(received), shifts, axis=0, mode="clip")

def by_source(received, index, count):
    shifts = (index - jnp.arange(count, dtype=jnp.int32)) % count
    return jnp.take(jnp.stack(received), shifts, axis=0, mode="clip")


def gather_with_parts(value, parts, axis_name):
    count = lax.axis_size(axis_name)
    index = lax.axis_index(axis_name)
    copies = [value]
    moved = [lax.dynamic_index_in_dim(parts, index, keepdims=False)]
    for shift in range(1, count):
        sent = lax.dynamic_index_in_dim(parts, (index + shift) % count, keepdims=False)
        copy, part = lax.ppermute(
            (value, sent), axis_name, [(i, (i + shift) % count) for i in range(count)]
        )
        copies.append(copy)
        moved.append(part)
    return by_source(copies, index, count), by_source(moved, index, count)


def sum_with_parts(pieces, parts, axis_name):
    count = lax.axis_size(axis_name)
    index = lax.axis_index(axis_name)
    total = lax.dynamic_index_in_dim(pieces, index, keepdims=False).astype(jnp.float32)
    moved = [lax.dynamic_index_in_dim(parts, index, keepdims=False)]
    for shift in range(1, count):
        target = (index + shift) % count
        piece, part = lax.ppermute(
            (
                lax.dynamic_index_in_dim(pieces, target, keepdims=False),
                lax.dynamic_index_in_dim(parts, target, keepdims=False),
            ),
            axis_name,
            [(i, (i + shift) % count) for i in range(count)],
        )
        total = total + piece.astype(jnp.float32)
        moved.append(part)
    return total, by_source(moved, index, count)


def widen(value):
    return value.astype(jnp.bfloat16).astype(jnp.float32)


def fill_tables(spread_ref, tile_ref=None):
    extent = SUBSPACE_EXTENT

    @pl.when(pl.program_id(0) == 0)
    def _():
        lane = lax.broadcasted_iota(jnp.int32, spread_ref.shape, 1)
        row = lax.broadcasted_iota(jnp.int32, spread_ref.shape, 0)
        spread_ref[...] = (lane // extent == row).astype(spread_ref.dtype)
        if tile_ref is not None:
            tile_ref[...] = (lane % extent == row).astype(tile_ref.dtype)


def recurrence_kernel(
    steps,
    recept_ref,
    key_ref,
    value_ref,
    decay_ref,
    gate_ref,
    params_ref,
    state_ref,
    mixed_ref,
    payload_ref,
    spread_ref,
):
    extent = SUBSPACE_EXTENT
    fill_tables(spread_ref)
    spread = spread_ref[...]
    state = state_ref[...]
    premium = params_ref[0]
    gain = params_ref[1]
    bias = params_ref[2]
    recept = [recept_ref[t] for t in range(steps)]
    key_vec = [key_ref[t] for t in range(steps)]
    valued = [value_ref[t] for t in range(steps)]
    decay_rate = [decay_ref[t] for t in range(steps)]
    flat = state.shape[-1]
    prefix = jnp.ones_like(recept[0])
    for t in range(steps):
        query = recept[t] * prefix
        high = query.astype(jnp.bfloat16)
        rest = query - high.astype(jnp.float32)
        middle = rest.astype(jnp.bfloat16)
        low = (rest - middle.astype(jnp.float32)).astype(jnp.bfloat16)
        spread_query = (
            jnp.dot(high, spread, preferred_element_type=jnp.float32)
            + jnp.dot(middle, spread, preferred_element_type=jnp.float32)
            + jnp.dot(low, spread, preferred_element_type=jnp.float32)
        )
        weighted = spread_query * state
        folded = weighted[:, 0:128]
        for c in range(1, flat // 128):
            folded = folded + weighted[:, 128 * c : 128 * (c + 1)]
        from_state = folded[:, :extent] + folded[:, extent:]
        bonus_term = jnp.sum(recept[t] * premium * key_vec[t], axis=-1, keepdims=True)
        total = bonus_term * valued[t] + from_state
        for s in range(t):
            factor = key_vec[s]
            for u in range(s + 1, t):
                factor = factor * decay_rate[u]
            total = total + jnp.sum(recept[t] * factor, axis=-1, keepdims=True) * valued[s]
        average = jnp.mean(total, axis=-1, keepdims=True)
        demeaned = total - average
        spread_squared = jnp.mean(demeaned * demeaned, axis=-1, keepdims=True)
        standardized = demeaned * lax.rsqrt(spread_squared + NORMALIZER_GUARD) * gain + bias
        mixed_ref[t] = (standardized * gate_ref[t]).astype(mixed_ref.dtype)
        prefix = prefix * decay_rate[t]
    payload_ref[0] = prefix.astype(payload_ref.dtype)
    for s in range(steps):
        factor = key_vec[s]
        for u in range(s + 1, steps):
            factor = factor * decay_rate[u]
        payload_ref[1 + s] = factor.astype(payload_ref.dtype)
        payload_ref[1 + steps + s] = valued[s].astype(payload_ref.dtype)


def row_block(rows):
    return 64 if rows % 64 == 0 else rows


def run_recurrence(projected, params, state):
    pieces = len(projected)
    steps, rows, extent = projected[0].shape
    flat = state.shape[-1]
    block = row_block(rows)
    return pl.pallas_call(
        functools.partial(recurrence_kernel, steps),
        grid=(rows // block,),
        in_specs=[
            *[pl.BlockSpec((steps, block, extent), lambda n: (0, n, 0))] * pieces,
            pl.BlockSpec((3, block, extent), lambda n: (0, n, 0)),
            pl.BlockSpec((block, flat), lambda n: (n, 0)),
        ],
        out_specs=[
            pl.BlockSpec((steps, block, extent), lambda n: (0, n, 0)),
            pl.BlockSpec((1 + 2 * steps, block, extent), lambda n: (0, n, 0)),
        ],
        out_shape=[
            jax.ShapeDtypeStruct((steps, rows, extent), jnp.bfloat16),
            jax.ShapeDtypeStruct((1 + 2 * steps, rows, extent), jnp.bfloat16),
        ],
        scratch_shapes=[pltpu.VMEM((extent, flat), jnp.bfloat16)],
        cost_estimate=pl.CostEstimate(
            flops=2 * rows * extent * flat * 3 * steps,
            transcendentals=steps * rows,
            bytes_accessed=rows * (flat * 4 + extent * (pieces * steps * 4 + 3 * 4 + steps * 2 + (1 + 2 * steps) * 2)),
        ),
    )(*projected, params, state)


def rebuild_kernel(steps, state_ref, terms_ref, out_ref, spread_ref, tile_ref):
    fill_tables(spread_ref, tile_ref)
    spread = spread_ref[...]
    tile = tile_ref[...]
    total = jnp.dot(terms_ref[0], spread, preferred_element_type=jnp.float32) * state_ref[...].astype(
        jnp.float32
    )
    for s in range(steps):
        total = total + jnp.dot(
            terms_ref[1 + s], spread, preferred_element_type=jnp.float32
        ) * jnp.dot(terms_ref[1 + steps + s], tile, preferred_element_type=jnp.float32)
    out_ref[...] = total


def rebuild_state(moved_state, moved_terms, steps):
    rows, flat = moved_state.shape
    pieces = moved_terms.shape[0]
    extent = SUBSPACE_EXTENT
    block = row_block(rows)
    return pl.pallas_call(
        functools.partial(rebuild_kernel, steps),
        grid=(rows // block,),
        in_specs=[
            pl.BlockSpec((block, flat), lambda n: (n, 0)),
            pl.BlockSpec((pieces, block, extent), lambda n: (0, n, 0)),
        ],
        out_specs=pl.BlockSpec((block, flat), lambda n: (n, 0)),
        out_shape=jax.ShapeDtypeStruct((rows, flat), jnp.float32),
        scratch_shapes=[
            pltpu.VMEM((extent, flat), jnp.bfloat16),
            pltpu.VMEM((extent, flat), jnp.bfloat16),
        ],
        cost_estimate=pl.CostEstimate(
            flops=2 * rows * extent * flat * (1 + 2 * steps),
            transcendentals=0,
            bytes_accessed=rows * (flat * 6 + pieces * extent * 2),
        ),
    )(moved_state, moved_terms)


def per_device(
    tier_feed_tensor,
    preceding_feed_each_stream,
    stream_kept_tableaux,
    position_mapping_target,
    lagging_mixture_weights,
    lagging_narrow_lowering,
    lagging_narrow_raising,
    fourfold_linear_maps,
    attenuation_narrow_lowering,
    attenuation_narrow_raising,
    attenuation_doublelog_anchor,
    instant_premium,
    norming_multiplier,
    norming_intercept,
    outgoing_linear_map,
):
    batch_count = lax.axis_size("batch")
    batch_index = lax.axis_index("batch")
    head_index = lax.axis_index("head")
    steps, sessions, feats = tier_feed_tensor.shape
    local_rows = sessions // batch_count
    heads_here = stream_kept_tableaux.shape[1]
    width = heads_here * SUBSPACE_EXTENT
    f32 = jnp.float32
    bf16 = jnp.bfloat16


    previous = jnp.concatenate([preceding_feed_each_stream[None], tier_feed_tensor[:-1]], axis=0)

    def by_block(value):
        return value.reshape(steps, batch_count, local_rows, feats).transpose(1, 0, 2, 3).reshape(
            batch_count * steps * local_rows, feats
        )

    x_float = by_block(tier_feed_tensor).astype(f32)
    shifted = by_block(previous).astype(f32) - x_float
    rows = x_float.shape[0]
    base_mix = (x_float + shifted * lagging_mixture_weights[0]).astype(bf16)
    partial_value = jnp.dot(base_mix, lagging_narrow_lowering, preferred_element_type=f32)
    hidden = jnp.tanh(
        jnp.sum(exchange_copies(partial_value.astype(bf16), "batch").astype(f32), axis=0)
    ).astype(bf16)
    hidden = hidden.reshape(rows, MIX_MAPS, lagging_narrow_raising.shape[1])
    offsets = jnp.einsum(
        "nim,imd->ind", hidden, lagging_narrow_raising, preferred_element_type=f32
    )
    mixed = (
        x_float[None] + shifted[None] * (lagging_mixture_weights[1:, None, :] + offsets)
    ).astype(bf16)
    main_part = jnp.einsum(
        "inf,ifc->inc", mixed[:4], fourfold_linear_maps, preferred_element_type=f32
    )
    decay_part = jnp.dot(mixed[4], attenuation_narrow_lowering, preferred_element_type=f32)
    main_sum, decay_sum = exchange_sum(
        (
            main_part.astype(bf16)
            .reshape(4, batch_count, steps * local_rows, width)
            .transpose(1, 0, 2, 3),
            decay_part.astype(bf16).reshape(batch_count, steps * local_rows, -1),
        ),
        "batch",
    )

    kept_for_move, main_sum, decay_sum = lax.optimization_barrier(
        (stream_kept_tableaux, main_sum, decay_sum)
    )
    moved_state = route_to_slots(
        kept_for_move.astype(bf16), position_mapping_target, batch_index, head_index
    )

    def heads_of(value):
        return value.reshape(steps, local_rows, heads_here, SUBSPACE_EXTENT)

    main_sum = main_sum.reshape(4, steps, local_rows, width)
    recept = heads_of(widen(main_sum[0]))
    key_vec = heads_of(widen(main_sum[1]))
    valued = heads_of(widen(main_sum[2]))
    gate_act = jax.nn.silu(main_sum[3])
    low_rank = jnp.tanh(decay_sum.reshape(steps, local_rows, -1)).astype(bf16)
    decay_rate = heads_of(
        jnp.exp(
            -jnp.exp(
                attenuation_doublelog_anchor
                + jnp.dot(low_rank, attenuation_narrow_raising, preferred_element_type=f32)
            )
        )
    )
    rows_here = local_rows * heads_here

    def by_row(value):
        return value.reshape(steps, rows_here, SUBSPACE_EXTENT)

    projected = tuple(by_row(value) for value in (recept, key_vec, valued, decay_rate, gate_act))
    params = jnp.broadcast_to(
        jnp.stack([instant_premium, norming_multiplier, norming_intercept]).reshape(
            3, 1, heads_here, SUBSPACE_EXTENT
        ),
        (3, local_rows, heads_here, SUBSPACE_EXTENT),
    ).reshape(3, rows_here, SUBSPACE_EXTENT)
    mixed_rows, payload = run_recurrence(
        projected, params, stream_kept_tableaux.reshape(rows_here, -1)
    )
    moved_state, mixed_rows, payload = lax.optimization_barrier((moved_state, mixed_rows, payload))
    combined_response = mixed_rows.reshape(steps, local_rows, width)
    pieces = payload.shape[0]
    head_count = lax.axis_size("head")
    cluster_number = head_count // 4
    slots_dev = local_rows // cluster_number
    per_pair = slots_dev // batch_count
    quarter = heads_here // 4
    own_map = lax.dynamic_slice_in_dim(
        position_mapping_target, batch_index * local_rows, local_rows
    )
    dest_key = own_map // slots_dev
    positions = jnp.arange(local_rows, dtype=jnp.int32)
    ahead = (dest_key[None, :] < dest_key[:, None]) | (
        (dest_key[None, :] == dest_key[:, None]) & (positions[None, :] < positions[:, None])
    )
    send_order = index_of(jnp.sum(ahead.astype(jnp.int32), axis=1), local_rows)
    factors = jnp.take(
        payload.reshape(pieces, local_rows, heads_here, SUBSPACE_EXTENT),
        send_order,
        axis=1,
        mode="clip",
    ).reshape(pieces, batch_count, cluster_number * per_pair, heads_here, SUBSPACE_EXTENT)
    gathered, factors = gather_with_parts(
        combined_response, factors.transpose(1, 0, 2, 3, 4), "batch"
    )
    gathered = gathered.transpose(1, 0, 2, 3).reshape(steps, sessions, width)
    factors = factors.reshape(
        batch_count, pieces, cluster_number, per_pair, 4, quarter, SUBSPACE_EXTENT
    ).transpose(4, 2, 0, 1, 3, 5, 6)
    factors = factors.reshape(
        head_count, batch_count, pieces, per_pair, quarter, SUBSPACE_EXTENT
    )
    inverse = index_of(position_mapping_target, sessions)
    arranged = jnp.concatenate(
        [gathered[:STEPS_A], jnp.take(gathered[STEPS_A:], inverse, axis=1, mode="clip")], axis=0
    )
    partial_y = jnp.einsum(
        "tnf,fo->tno", arranged, outgoing_linear_map, preferred_element_type=f32
    ).astype(bf16)
    produced, factors = sum_with_parts(
        partial_y.reshape(steps, head_count, sessions // head_count, -1).transpose(1, 0, 2, 3),
        factors,
        "head",
    )
    produced = produced.astype(bf16)
    factors = factors.transpose(2, 1, 3, 0, 4, 5).reshape(
        pieces, batch_count * per_pair, head_count * quarter, SUBSPACE_EXTENT
    )
    target = batch_index * cluster_number + head_index % cluster_number
    chosen = lax.dynamic_slice_in_dim(inverse, target * slots_dev, slots_dev)
    every = jnp.arange(sessions, dtype=jnp.int32)
    coming = (position_mapping_target // slots_dev) == target
    placing = jnp.sum(
        ((every[None, :] < chosen[:, None]) & coming[None, :]).astype(jnp.int32), axis=1
    )
    moved_terms = jnp.take(factors, placing, axis=1, mode="clip").reshape(
        pieces, slots_dev * head_count * quarter, SUBSPACE_EXTENT
    )
    columns = head_count * quarter
    final_state = rebuild_state(
        moved_state.reshape(slots_dev * columns, -1), moved_terms, steps
    ).reshape(slots_dev, columns, -1)
    return (produced[:STEPS_A], produced[STEPS_A:], final_state)


def solution(mesh):
    in_specs = (
        P(None, "groups", "batch"),
        P("groups", "batch"),
        P(("groups", "batch"), "head", None),
        P("groups"),
        P(None, "batch"),
        P("batch", None),
        P(None, None, "batch"),
        P(None, "batch", "head"),
        P("batch", None),
        P(None, "head"),
        P("head"),
        P("head"),
        P("head"),
        P("head"),
        P("head", "batch"),
    )
    out_specs = (
        P(None, ("groups", "head"), "batch"),
        P(None, ("groups", "head"), "batch"),
        P(("groups", "batch", "head"), None, None),
    )
    return jax.shard_map(
        per_device, mesh=mesh, in_specs=in_specs, out_specs=out_specs, check_vma=False
    )
```

```python
import functools

import jax
import jax.numpy as jnp
from jax import lax
from jax.experimental import pallas as pl
from jax.experimental.pallas import tpu as pltpu
from jax.sharding import PartitionSpec as P

SUBSPACE_EXTENT = 64
STEPS_A = 2
MIX_MAPS = 5
NORMALIZER_GUARD = 0.00064


def index_of(values, count):
    positions = jnp.arange(values.shape[0], dtype=jnp.int32)
    wanted = jnp.arange(count, dtype=jnp.int32)
    return jnp.sum(jnp.where(values[None, :] == wanted[:, None], positions[None, :], 0), axis=1)


def route_to_slots(value, position_mapping_target, batch_index, head_index, after=None):
    batch_count = lax.axis_size("batch")
    head_count = lax.axis_size("head")
    local_rows, heads_here, width = value.shape
    cluster_number = head_count // 4
    slots_dev = local_rows // cluster_number
    per_pair = slots_dev // batch_count
    quarter = heads_here // 4
    own_map = lax.dynamic_slice_in_dim(
        position_mapping_target, batch_index * local_rows, local_rows
    )
    dest_key = own_map // slots_dev
    positions = jnp.arange(local_rows, dtype=jnp.int32)
    ahead = (dest_key[None, :] < dest_key[:, None]) | (
        (dest_key[None, :] == dest_key[:, None]) & (positions[None, :] < positions[:, None])
    )
    send_order = index_of(jnp.sum(ahead.astype(jnp.int32), axis=1), local_rows)
    dest = jnp.arange(batch_count * head_count, dtype=jnp.int32)
    dest_block = (dest // head_count) * cluster_number + dest % cluster_number
    quad = (dest % head_count) // cluster_number
    pair = jnp.arange(per_pair, dtype=jnp.int32)
    within = jnp.arange(quarter, dtype=jnp.int32)
    sent_sessions = jnp.take(
        send_order, dest_block[:, None] * per_pair + pair[None, :], mode="clip"
    )
    sent_rows = (
        sent_sessions[:, :, None] * heads_here
        + (quad * quarter)[:, None, None]
        + within[None, None, :]
    )
    packed = jnp.take(
        value.reshape(local_rows * heads_here, width), sent_rows.reshape(-1), axis=0, mode="clip"
    ).reshape(batch_count * head_count, per_pair * quarter, width)
    if after is not None:
        packed, after = lax.optimization_barrier((packed, after))
    arrived = lax.all_to_all(packed, ("batch", "head"), split_axis=0, concat_axis=0, tiled=True)
    target = batch_index * cluster_number + head_index % cluster_number
    sessions = position_mapping_target.shape[0]
    chosen = lax.dynamic_slice_in_dim(
        index_of(position_mapping_target, sessions), target * slots_dev, slots_dev
    )
    every = jnp.arange(sessions, dtype=jnp.int32)
    coming = (position_mapping_target // slots_dev) == target
    placing = jnp.sum(
        ((every[None, :] < chosen[:, None]) & coming[None, :]).astype(jnp.int32), axis=1
    )
    source_head = jnp.arange(head_count, dtype=jnp.int32)
    kept_rows = (
        (
            (placing[:, None, None] // per_pair) * head_count + source_head[None, :, None]
        )
        * per_pair
        + placing[:, None, None] % per_pair
    ) * quarter + within[None, None, :]
    return jnp.take(
        arrived.reshape(-1, width), kept_rows.reshape(-1), axis=0, mode="clip"
    ).reshape(slots_dev, head_count * quarter, width)

def exchange_sum(pieces, axis_name):
    count = lax.axis_size(axis_name)
    index = lax.axis_index(axis_name)

    def own(shift):
        return jax.tree.map(
            lambda value: lax.dynamic_index_in_dim(value, (index + shift) % count, keepdims=False),
            pieces,
        )

    total = jax.tree.map(lambda value: value.astype(jnp.float32), own(0))
    for shift in range(1, count):
        arrived = lax.ppermute(
            own(shift), axis_name, [(i, (i + shift) % count) for i in range(count)]
        )
        total = jax.tree.map(lambda acc, value: acc + value.astype(jnp.float32), total, arrived)
    return total

def exchange_copies(value, axis_name):
    count = lax.axis_size(axis_name)
    index = lax.axis_index(axis_name)
    received = [value]
    for shift in range(1, count):
        received.append(
            lax.ppermute(value, axis_name, [(i, (i + shift) % count) for i in range(count)])
        )
    shifts = (index - jnp.arange(count, dtype=jnp.int32)) % count
    return jnp.take(jnp.stack(received), shifts, axis=0, mode="clip")

def by_source(received, index, count):
    shifts = (index - jnp.arange(count, dtype=jnp.int32)) % count
    return jnp.take(jnp.stack(received), shifts, axis=0, mode="clip")


def gather_with_parts(value, parts, axis_name):
    count = lax.axis_size(axis_name)
    index = lax.axis_index(axis_name)
    copies = [value]
    moved = [lax.dynamic_index_in_dim(parts, index, keepdims=False)]
    for shift in range(1, count):
        sent = lax.dynamic_index_in_dim(parts, (index + shift) % count, keepdims=False)
        copy, part = lax.ppermute(
            (value, sent), axis_name, [(i, (i + shift) % count) for i in range(count)]
        )
        copies.append(copy)
        moved.append(part)
    return by_source(copies, index, count), by_source(moved, index, count)


def sum_with_parts(pieces, parts, axis_name):
    count = lax.axis_size(axis_name)
    index = lax.axis_index(axis_name)
    total = lax.dynamic_index_in_dim(pieces, index, keepdims=False).astype(jnp.float32)
    moved = [lax.dynamic_index_in_dim(parts, index, keepdims=False)]
    for shift in range(1, count):
        target = (index + shift) % count
        piece, part = lax.ppermute(
            (
                lax.dynamic_index_in_dim(pieces, target, keepdims=False),
                lax.dynamic_index_in_dim(parts, target, keepdims=False),
            ),
            axis_name,
            [(i, (i + shift) % count) for i in range(count)],
        )
        total = total + piece.astype(jnp.float32)
        moved.append(part)
    return total, by_source(moved, index, count)


def widen(value):
    return value.astype(jnp.bfloat16).astype(jnp.float32)


def fill_tables(spread_ref, tile_ref=None):
    extent = SUBSPACE_EXTENT

    @pl.when(pl.program_id(0) == 0)
    def _():
        lane = lax.broadcasted_iota(jnp.int32, spread_ref.shape, 1)
        row = lax.broadcasted_iota(jnp.int32, spread_ref.shape, 0)
        spread_ref[...] = (lane // extent == row).astype(spread_ref.dtype)
        if tile_ref is not None:
            tile_ref[...] = (lane % extent == row).astype(tile_ref.dtype)


def recurrence_kernel(
    steps,
    recept_ref,
    key_ref,
    value_ref,
    decay_ref,
    gate_ref,
    params_ref,
    state_ref,
    mixed_ref,
    payload_ref,
    spread_ref,
):
    extent = SUBSPACE_EXTENT
    fill_tables(spread_ref)
    spread = spread_ref[...]
    state = state_ref[...]
    premium = params_ref[0]
    gain = params_ref[1]
    bias = params_ref[2]
    recept = [recept_ref[t] for t in range(steps)]
    key_vec = [key_ref[t] for t in range(steps)]
    valued = [value_ref[t] for t in range(steps)]
    decay_rate = [decay_ref[t] for t in range(steps)]
    flat = state.shape[-1]
    prefix = jnp.ones_like(recept[0])
    for t in range(steps):
        query = recept[t] * prefix
        high = query.astype(jnp.bfloat16)
        rest = query - high.astype(jnp.float32)
        middle = rest.astype(jnp.bfloat16)
        low = (rest - middle.astype(jnp.float32)).astype(jnp.bfloat16)
        spread_query = (
            jnp.dot(high, spread, preferred_element_type=jnp.float32)
            + jnp.dot(middle, spread, preferred_element_type=jnp.float32)
            + jnp.dot(low, spread, preferred_element_type=jnp.float32)
        )
        weighted = spread_query * state
        folded = weighted[:, 0:128]
        for c in range(1, flat // 128):
            folded = folded + weighted[:, 128 * c : 128 * (c + 1)]
        from_state = folded[:, :extent] + folded[:, extent:]
        bonus_term = jnp.sum(recept[t] * premium * key_vec[t], axis=-1, keepdims=True)
        total = bonus_term * valued[t] + from_state
        for s in range(t):
            factor = key_vec[s]
            for u in range(s + 1, t):
                factor = factor * decay_rate[u]
            total = total + jnp.sum(recept[t] * factor, axis=-1, keepdims=True) * valued[s]
        average = jnp.mean(total, axis=-1, keepdims=True)
        demeaned = total - average
        spread_squared = jnp.mean(demeaned * demeaned, axis=-1, keepdims=True)
        standardized = demeaned * lax.rsqrt(spread_squared + NORMALIZER_GUARD) * gain + bias
        mixed_ref[t] = (standardized * gate_ref[t]).astype(mixed_ref.dtype)
        prefix = prefix * decay_rate[t]
    payload_ref[0] = prefix.astype(payload_ref.dtype)
    for s in range(steps):
        factor = key_vec[s]
        for u in range(s + 1, steps):
            factor = factor * decay_rate[u]
        payload_ref[1 + s] = factor.astype(payload_ref.dtype)
        payload_ref[1 + steps + s] = valued[s].astype(payload_ref.dtype)


def row_block(rows):
    return 64 if rows % 64 == 0 else rows


def run_recurrence(projected, params, state):
    pieces = len(projected)
    steps, rows, extent = projected[0].shape
    flat = state.shape[-1]
    block = row_block(rows)
    return pl.pallas_call(
        functools.partial(recurrence_kernel, steps),
        grid=(rows // block,),
        in_specs=[
            *[pl.BlockSpec((steps, block, extent), lambda n: (0, n, 0))] * pieces,
            pl.BlockSpec((3, block, extent), lambda n: (0, n, 0)),
            pl.BlockSpec((block, flat), lambda n: (n, 0)),
        ],
        out_specs=[
            pl.BlockSpec((steps, block, extent), lambda n: (0, n, 0)),
            pl.BlockSpec((1 + 2 * steps, block, extent), lambda n: (0, n, 0)),
        ],
        out_shape=[
            jax.ShapeDtypeStruct((steps, rows, extent), jnp.bfloat16),
            jax.ShapeDtypeStruct((1 + 2 * steps, rows, extent), jnp.bfloat16),
        ],
        scratch_shapes=[pltpu.VMEM((extent, flat), jnp.bfloat16)],
        cost_estimate=pl.CostEstimate(
            flops=2 * rows * extent * flat * 3 * steps,
            transcendentals=steps * rows,
            bytes_accessed=rows * (flat * 4 + extent * (pieces * steps * 4 + 3 * 4 + steps * 2 + (1 + 2 * steps) * 2)),
        ),
    )(*projected, params, state)


def rebuild_kernel(steps, state_ref, terms_ref, out_ref, spread_ref, tile_ref):
    fill_tables(spread_ref, tile_ref)
    spread = spread_ref[...]
    tile = tile_ref[...]
    total = jnp.dot(terms_ref[0], spread, preferred_element_type=jnp.float32) * state_ref[...].astype(
        jnp.float32
    )
    for s in range(steps):
        total = total + jnp.dot(
            terms_ref[1 + s], spread, preferred_element_type=jnp.float32
        ) * jnp.dot(terms_ref[1 + steps + s], tile, preferred_element_type=jnp.float32)
    out_ref[...] = total


def rebuild_state(moved_state, moved_terms, steps):
    rows, flat = moved_state.shape
    pieces = moved_terms.shape[0]
    extent = SUBSPACE_EXTENT
    block = row_block(rows)
    return pl.pallas_call(
        functools.partial(rebuild_kernel, steps),
        grid=(rows // block,),
        in_specs=[
            pl.BlockSpec((block, flat), lambda n: (n, 0)),
            pl.BlockSpec((pieces, block, extent), lambda n: (0, n, 0)),
        ],
        out_specs=pl.BlockSpec((block, flat), lambda n: (n, 0)),
        out_shape=jax.ShapeDtypeStruct((rows, flat), jnp.float32),
        scratch_shapes=[
            pltpu.VMEM((extent, flat), jnp.bfloat16),
            pltpu.VMEM((extent, flat), jnp.bfloat16),
        ],
        cost_estimate=pl.CostEstimate(
            flops=2 * rows * extent * flat * (1 + 2 * steps),
            transcendentals=0,
            bytes_accessed=rows * (flat * 6 + pieces * extent * 2),
        ),
    )(moved_state, moved_terms)


def per_device(
    tier_feed_tensor,
    preceding_feed_each_stream,
    stream_kept_tableaux,
    position_mapping_target,
    lagging_mixture_weights,
    lagging_narrow_lowering,
    lagging_narrow_raising,
    fourfold_linear_maps,
    attenuation_narrow_lowering,
    attenuation_narrow_raising,
    attenuation_doublelog_anchor,
    instant_premium,
    norming_multiplier,
    norming_intercept,
    outgoing_linear_map,
):
    batch_count = lax.axis_size("batch")
    batch_index = lax.axis_index("batch")
    head_index = lax.axis_index("head")
    steps, sessions, feats = tier_feed_tensor.shape
    local_rows = sessions // batch_count
    heads_here = stream_kept_tableaux.shape[1]
    width = heads_here * SUBSPACE_EXTENT
    f32 = jnp.float32
    bf16 = jnp.bfloat16


    previous = jnp.concatenate([preceding_feed_each_stream[None], tier_feed_tensor[:-1]], axis=0)

    def by_block(value):
        return value.reshape(steps, batch_count, local_rows, feats).transpose(1, 0, 2, 3).reshape(
            batch_count * steps * local_rows, feats
        )

    x_float = by_block(tier_feed_tensor).astype(f32)
    shifted = by_block(previous).astype(f32) - x_float
    rows = x_float.shape[0]
    base_mix = (x_float + shifted * lagging_mixture_weights[0]).astype(bf16)
    partial_value = jnp.dot(base_mix, lagging_narrow_lowering, preferred_element_type=f32)
    hidden = jnp.tanh(
        jnp.sum(exchange_copies(partial_value.astype(bf16), "batch").astype(f32), axis=0)
    ).astype(bf16)
    hidden = hidden.reshape(rows, MIX_MAPS, lagging_narrow_raising.shape[1])
    offsets = jnp.einsum(
        "nim,imd->ind", hidden, lagging_narrow_raising, preferred_element_type=f32
    )
    mixed = (
        x_float[None] + shifted[None] * (lagging_mixture_weights[1:, None, :] + offsets)
    ).astype(bf16)
    main_part = jnp.einsum(
        "inf,ifc->inc", mixed[:4], fourfold_linear_maps, preferred_element_type=f32
    )
    decay_part = jnp.dot(mixed[4], attenuation_narrow_lowering, preferred_element_type=f32)
    main_sum, decay_sum = exchange_sum(
        (
            main_part.astype(bf16)
            .reshape(4, batch_count, steps * local_rows, width)
            .transpose(1, 0, 2, 3),
            decay_part.astype(bf16).reshape(batch_count, steps * local_rows, -1),
        ),
        "batch",
    )

    moved_state = route_to_slots(
        stream_kept_tableaux.astype(bf16),
        position_mapping_target,
        batch_index,
        head_index,
        after=(main_sum, decay_sum),
    )

    def heads_of(value):
        return value.reshape(steps, local_rows, heads_here, SUBSPACE_EXTENT)

    main_sum = main_sum.reshape(4, steps, local_rows, width)
    recept = heads_of(widen(main_sum[0]))
    key_vec = heads_of(widen(main_sum[1]))
    valued = heads_of(widen(main_sum[2]))
    gate_act = jax.nn.silu(main_sum[3])
    low_rank = jnp.tanh(decay_sum.reshape(steps, local_rows, -1)).astype(bf16)
    decay_rate = heads_of(
        jnp.exp(
            -jnp.exp(
                attenuation_doublelog_anchor
                + jnp.dot(low_rank, attenuation_narrow_raising, preferred_element_type=f32)
            )
        )
    )
    rows_here = local_rows * heads_here

    def by_row(value):
        return value.reshape(steps, rows_here, SUBSPACE_EXTENT)

    projected = tuple(by_row(value) for value in (recept, key_vec, valued, decay_rate, gate_act))
    params = jnp.broadcast_to(
        jnp.stack([instant_premium, norming_multiplier, norming_intercept]).reshape(
            3, 1, heads_here, SUBSPACE_EXTENT
        ),
        (3, local_rows, heads_here, SUBSPACE_EXTENT),
    ).reshape(3, rows_here, SUBSPACE_EXTENT)
    mixed_rows, payload = run_recurrence(
        projected, params, stream_kept_tableaux.reshape(rows_here, -1)
    )
    moved_state, mixed_rows, payload = lax.optimization_barrier((moved_state, mixed_rows, payload))
    combined_response = mixed_rows.reshape(steps, local_rows, width)
    pieces = payload.shape[0]
    head_count = lax.axis_size("head")
    cluster_number = head_count // 4
    slots_dev = local_rows // cluster_number
    per_pair = slots_dev // batch_count
    quarter = heads_here // 4
    own_map = lax.dynamic_slice_in_dim(
        position_mapping_target, batch_index * local_rows, local_rows
    )
    dest_key = own_map // slots_dev
    positions = jnp.arange(local_rows, dtype=jnp.int32)
    ahead = (dest_key[None, :] < dest_key[:, None]) | (
        (dest_key[None, :] == dest_key[:, None]) & (positions[None, :] < positions[:, None])
    )
    send_order = index_of(jnp.sum(ahead.astype(jnp.int32), axis=1), local_rows)
    factors = jnp.take(
        payload.reshape(pieces, local_rows, heads_here, SUBSPACE_EXTENT),
        send_order,
        axis=1,
        mode="clip",
    ).reshape(pieces, batch_count, cluster_number * per_pair, heads_here, SUBSPACE_EXTENT)
    gathered, factors = gather_with_parts(
        combined_response, factors.transpose(1, 0, 2, 3, 4), "batch"
    )
    gathered = gathered.transpose(1, 0, 2, 3).reshape(steps, sessions, width)
    factors = factors.reshape(
        batch_count, pieces, cluster_number, per_pair, 4, quarter, SUBSPACE_EXTENT
    ).transpose(4, 2, 0, 1, 3, 5, 6)
    factors = factors.reshape(
        head_count, batch_count, pieces, per_pair, quarter, SUBSPACE_EXTENT
    )
    inverse = index_of(position_mapping_target, sessions)
    arranged = jnp.concatenate(
        [gathered[:STEPS_A], jnp.take(gathered[STEPS_A:], inverse, axis=1, mode="clip")], axis=0
    )
    partial_y = jnp.einsum(
        "tnf,fo->tno", arranged, outgoing_linear_map, preferred_element_type=f32
    ).astype(bf16)
    produced, factors = sum_with_parts(
        partial_y.reshape(steps, head_count, sessions // head_count, -1).transpose(1, 0, 2, 3),
        factors,
        "head",
    )
    produced = produced.astype(bf16)
    factors = factors.transpose(2, 1, 3, 0, 4, 5).reshape(
        pieces, batch_count * per_pair, head_count * quarter, SUBSPACE_EXTENT
    )
    target = batch_index * cluster_number + head_index % cluster_number
    chosen = lax.dynamic_slice_in_dim(inverse, target * slots_dev, slots_dev)
    every = jnp.arange(sessions, dtype=jnp.int32)
    coming = (position_mapping_target // slots_dev) == target
    placing = jnp.sum(
        ((every[None, :] < chosen[:, None]) & coming[None, :]).astype(jnp.int32), axis=1
    )
    moved_terms = jnp.take(factors, placing, axis=1, mode="clip").reshape(
        pieces, slots_dev * head_count * quarter, SUBSPACE_EXTENT
    )
    columns = head_count * quarter
    final_state = rebuild_state(
        moved_state.reshape(slots_dev * columns, -1), moved_terms, steps
    ).reshape(slots_dev, columns, -1)
    return (produced[:STEPS_A], produced[STEPS_A:], final_state)


def solution(mesh):
    in_specs = (
        P(None, "groups", "batch"),
        P("groups", "batch"),
        P(("groups", "batch"), "head", None),
        P("groups"),
        P(None, "batch"),
        P("batch", None),
        P(None, None, "batch"),
        P(None, "batch", "head"),
        P("batch", None),
        P(None, "head"),
        P("head"),
        P("head"),
        P("head"),
        P("head"),
        P("head", "batch"),
    )
    out_specs = (
        P(None, ("groups", "head"), "batch"),
        P(None, ("groups", "head"), "batch"),
        P(("groups", "batch", "head"), None, None),
    )
    return jax.shard_map(
        per_device, mesh=mesh, in_specs=in_specs, out_specs=out_specs, check_vma=False
    )
```

```python
import functools

import jax
import jax.numpy as jnp
from jax import lax
from jax.experimental import pallas as pl
from jax.experimental.pallas import tpu as pltpu
from jax.sharding import PartitionSpec as P

SUBSPACE_EXTENT = 64
STEPS_A = 2
MIX_MAPS = 5
NORMALIZER_GUARD = 0.00064


def index_of(values, count):
    positions = jnp.arange(values.shape[0], dtype=jnp.int32)
    wanted = jnp.arange(count, dtype=jnp.int32)
    return jnp.sum(jnp.where(values[None, :] == wanted[:, None], positions[None, :], 0), axis=1)


def slot_routes(position_mapping_target, local_rows, heads_here, batch_index, head_index):
    batch_count = lax.axis_size("batch")
    head_count = lax.axis_size("head")
    sessions = position_mapping_target.shape[0]
    cluster_number = head_count // 4
    slots_dev = local_rows // cluster_number
    per_pair = slots_dev // batch_count
    quarter = heads_here // 4
    own_map = lax.dynamic_slice_in_dim(
        position_mapping_target, batch_index * local_rows, local_rows
    )
    dest_key = own_map // slots_dev
    positions = jnp.arange(local_rows, dtype=jnp.int32)
    ahead = (dest_key[None, :] < dest_key[:, None]) | (
        (dest_key[None, :] == dest_key[:, None]) & (positions[None, :] < positions[:, None])
    )
    send_order = index_of(jnp.sum(ahead.astype(jnp.int32), axis=1), local_rows)
    dest = jnp.arange(batch_count * head_count, dtype=jnp.int32)
    dest_block = (dest // head_count) * cluster_number + dest % cluster_number
    quad = (dest % head_count) // cluster_number
    pair = jnp.arange(per_pair, dtype=jnp.int32)
    within = jnp.arange(quarter, dtype=jnp.int32)
    sent_sessions = jnp.take(
        send_order, dest_block[:, None] * per_pair + pair[None, :], mode="clip"
    )
    sent_rows = (
        sent_sessions[:, :, None] * heads_here
        + (quad * quarter)[:, None, None]
        + within[None, None, :]
    ).reshape(-1)
    inverse = index_of(position_mapping_target, sessions)
    target = batch_index * cluster_number + head_index % cluster_number
    chosen = lax.dynamic_slice_in_dim(inverse, target * slots_dev, slots_dev)
    every = jnp.arange(sessions, dtype=jnp.int32)
    coming = (position_mapping_target // slots_dev) == target
    placing = jnp.sum(
        ((every[None, :] < chosen[:, None]) & coming[None, :]).astype(jnp.int32), axis=1
    )
    source_head = jnp.arange(head_count, dtype=jnp.int32)
    kept_rows = (
        (
            (placing[:, None, None] // per_pair) * head_count + source_head[None, :, None]
        )
        * per_pair
        + placing[:, None, None] % per_pair
    ) * quarter + within[None, None, :]
    return {
        "send_order": send_order,
        "sent_rows": sent_rows,
        "inverse": inverse,
        "placing": placing,
        "kept_rows": kept_rows.reshape(-1),
    }


def route_to_slots(value, routes, after=None):
    batch_count = lax.axis_size("batch")
    head_count = lax.axis_size("head")
    local_rows, heads_here, width = value.shape
    cluster_number = head_count // 4
    slots_dev = local_rows // cluster_number
    quarter = heads_here // 4
    packed = jnp.take(
        value.reshape(local_rows * heads_here, width), routes["sent_rows"], axis=0, mode="clip"
    ).reshape(batch_count * head_count, -1, width)
    if after is not None:
        packed, after = lax.optimization_barrier((packed, after))
    arrived = lax.all_to_all(packed, ("batch", "head"), split_axis=0, concat_axis=0, tiled=True)
    return jnp.take(
        arrived.reshape(-1, width), routes["kept_rows"], axis=0, mode="clip"
    ).reshape(slots_dev, head_count * quarter, width)

def exchange_sum(pieces, axis_name):
    count = lax.axis_size(axis_name)
    index = lax.axis_index(axis_name)

    def own(shift):
        return jax.tree.map(
            lambda value: lax.dynamic_index_in_dim(value, (index + shift) % count, keepdims=False),
            pieces,
        )

    total = jax.tree.map(lambda value: value.astype(jnp.float32), own(0))
    for shift in range(1, count):
        arrived = lax.ppermute(
            own(shift), axis_name, [(i, (i + shift) % count) for i in range(count)]
        )
        total = jax.tree.map(lambda acc, value: acc + value.astype(jnp.float32), total, arrived)
    return total

def exchange_copies(value, axis_name):
    count = lax.axis_size(axis_name)
    index = lax.axis_index(axis_name)
    received = [value]
    for shift in range(1, count):
        received.append(
            lax.ppermute(value, axis_name, [(i, (i + shift) % count) for i in range(count)])
        )
    shifts = (index - jnp.arange(count, dtype=jnp.int32)) % count
    return jnp.take(jnp.stack(received), shifts, axis=0, mode="clip")

def by_source(received, index, count):
    shifts = (index - jnp.arange(count, dtype=jnp.int32)) % count
    return jnp.take(jnp.stack(received), shifts, axis=0, mode="clip")


def gather_with_parts(value, parts, axis_name):
    count = lax.axis_size(axis_name)
    index = lax.axis_index(axis_name)
    copies = [value]
    moved = [lax.dynamic_index_in_dim(parts, index, keepdims=False)]
    for shift in range(1, count):
        sent = lax.dynamic_index_in_dim(parts, (index + shift) % count, keepdims=False)
        copy, part = lax.ppermute(
            (value, sent), axis_name, [(i, (i + shift) % count) for i in range(count)]
        )
        copies.append(copy)
        moved.append(part)
    return by_source(copies, index, count), by_source(moved, index, count)


def sum_with_parts(pieces, parts, axis_name):
    count = lax.axis_size(axis_name)
    index = lax.axis_index(axis_name)
    total = lax.dynamic_index_in_dim(pieces, index, keepdims=False).astype(jnp.float32)
    moved = [lax.dynamic_index_in_dim(parts, index, keepdims=False)]
    for shift in range(1, count):
        target = (index + shift) % count
        piece, part = lax.ppermute(
            (
                lax.dynamic_index_in_dim(pieces, target, keepdims=False),
                lax.dynamic_index_in_dim(parts, target, keepdims=False),
            ),
            axis_name,
            [(i, (i + shift) % count) for i in range(count)],
        )
        total = total + piece.astype(jnp.float32)
        moved.append(part)
    return total, by_source(moved, index, count)


def widen(value):
    return value.astype(jnp.bfloat16).astype(jnp.float32)


def fill_tables(spread_ref, tile_ref=None):
    extent = SUBSPACE_EXTENT

    @pl.when(pl.program_id(0) == 0)
    def _():
        lane = lax.broadcasted_iota(jnp.int32, spread_ref.shape, 1)
        row = lax.broadcasted_iota(jnp.int32, spread_ref.shape, 0)
        spread_ref[...] = (lane // extent == row).astype(spread_ref.dtype)
        if tile_ref is not None:
            tile_ref[...] = (lane % extent == row).astype(tile_ref.dtype)


def recurrence_kernel(
    steps,
    recept_ref,
    key_ref,
    value_ref,
    decay_ref,
    gate_ref,
    params_ref,
    state_ref,
    mixed_ref,
    payload_ref,
    spread_ref,
):
    extent = SUBSPACE_EXTENT
    fill_tables(spread_ref)
    spread = spread_ref[...]
    state = state_ref[...]
    premium = params_ref[0]
    gain = params_ref[1]
    bias = params_ref[2]
    recept = [recept_ref[t] for t in range(steps)]
    key_vec = [key_ref[t] for t in range(steps)]
    valued = [value_ref[t] for t in range(steps)]
    decay_rate = [decay_ref[t] for t in range(steps)]
    flat = state.shape[-1]
    prefix = jnp.ones_like(recept[0])
    for t in range(steps):
        query = recept[t] * prefix
        high = query.astype(jnp.bfloat16)
        rest = query - high.astype(jnp.float32)
        middle = rest.astype(jnp.bfloat16)
        low = (rest - middle.astype(jnp.float32)).astype(jnp.bfloat16)
        spread_query = (
            jnp.dot(high, spread, preferred_element_type=jnp.float32)
            + jnp.dot(middle, spread, preferred_element_type=jnp.float32)
            + jnp.dot(low, spread, preferred_element_type=jnp.float32)
        )
        weighted = spread_query * state
        folded = weighted[:, 0:128]
        for c in range(1, flat // 128):
            folded = folded + weighted[:, 128 * c : 128 * (c + 1)]
        from_state = folded[:, :extent] + folded[:, extent:]
        bonus_term = jnp.sum(recept[t] * premium * key_vec[t], axis=-1, keepdims=True)
        total = bonus_term * valued[t] + from_state
        for s in range(t):
            factor = key_vec[s]
            for u in range(s + 1, t):
                factor = factor * decay_rate[u]
            total = total + jnp.sum(recept[t] * factor, axis=-1, keepdims=True) * valued[s]
        average = jnp.mean(total, axis=-1, keepdims=True)
        demeaned = total - average
        spread_squared = jnp.mean(demeaned * demeaned, axis=-1, keepdims=True)
        standardized = demeaned * lax.rsqrt(spread_squared + NORMALIZER_GUARD) * gain + bias
        mixed_ref[t] = (standardized * gate_ref[t]).astype(mixed_ref.dtype)
        prefix = prefix * decay_rate[t]
    payload_ref[0] = prefix.astype(payload_ref.dtype)
    for s in range(steps):
        factor = key_vec[s]
        for u in range(s + 1, steps):
            factor = factor * decay_rate[u]
        payload_ref[1 + s] = factor.astype(payload_ref.dtype)
        payload_ref[1 + steps + s] = valued[s].astype(payload_ref.dtype)


def row_block(rows):
    return 64 if rows % 64 == 0 else rows


def run_recurrence(projected, params, state):
    pieces = len(projected)
    steps, rows, extent = projected[0].shape
    flat = state.shape[-1]
    block = row_block(rows)
    return pl.pallas_call(
        functools.partial(recurrence_kernel, steps),
        grid=(rows // block,),
        in_specs=[
            *[pl.BlockSpec((steps, block, extent), lambda n: (0, n, 0))] * pieces,
            pl.BlockSpec((3, block, extent), lambda n: (0, n, 0)),
            pl.BlockSpec((block, flat), lambda n: (n, 0)),
        ],
        out_specs=[
            pl.BlockSpec((steps, block, extent), lambda n: (0, n, 0)),
            pl.BlockSpec((1 + 2 * steps, block, extent), lambda n: (0, n, 0)),
        ],
        out_shape=[
            jax.ShapeDtypeStruct((steps, rows, extent), jnp.bfloat16),
            jax.ShapeDtypeStruct((1 + 2 * steps, rows, extent), jnp.bfloat16),
        ],
        scratch_shapes=[pltpu.VMEM((extent, flat), jnp.bfloat16)],
        cost_estimate=pl.CostEstimate(
            flops=2 * rows * extent * flat * 3 * steps,
            transcendentals=steps * rows,
            bytes_accessed=rows * (flat * 4 + extent * (pieces * steps * 4 + 3 * 4 + steps * 2 + (1 + 2 * steps) * 2)),
        ),
    )(*projected, params, state)


def rebuild_kernel(steps, state_ref, terms_ref, out_ref, spread_ref, tile_ref):
    fill_tables(spread_ref, tile_ref)
    spread = spread_ref[...]
    tile = tile_ref[...]
    total = jnp.dot(terms_ref[0], spread, preferred_element_type=jnp.float32) * state_ref[...].astype(
        jnp.float32
    )
    for s in range(steps):
        total = total + jnp.dot(
            terms_ref[1 + s], spread, preferred_element_type=jnp.float32
        ) * jnp.dot(terms_ref[1 + steps + s], tile, preferred_element_type=jnp.float32)
    out_ref[...] = total


def rebuild_state(moved_state, moved_terms, steps):
    rows, flat = moved_state.shape
    pieces = moved_terms.shape[0]
    extent = SUBSPACE_EXTENT
    block = row_block(rows)
    return pl.pallas_call(
        functools.partial(rebuild_kernel, steps),
        grid=(rows // block,),
        in_specs=[
            pl.BlockSpec((block, flat), lambda n: (n, 0)),
            pl.BlockSpec((pieces, block, extent), lambda n: (0, n, 0)),
        ],
        out_specs=pl.BlockSpec((block, flat), lambda n: (n, 0)),
        out_shape=jax.ShapeDtypeStruct((rows, flat), jnp.float32),
        scratch_shapes=[
            pltpu.VMEM((extent, flat), jnp.bfloat16),
            pltpu.VMEM((extent, flat), jnp.bfloat16),
        ],
        cost_estimate=pl.CostEstimate(
            flops=2 * rows * extent * flat * (1 + 2 * steps),
            transcendentals=0,
            bytes_accessed=rows * (flat * 6 + pieces * extent * 2),
        ),
    )(moved_state, moved_terms)


def per_device(
    tier_feed_tensor,
    preceding_feed_each_stream,
    stream_kept_tableaux,
    position_mapping_target,
    lagging_mixture_weights,
    lagging_narrow_lowering,
    lagging_narrow_raising,
    fourfold_linear_maps,
    attenuation_narrow_lowering,
    attenuation_narrow_raising,
    attenuation_doublelog_anchor,
    instant_premium,
    norming_multiplier,
    norming_intercept,
    outgoing_linear_map,
):
    batch_count = lax.axis_size("batch")
    batch_index = lax.axis_index("batch")
    head_index = lax.axis_index("head")
    steps, sessions, feats = tier_feed_tensor.shape
    local_rows = sessions // batch_count
    heads_here = stream_kept_tableaux.shape[1]
    width = heads_here * SUBSPACE_EXTENT
    f32 = jnp.float32
    bf16 = jnp.bfloat16


    previous = jnp.concatenate([preceding_feed_each_stream[None], tier_feed_tensor[:-1]], axis=0)

    def by_block(value):
        return value.reshape(steps, batch_count, local_rows, feats).transpose(1, 0, 2, 3).reshape(
            batch_count * steps * local_rows, feats
        )

    x_float = by_block(tier_feed_tensor).astype(f32)
    shifted = by_block(previous).astype(f32) - x_float
    rows = x_float.shape[0]
    base_mix = (x_float + shifted * lagging_mixture_weights[0]).astype(bf16)
    partial_value = jnp.dot(base_mix, lagging_narrow_lowering, preferred_element_type=f32)
    hidden = jnp.tanh(
        jnp.sum(exchange_copies(partial_value.astype(bf16), "batch").astype(f32), axis=0)
    ).astype(bf16)
    routes = slot_routes(
        position_mapping_target, local_rows, heads_here, batch_index, head_index
    )
    routes, hidden = lax.optimization_barrier((routes, hidden))
    hidden = hidden.reshape(rows, MIX_MAPS, lagging_narrow_raising.shape[1])
    offsets = jnp.einsum(
        "nim,imd->ind", hidden, lagging_narrow_raising, preferred_element_type=f32
    )
    mixed = (
        x_float[None] + shifted[None] * (lagging_mixture_weights[1:, None, :] + offsets)
    ).astype(bf16)
    main_part = jnp.einsum(
        "inf,ifc->inc", mixed[:4], fourfold_linear_maps, preferred_element_type=f32
    )
    decay_part = jnp.dot(mixed[4], attenuation_narrow_lowering, preferred_element_type=f32)
    main_sum, decay_sum = exchange_sum(
        (
            main_part.astype(bf16)
            .reshape(4, batch_count, steps * local_rows, width)
            .transpose(1, 0, 2, 3),
            decay_part.astype(bf16).reshape(batch_count, steps * local_rows, -1),
        ),
        "batch",
    )

    moved_state = route_to_slots(
        stream_kept_tableaux.astype(bf16), routes, after=(main_sum, decay_sum)
    )

    def heads_of(value):
        return value.reshape(steps, local_rows, heads_here, SUBSPACE_EXTENT)

    main_sum = main_sum.reshape(4, steps, local_rows, width)
    recept = heads_of(widen(main_sum[0]))
    key_vec = heads_of(widen(main_sum[1]))
    valued = heads_of(widen(main_sum[2]))
    gate_act = jax.nn.silu(main_sum[3])
    low_rank = jnp.tanh(decay_sum.reshape(steps, local_rows, -1)).astype(bf16)
    decay_rate = heads_of(
        jnp.exp(
            -jnp.exp(
                attenuation_doublelog_anchor
                + jnp.dot(low_rank, attenuation_narrow_raising, preferred_element_type=f32)
            )
        )
    )
    rows_here = local_rows * heads_here

    def by_row(value):
        return value.reshape(steps, rows_here, SUBSPACE_EXTENT)

    projected = tuple(by_row(value) for value in (recept, key_vec, valued, decay_rate, gate_act))
    params = jnp.broadcast_to(
        jnp.stack([instant_premium, norming_multiplier, norming_intercept]).reshape(
            3, 1, heads_here, SUBSPACE_EXTENT
        ),
        (3, local_rows, heads_here, SUBSPACE_EXTENT),
    ).reshape(3, rows_here, SUBSPACE_EXTENT)
    mixed_rows, payload = run_recurrence(
        projected, params, stream_kept_tableaux.reshape(rows_here, -1)
    )
    moved_state, mixed_rows, payload = lax.optimization_barrier((moved_state, mixed_rows, payload))
    combined_response = mixed_rows.reshape(steps, local_rows, width)
    pieces = payload.shape[0]
    head_count = lax.axis_size("head")
    cluster_number = head_count // 4
    slots_dev = local_rows // cluster_number
    per_pair = slots_dev // batch_count
    quarter = heads_here // 4
    send_order = routes["send_order"]
    factors = jnp.take(
        payload.reshape(pieces, local_rows, heads_here, SUBSPACE_EXTENT),
        send_order,
        axis=1,
        mode="clip",
    ).reshape(pieces, batch_count, cluster_number * per_pair, heads_here, SUBSPACE_EXTENT)
    gathered, factors = gather_with_parts(
        combined_response, factors.transpose(1, 0, 2, 3, 4), "batch"
    )
    gathered = gathered.transpose(1, 0, 2, 3).reshape(steps, sessions, width)
    factors = factors.reshape(
        batch_count, pieces, cluster_number, per_pair, 4, quarter, SUBSPACE_EXTENT
    ).transpose(4, 2, 0, 1, 3, 5, 6)
    factors = factors.reshape(
        head_count, batch_count, pieces, per_pair, quarter, SUBSPACE_EXTENT
    )
    inverse = routes["inverse"]
    arranged = jnp.concatenate(
        [gathered[:STEPS_A], jnp.take(gathered[STEPS_A:], inverse, axis=1, mode="clip")], axis=0
    )
    partial_y = jnp.einsum(
        "tnf,fo->tno", arranged, outgoing_linear_map, preferred_element_type=f32
    ).astype(bf16)
    produced, factors = sum_with_parts(
        partial_y.reshape(steps, head_count, sessions // head_count, -1).transpose(1, 0, 2, 3),
        factors,
        "head",
    )
    produced = produced.astype(bf16)
    factors = factors.transpose(2, 1, 3, 0, 4, 5).reshape(
        pieces, batch_count * per_pair, head_count * quarter, SUBSPACE_EXTENT
    )
    placing = routes["placing"]
    moved_terms = jnp.take(factors, placing, axis=1, mode="clip").reshape(
        pieces, slots_dev * head_count * quarter, SUBSPACE_EXTENT
    )
    columns = head_count * quarter
    final_state = rebuild_state(
        moved_state.reshape(slots_dev * columns, -1), moved_terms, steps
    ).reshape(slots_dev, columns, -1)
    return (produced[:STEPS_A], produced[STEPS_A:], final_state)


def solution(mesh):
    in_specs = (
        P(None, "groups", "batch"),
        P("groups", "batch"),
        P(("groups", "batch"), "head", None),
        P("groups"),
        P(None, "batch"),
        P("batch", None),
        P(None, None, "batch"),
        P(None, "batch", "head"),
        P("batch", None),
        P(None, "head"),
        P("head"),
        P("head"),
        P("head"),
        P("head"),
        P("head", "batch"),
    )
    out_specs = (
        P(None, ("groups", "head"), "batch"),
        P(None, ("groups", "head"), "batch"),
        P(("groups", "batch", "head"), None, None),
    )
    return jax.shard_map(
        per_device, mesh=mesh, in_specs=in_specs, out_specs=out_specs, check_vma=False
    )
```

```python
import functools

import jax
import jax.numpy as jnp
from jax import lax
from jax.experimental import pallas as pl
from jax.experimental.pallas import tpu as pltpu
from jax.sharding import PartitionSpec as P

SUBSPACE_EXTENT = 64
STEPS_A = 2
MIX_MAPS = 5
NORMALIZER_GUARD = 0.00064


def index_of(values, count):
    positions = jnp.arange(values.shape[0], dtype=jnp.int32)
    wanted = jnp.arange(count, dtype=jnp.int32)
    return jnp.sum(jnp.where(values[None, :] == wanted[:, None], positions[None, :], 0), axis=1)


def route_to_slots(value, position_mapping_target, batch_index, head_index, after=None):
    batch_count = lax.axis_size("batch")
    head_count = lax.axis_size("head")
    local_rows, heads_here, width = value.shape
    cluster_number = head_count // 4
    slots_dev = local_rows // cluster_number
    per_pair = slots_dev // batch_count
    quarter = heads_here // 4
    own_map = lax.dynamic_slice_in_dim(
        position_mapping_target, batch_index * local_rows, local_rows
    )
    dest_key = own_map // slots_dev
    positions = jnp.arange(local_rows, dtype=jnp.int32)
    ahead = (dest_key[None, :] < dest_key[:, None]) | (
        (dest_key[None, :] == dest_key[:, None]) & (positions[None, :] < positions[:, None])
    )
    send_order = index_of(jnp.sum(ahead.astype(jnp.int32), axis=1), local_rows)
    dest = jnp.arange(batch_count * head_count, dtype=jnp.int32)
    dest_block = (dest // head_count) * cluster_number + dest % cluster_number
    quad = (dest % head_count) // cluster_number
    pair = jnp.arange(per_pair, dtype=jnp.int32)
    within = jnp.arange(quarter, dtype=jnp.int32)
    sent_sessions = jnp.take(
        send_order, dest_block[:, None] * per_pair + pair[None, :], mode="clip"
    )
    sent_rows = (
        sent_sessions[:, :, None] * heads_here
        + (quad * quarter)[:, None, None]
        + within[None, None, :]
    )
    packed = jnp.take(
        value.reshape(local_rows * heads_here, width), sent_rows.reshape(-1), axis=0, mode="clip"
    ).reshape(batch_count * head_count, per_pair * quarter, width)
    if after is not None:
        packed, after = lax.optimization_barrier((packed, after))
    arrived = lax.all_to_all(packed, ("batch", "head"), split_axis=0, concat_axis=0, tiled=True)
    target = batch_index * cluster_number + head_index % cluster_number
    sessions = position_mapping_target.shape[0]
    chosen = lax.dynamic_slice_in_dim(
        index_of(position_mapping_target, sessions), target * slots_dev, slots_dev
    )
    every = jnp.arange(sessions, dtype=jnp.int32)
    coming = (position_mapping_target // slots_dev) == target
    placing = jnp.sum(
        ((every[None, :] < chosen[:, None]) & coming[None, :]).astype(jnp.int32), axis=1
    )
    source_head = jnp.arange(head_count, dtype=jnp.int32)
    kept_rows = (
        (
            (placing[:, None, None] // per_pair) * head_count + source_head[None, :, None]
        )
        * per_pair
        + placing[:, None, None] % per_pair
    ) * quarter + within[None, None, :]
    return jnp.take(
        arrived.reshape(-1, width), kept_rows.reshape(-1), axis=0, mode="clip"
    ).reshape(slots_dev, head_count * quarter, width)

def exchange_sum(pieces, axis_name):
    count = lax.axis_size(axis_name)
    index = lax.axis_index(axis_name)

    def own(shift):
        return jax.tree.map(
            lambda value: lax.dynamic_index_in_dim(value, (index + shift) % count, keepdims=False),
            pieces,
        )

    total = jax.tree.map(lambda value: value.astype(jnp.float32), own(0))
    for shift in range(1, count):
        arrived = lax.ppermute(
            own(shift), axis_name, [(i, (i + shift) % count) for i in range(count)]
        )
        total = jax.tree.map(lambda acc, value: acc + value.astype(jnp.float32), total, arrived)
    return total

def exchange_copies(value, axis_name):
    count = lax.axis_size(axis_name)
    index = lax.axis_index(axis_name)
    received = [value]
    for shift in range(1, count):
        received.append(
            lax.ppermute(value, axis_name, [(i, (i + shift) % count) for i in range(count)])
        )
    shifts = (index - jnp.arange(count, dtype=jnp.int32)) % count
    return jnp.take(jnp.stack(received), shifts, axis=0, mode="clip")

def by_source(received, index, count):
    shifts = (index - jnp.arange(count, dtype=jnp.int32)) % count
    return jnp.take(jnp.stack(received), shifts, axis=0, mode="clip")


def gather_with_parts(value, parts, axis_name):
    count = lax.axis_size(axis_name)
    index = lax.axis_index(axis_name)
    copies = [value]
    moved = [lax.dynamic_index_in_dim(parts, index, keepdims=False)]
    for shift in range(1, count):
        sent = lax.dynamic_index_in_dim(parts, (index + shift) % count, keepdims=False)
        copy, part = lax.ppermute(
            (value, sent), axis_name, [(i, (i + shift) % count) for i in range(count)]
        )
        copies.append(copy)
        moved.append(part)
    return by_source(copies, index, count), by_source(moved, index, count)


def sum_with_parts(pieces, parts, axis_name):
    count = lax.axis_size(axis_name)
    index = lax.axis_index(axis_name)
    total = lax.dynamic_index_in_dim(pieces, index, keepdims=False).astype(jnp.float32)
    moved = [lax.dynamic_index_in_dim(parts, index, keepdims=False)]
    for shift in range(1, count):
        target = (index + shift) % count
        piece, part = lax.ppermute(
            (
                lax.dynamic_index_in_dim(pieces, target, keepdims=False),
                lax.dynamic_index_in_dim(parts, target, keepdims=False),
            ),
            axis_name,
            [(i, (i + shift) % count) for i in range(count)],
        )
        total = total + piece.astype(jnp.float32)
        moved.append(part)
    return total, by_source(moved, index, count)


def widen(value):
    return value.astype(jnp.bfloat16).astype(jnp.float32)


def fill_tables(spread_ref, tile_ref=None):
    extent = SUBSPACE_EXTENT

    @pl.when(pl.program_id(0) == 0)
    def _():
        lane = lax.broadcasted_iota(jnp.int32, spread_ref.shape, 1)
        row = lax.broadcasted_iota(jnp.int32, spread_ref.shape, 0)
        spread_ref[...] = (lane // extent == row).astype(spread_ref.dtype)
        if tile_ref is not None:
            tile_ref[...] = (lane % extent == row).astype(tile_ref.dtype)


def recurrence_kernel(
    steps,
    recept_ref,
    key_ref,
    value_ref,
    decay_ref,
    gate_ref,
    params_ref,
    state_ref,
    mixed_ref,
    payload_ref,
    spread_ref,
):
    extent = SUBSPACE_EXTENT
    fill_tables(spread_ref)
    spread = spread_ref[...]
    state = state_ref[...]
    premium = params_ref[0]
    gain = params_ref[1]
    bias = params_ref[2]
    recept = [recept_ref[t] for t in range(steps)]
    key_vec = [key_ref[t] for t in range(steps)]
    valued = [value_ref[t] for t in range(steps)]
    decay_rate = [decay_ref[t] for t in range(steps)]
    flat = state.shape[-1]
    prefix = jnp.ones_like(recept[0])
    for t in range(steps):
        query = recept[t] * prefix
        high = query.astype(jnp.bfloat16)
        rest = query - high.astype(jnp.float32)
        middle = rest.astype(jnp.bfloat16)
        low = (rest - middle.astype(jnp.float32)).astype(jnp.bfloat16)
        spread_query = (
            jnp.dot(high, spread, preferred_element_type=jnp.float32)
            + jnp.dot(middle, spread, preferred_element_type=jnp.float32)
            + jnp.dot(low, spread, preferred_element_type=jnp.float32)
        )
        weighted = spread_query * state
        folded = weighted[:, 0:128]
        for c in range(1, flat // 128):
            folded = folded + weighted[:, 128 * c : 128 * (c + 1)]
        from_state = folded[:, :extent] + folded[:, extent:]
        bonus_term = jnp.sum(recept[t] * premium * key_vec[t], axis=-1, keepdims=True)
        total = bonus_term * valued[t] + from_state
        for s in range(t):
            factor = key_vec[s]
            for u in range(s + 1, t):
                factor = factor * decay_rate[u]
            total = total + jnp.sum(recept[t] * factor, axis=-1, keepdims=True) * valued[s]
        average = jnp.mean(total, axis=-1, keepdims=True)
        demeaned = total - average
        spread_squared = jnp.mean(demeaned * demeaned, axis=-1, keepdims=True)
        standardized = demeaned * lax.rsqrt(spread_squared + NORMALIZER_GUARD) * gain + bias
        mixed_ref[t] = (standardized * gate_ref[t]).astype(mixed_ref.dtype)
        prefix = prefix * decay_rate[t]
    payload_ref[0] = prefix.astype(payload_ref.dtype)
    for s in range(steps):
        factor = key_vec[s]
        for u in range(s + 1, steps):
            factor = factor * decay_rate[u]
        payload_ref[1 + s] = factor.astype(payload_ref.dtype)
        payload_ref[1 + steps + s] = valued[s].astype(payload_ref.dtype)


def row_block(rows):
    return 128 if rows % 128 == 0 else rows


def run_recurrence(projected, params, state):
    pieces = len(projected)
    steps, rows, extent = projected[0].shape
    flat = state.shape[-1]
    block = row_block(rows)
    return pl.pallas_call(
        functools.partial(recurrence_kernel, steps),
        grid=(rows // block,),
        in_specs=[
            *[pl.BlockSpec((steps, block, extent), lambda n: (0, n, 0))] * pieces,
            pl.BlockSpec((3, block, extent), lambda n: (0, n, 0)),
            pl.BlockSpec((block, flat), lambda n: (n, 0)),
        ],
        out_specs=[
            pl.BlockSpec((steps, block, extent), lambda n: (0, n, 0)),
            pl.BlockSpec((1 + 2 * steps, block, extent), lambda n: (0, n, 0)),
        ],
        out_shape=[
            jax.ShapeDtypeStruct((steps, rows, extent), jnp.bfloat16),
            jax.ShapeDtypeStruct((1 + 2 * steps, rows, extent), jnp.bfloat16),
        ],
        scratch_shapes=[pltpu.VMEM((extent, flat), jnp.bfloat16)],
        cost_estimate=pl.CostEstimate(
            flops=2 * rows * extent * flat * 3 * steps,
            transcendentals=steps * rows,
            bytes_accessed=rows * (flat * 4 + extent * (pieces * steps * 4 + 3 * 4 + steps * 2 + (1 + 2 * steps) * 2)),
        ),
    )(*projected, params, state)


def rebuild_kernel(steps, state_ref, terms_ref, out_ref, spread_ref, tile_ref):
    fill_tables(spread_ref, tile_ref)
    spread = spread_ref[...]
    tile = tile_ref[...]
    total = jnp.dot(terms_ref[0], spread, preferred_element_type=jnp.float32) * state_ref[...].astype(
        jnp.float32
    )
    for s in range(steps):
        total = total + jnp.dot(
            terms_ref[1 + s], spread, preferred_element_type=jnp.float32
        ) * jnp.dot(terms_ref[1 + steps + s], tile, preferred_element_type=jnp.float32)
    out_ref[...] = total


def rebuild_state(moved_state, moved_terms, steps):
    rows, flat = moved_state.shape
    pieces = moved_terms.shape[0]
    extent = SUBSPACE_EXTENT
    block = row_block(rows)
    return pl.pallas_call(
        functools.partial(rebuild_kernel, steps),
        grid=(rows // block,),
        in_specs=[
            pl.BlockSpec((block, flat), lambda n: (n, 0)),
            pl.BlockSpec((pieces, block, extent), lambda n: (0, n, 0)),
        ],
        out_specs=pl.BlockSpec((block, flat), lambda n: (n, 0)),
        out_shape=jax.ShapeDtypeStruct((rows, flat), jnp.float32),
        scratch_shapes=[
            pltpu.VMEM((extent, flat), jnp.bfloat16),
            pltpu.VMEM((extent, flat), jnp.bfloat16),
        ],
        cost_estimate=pl.CostEstimate(
            flops=2 * rows * extent * flat * (1 + 2 * steps),
            transcendentals=0,
            bytes_accessed=rows * (flat * 6 + pieces * extent * 2),
        ),
    )(moved_state, moved_terms)


def per_device(
    tier_feed_tensor,
    preceding_feed_each_stream,
    stream_kept_tableaux,
    position_mapping_target,
    lagging_mixture_weights,
    lagging_narrow_lowering,
    lagging_narrow_raising,
    fourfold_linear_maps,
    attenuation_narrow_lowering,
    attenuation_narrow_raising,
    attenuation_doublelog_anchor,
    instant_premium,
    norming_multiplier,
    norming_intercept,
    outgoing_linear_map,
):
    batch_count = lax.axis_size("batch")
    batch_index = lax.axis_index("batch")
    head_index = lax.axis_index("head")
    steps, sessions, feats = tier_feed_tensor.shape
    local_rows = sessions // batch_count
    heads_here = stream_kept_tableaux.shape[1]
    width = heads_here * SUBSPACE_EXTENT
    f32 = jnp.float32
    bf16 = jnp.bfloat16


    previous = jnp.concatenate([preceding_feed_each_stream[None], tier_feed_tensor[:-1]], axis=0)

    def by_block(value):
        return value.reshape(steps, batch_count, local_rows, feats).transpose(1, 0, 2, 3).reshape(
            batch_count * steps * local_rows, feats
        )

    x_float = by_block(tier_feed_tensor).astype(f32)
    shifted = by_block(previous).astype(f32) - x_float
    rows = x_float.shape[0]
    base_mix = (x_float + shifted * lagging_mixture_weights[0]).astype(bf16)
    partial_value = jnp.dot(base_mix, lagging_narrow_lowering, preferred_element_type=f32)
    hidden = jnp.tanh(
        jnp.sum(exchange_copies(partial_value.astype(bf16), "batch").astype(f32), axis=0)
    ).astype(bf16)
    hidden = hidden.reshape(rows, MIX_MAPS, lagging_narrow_raising.shape[1])
    offsets = jnp.einsum(
        "nim,imd->ind", hidden, lagging_narrow_raising, preferred_element_type=f32
    )
    mixed = (
        x_float[None] + shifted[None] * (lagging_mixture_weights[1:, None, :] + offsets)
    ).astype(bf16)
    main_part = jnp.einsum(
        "inf,ifc->inc", mixed[:4], fourfold_linear_maps, preferred_element_type=f32
    )
    decay_part = jnp.dot(mixed[4], attenuation_narrow_lowering, preferred_element_type=f32)
    main_sum, decay_sum = exchange_sum(
        (
            main_part.astype(bf16)
            .reshape(4, batch_count, steps * local_rows, width)
            .transpose(1, 0, 2, 3),
            decay_part.astype(bf16).reshape(batch_count, steps * local_rows, -1),
        ),
        "batch",
    )

    moved_state = route_to_slots(
        stream_kept_tableaux.astype(bf16),
        position_mapping_target,
        batch_index,
        head_index,
        after=(main_sum, decay_sum),
    )

    def heads_of(value):
        return value.reshape(steps, local_rows, heads_here, SUBSPACE_EXTENT)

    main_sum = main_sum.reshape(4, steps, local_rows, width)
    recept = heads_of(widen(main_sum[0]))
    key_vec = heads_of(widen(main_sum[1]))
    valued = heads_of(widen(main_sum[2]))
    gate_act = jax.nn.silu(main_sum[3])
    low_rank = jnp.tanh(decay_sum.reshape(steps, local_rows, -1)).astype(bf16)
    decay_rate = heads_of(
        jnp.exp(
            -jnp.exp(
                attenuation_doublelog_anchor
                + jnp.dot(low_rank, attenuation_narrow_raising, preferred_element_type=f32)
            )
        )
    )
    rows_here = local_rows * heads_here

    def by_row(value):
        return value.reshape(steps, rows_here, SUBSPACE_EXTENT)

    projected = tuple(by_row(value) for value in (recept, key_vec, valued, decay_rate, gate_act))
    params = jnp.broadcast_to(
        jnp.stack([instant_premium, norming_multiplier, norming_intercept]).reshape(
            3, 1, heads_here, SUBSPACE_EXTENT
        ),
        (3, local_rows, heads_here, SUBSPACE_EXTENT),
    ).reshape(3, rows_here, SUBSPACE_EXTENT)
    mixed_rows, payload = run_recurrence(
        projected, params, stream_kept_tableaux.reshape(rows_here, -1)
    )
    moved_state, mixed_rows, payload = lax.optimization_barrier((moved_state, mixed_rows, payload))
    combined_response = mixed_rows.reshape(steps, local_rows, width)
    pieces = payload.shape[0]
    head_count = lax.axis_size("head")
    cluster_number = head_count // 4
    slots_dev = local_rows // cluster_number
    per_pair = slots_dev // batch_count
    quarter = heads_here // 4
    own_map = lax.dynamic_slice_in_dim(
        position_mapping_target, batch_index * local_rows, local_rows
    )
    dest_key = own_map // slots_dev
    positions = jnp.arange(local_rows, dtype=jnp.int32)
    ahead = (dest_key[None, :] < dest_key[:, None]) | (
        (dest_key[None, :] == dest_key[:, None]) & (positions[None, :] < positions[:, None])
    )
    send_order = index_of(jnp.sum(ahead.astype(jnp.int32), axis=1), local_rows)
    factors = jnp.take(
        payload.reshape(pieces, local_rows, heads_here, SUBSPACE_EXTENT),
        send_order,
        axis=1,
        mode="clip",
    ).reshape(pieces, batch_count, cluster_number * per_pair, heads_here, SUBSPACE_EXTENT)
    gathered, factors = gather_with_parts(
        combined_response, factors.transpose(1, 0, 2, 3, 4), "batch"
    )
    gathered = gathered.transpose(1, 0, 2, 3).reshape(steps, sessions, width)
    factors = factors.reshape(
        batch_count, pieces, cluster_number, per_pair, 4, quarter, SUBSPACE_EXTENT
    ).transpose(4, 2, 0, 1, 3, 5, 6)
    factors = factors.reshape(
        head_count, batch_count, pieces, per_pair, quarter, SUBSPACE_EXTENT
    )
    inverse = index_of(position_mapping_target, sessions)
    arranged = jnp.concatenate(
        [gathered[:STEPS_A], jnp.take(gathered[STEPS_A:], inverse, axis=1, mode="clip")], axis=0
    )
    partial_y = jnp.einsum(
        "tnf,fo->tno", arranged, outgoing_linear_map, preferred_element_type=f32
    ).astype(bf16)
    produced, factors = sum_with_parts(
        partial_y.reshape(steps, head_count, sessions // head_count, -1).transpose(1, 0, 2, 3),
        factors,
        "head",
    )
    produced = produced.astype(bf16)
    factors = factors.transpose(2, 1, 3, 0, 4, 5).reshape(
        pieces, batch_count * per_pair, head_count * quarter, SUBSPACE_EXTENT
    )
    target = batch_index * cluster_number + head_index % cluster_number
    chosen = lax.dynamic_slice_in_dim(inverse, target * slots_dev, slots_dev)
    every = jnp.arange(sessions, dtype=jnp.int32)
    coming = (position_mapping_target // slots_dev) == target
    placing = jnp.sum(
        ((every[None, :] < chosen[:, None]) & coming[None, :]).astype(jnp.int32), axis=1
    )
    moved_terms = jnp.take(factors, placing, axis=1, mode="clip").reshape(
        pieces, slots_dev * head_count * quarter, SUBSPACE_EXTENT
    )
    columns = head_count * quarter
    final_state = rebuild_state(
        moved_state.reshape(slots_dev * columns, -1), moved_terms, steps
    ).reshape(slots_dev, columns, -1)
    return (produced[:STEPS_A], produced[STEPS_A:], final_state)


def solution(mesh):
    in_specs = (
        P(None, "groups", "batch"),
        P("groups", "batch"),
        P(("groups", "batch"), "head", None),
        P("groups"),
        P(None, "batch"),
        P("batch", None),
        P(None, None, "batch"),
        P(None, "batch", "head"),
        P("batch", None),
        P(None, "head"),
        P("head"),
        P("head"),
        P("head"),
        P("head"),
        P("head", "batch"),
    )
    out_specs = (
        P(None, ("groups", "head"), "batch"),
        P(None, ("groups", "head"), "batch"),
        P(("groups", "batch", "head"), None, None),
    )
    return jax.shard_map(
        per_device, mesh=mesh, in_specs=in_specs, out_specs=out_specs, check_vma=False
    )
```

```python
import functools

import jax
import jax.numpy as jnp
from jax import lax
from jax.experimental import pallas as pl
from jax.experimental.pallas import tpu as pltpu
from jax.sharding import PartitionSpec as P

SUBSPACE_EXTENT = 64
STEPS_A = 2
MIX_MAPS = 5
NORMALIZER_GUARD = 0.00064


def index_of(values, count):
    positions = jnp.arange(values.shape[0], dtype=jnp.int32)
    wanted = jnp.arange(count, dtype=jnp.int32)
    return jnp.sum(jnp.where(values[None, :] == wanted[:, None], positions[None, :], 0), axis=1)


def route_to_slots(value, position_mapping_target, batch_index, head_index, after=None):
    batch_count = lax.axis_size("batch")
    head_count = lax.axis_size("head")
    local_rows, heads_here, width = value.shape
    cluster_number = head_count // 4
    slots_dev = local_rows // cluster_number
    per_pair = slots_dev // batch_count
    quarter = heads_here // 4
    own_map = lax.dynamic_slice_in_dim(
        position_mapping_target, batch_index * local_rows, local_rows
    )
    dest_key = own_map // slots_dev
    positions = jnp.arange(local_rows, dtype=jnp.int32)
    ahead = (dest_key[None, :] < dest_key[:, None]) | (
        (dest_key[None, :] == dest_key[:, None]) & (positions[None, :] < positions[:, None])
    )
    send_order = index_of(jnp.sum(ahead.astype(jnp.int32), axis=1), local_rows)
    dest = jnp.arange(batch_count * head_count, dtype=jnp.int32)
    dest_block = (dest // head_count) * cluster_number + dest % cluster_number
    quad = (dest % head_count) // cluster_number
    pair = jnp.arange(per_pair, dtype=jnp.int32)
    within = jnp.arange(quarter, dtype=jnp.int32)
    sent_sessions = jnp.take(
        send_order, dest_block[:, None] * per_pair + pair[None, :], mode="clip"
    )
    sent_rows = (
        sent_sessions[:, :, None] * heads_here
        + (quad * quarter)[:, None, None]
        + within[None, None, :]
    )
    packed = jnp.take(
        value.reshape(local_rows * heads_here, width), sent_rows.reshape(-1), axis=0, mode="clip"
    ).reshape(batch_count * head_count, per_pair * quarter, width)
    if after is not None:
        packed, after = lax.optimization_barrier((packed, after))
    arrived = lax.all_to_all(packed, ("batch", "head"), split_axis=0, concat_axis=0, tiled=True)
    target = batch_index * cluster_number + head_index % cluster_number
    sessions = position_mapping_target.shape[0]
    chosen = lax.dynamic_slice_in_dim(
        index_of(position_mapping_target, sessions), target * slots_dev, slots_dev
    )
    every = jnp.arange(sessions, dtype=jnp.int32)
    coming = (position_mapping_target // slots_dev) == target
    placing = jnp.sum(
        ((every[None, :] < chosen[:, None]) & coming[None, :]).astype(jnp.int32), axis=1
    )
    source_head = jnp.arange(head_count, dtype=jnp.int32)
    kept_rows = (
        (
            (placing[:, None, None] // per_pair) * head_count + source_head[None, :, None]
        )
        * per_pair
        + placing[:, None, None] % per_pair
    ) * quarter + within[None, None, :]
    return jnp.take(
        arrived.reshape(-1, width), kept_rows.reshape(-1), axis=0, mode="clip"
    ).reshape(slots_dev, head_count * quarter, width)

def exchange_sum(pieces, axis_name):
    count = lax.axis_size(axis_name)
    index = lax.axis_index(axis_name)

    def own(shift):
        return jax.tree.map(
            lambda value: lax.dynamic_index_in_dim(value, (index + shift) % count, keepdims=False),
            pieces,
        )

    total = jax.tree.map(lambda value: value.astype(jnp.float32), own(0))
    for shift in range(1, count):
        arrived = lax.ppermute(
            own(shift), axis_name, [(i, (i + shift) % count) for i in range(count)]
        )
        total = jax.tree.map(lambda acc, value: acc + value.astype(jnp.float32), total, arrived)
    return total

def exchange_copies(value, axis_name):
    count = lax.axis_size(axis_name)
    index = lax.axis_index(axis_name)
    received = [value]
    for shift in range(1, count):
        received.append(
            lax.ppermute(value, axis_name, [(i, (i + shift) % count) for i in range(count)])
        )
    shifts = (index - jnp.arange(count, dtype=jnp.int32)) % count
    return jnp.take(jnp.stack(received), shifts, axis=0, mode="clip")

def by_source(received, index, count):
    shifts = (index - jnp.arange(count, dtype=jnp.int32)) % count
    return jnp.take(jnp.stack(received), shifts, axis=0, mode="clip")


def gather_with_parts(value, parts, axis_name):
    count = lax.axis_size(axis_name)
    index = lax.axis_index(axis_name)
    copies = [value]
    moved = [lax.dynamic_index_in_dim(parts, index, keepdims=False)]
    for shift in range(1, count):
        sent = lax.dynamic_index_in_dim(parts, (index + shift) % count, keepdims=False)
        copy, part = lax.ppermute(
            (value, sent), axis_name, [(i, (i + shift) % count) for i in range(count)]
        )
        copies.append(copy)
        moved.append(part)
    return by_source(copies, index, count), by_source(moved, index, count)


def sum_with_parts(pieces, parts, axis_name):
    count = lax.axis_size(axis_name)
    index = lax.axis_index(axis_name)
    total = lax.dynamic_index_in_dim(pieces, index, keepdims=False).astype(jnp.float32)
    moved = [lax.dynamic_index_in_dim(parts, index, keepdims=False)]
    for shift in range(1, count):
        target = (index + shift) % count
        piece, part = lax.ppermute(
            (
                lax.dynamic_index_in_dim(pieces, target, keepdims=False),
                lax.dynamic_index_in_dim(parts, target, keepdims=False),
            ),
            axis_name,
            [(i, (i + shift) % count) for i in range(count)],
        )
        total = total + piece.astype(jnp.float32)
        moved.append(part)
    return total, by_source(moved, index, count)


def widen(value):
    return value.astype(jnp.bfloat16).astype(jnp.float32)


def fill_tables(spread_ref, tile_ref=None):
    extent = SUBSPACE_EXTENT

    @pl.when(pl.program_id(0) == 0)
    def _():
        lane = lax.broadcasted_iota(jnp.int32, spread_ref.shape, 1)
        row = lax.broadcasted_iota(jnp.int32, spread_ref.shape, 0)
        spread_ref[...] = (lane // extent == row).astype(spread_ref.dtype)
        if tile_ref is not None:
            tile_ref[...] = (lane % extent == row).astype(tile_ref.dtype)


def recurrence_kernel(
    steps,
    recept_ref,
    key_ref,
    value_ref,
    decay_ref,
    gate_ref,
    params_ref,
    state_ref,
    mixed_ref,
    payload_ref,
    spread_ref,
):
    extent = SUBSPACE_EXTENT
    fill_tables(spread_ref)
    spread = spread_ref[...]
    state = state_ref[...]
    premium = params_ref[0]
    gain = params_ref[1]
    bias = params_ref[2]
    recept = [recept_ref[t] for t in range(steps)]
    key_vec = [key_ref[t] for t in range(steps)]
    valued = [value_ref[t] for t in range(steps)]
    decay_rate = [decay_ref[t] for t in range(steps)]
    flat = state.shape[-1]
    prefix = jnp.ones_like(recept[0])
    for t in range(steps):
        query = recept[t] * prefix
        high = query.astype(jnp.bfloat16)
        rest = query - high.astype(jnp.float32)
        middle = rest.astype(jnp.bfloat16)
        low = (rest - middle.astype(jnp.float32)).astype(jnp.bfloat16)
        spread_query = (
            jnp.dot(high, spread, preferred_element_type=jnp.float32)
            + jnp.dot(middle, spread, preferred_element_type=jnp.float32)
            + jnp.dot(low, spread, preferred_element_type=jnp.float32)
        )
        weighted = spread_query * state
        folded = weighted[:, 0:128]
        for c in range(1, flat // 128):
            folded = folded + weighted[:, 128 * c : 128 * (c + 1)]
        from_state = folded[:, :extent] + folded[:, extent:]
        bonus_term = jnp.sum(recept[t] * premium * key_vec[t], axis=-1, keepdims=True)
        total = bonus_term * valued[t] + from_state
        for s in range(t):
            factor = key_vec[s]
            for u in range(s + 1, t):
                factor = factor * decay_rate[u]
            total = total + jnp.sum(recept[t] * factor, axis=-1, keepdims=True) * valued[s]
        average = jnp.mean(total, axis=-1, keepdims=True)
        demeaned = total - average
        spread_squared = jnp.mean(demeaned * demeaned, axis=-1, keepdims=True)
        standardized = demeaned * lax.rsqrt(spread_squared + NORMALIZER_GUARD) * gain + bias
        mixed_ref[t] = (standardized * gate_ref[t]).astype(mixed_ref.dtype)
        prefix = prefix * decay_rate[t]
    payload_ref[0] = prefix.astype(payload_ref.dtype)
    for s in range(steps):
        factor = key_vec[s]
        for u in range(s + 1, steps):
            factor = factor * decay_rate[u]
        payload_ref[1 + s] = factor.astype(payload_ref.dtype)
        payload_ref[1 + steps + s] = valued[s].astype(payload_ref.dtype)


def row_block(rows):
    return 64 if rows % 64 == 0 else rows


def run_recurrence(projected, params, state):
    pieces = len(projected)
    steps, rows, extent = projected[0].shape
    flat = state.shape[-1]
    block = row_block(rows)
    return pl.pallas_call(
        functools.partial(recurrence_kernel, steps),
        grid=(rows // block,),
        in_specs=[
            *[pl.BlockSpec((steps, block, extent), lambda n: (0, n, 0))] * pieces,
            pl.BlockSpec((3, block, extent), lambda n: (0, 0, 0)),
            pl.BlockSpec((block, flat), lambda n: (n, 0)),
        ],
        out_specs=[
            pl.BlockSpec((steps, block, extent), lambda n: (0, n, 0)),
            pl.BlockSpec((1 + 2 * steps, block, extent), lambda n: (0, n, 0)),
        ],
        out_shape=[
            jax.ShapeDtypeStruct((steps, rows, extent), jnp.bfloat16),
            jax.ShapeDtypeStruct((1 + 2 * steps, rows, extent), jnp.bfloat16),
        ],
        scratch_shapes=[pltpu.VMEM((extent, flat), jnp.bfloat16)],
        cost_estimate=pl.CostEstimate(
            flops=2 * rows * extent * flat * 3 * steps,
            transcendentals=steps * rows,
            bytes_accessed=rows * (flat * 4 + extent * (pieces * steps * 4 + 3 * 4 + steps * 2 + (1 + 2 * steps) * 2)),
        ),
    )(*projected, params, state)


def rebuild_kernel(steps, state_ref, terms_ref, out_ref, spread_ref, tile_ref):
    fill_tables(spread_ref, tile_ref)
    spread = spread_ref[...]
    tile = tile_ref[...]
    total = jnp.dot(terms_ref[0], spread, preferred_element_type=jnp.float32) * state_ref[...].astype(
        jnp.float32
    )
    for s in range(steps):
        total = total + jnp.dot(
            terms_ref[1 + s], spread, preferred_element_type=jnp.float32
        ) * jnp.dot(terms_ref[1 + steps + s], tile, preferred_element_type=jnp.float32)
    out_ref[...] = total


def rebuild_state(moved_state, moved_terms, steps):
    rows, flat = moved_state.shape
    pieces = moved_terms.shape[0]
    extent = SUBSPACE_EXTENT
    block = row_block(rows)
    return pl.pallas_call(
        functools.partial(rebuild_kernel, steps),
        grid=(rows // block,),
        in_specs=[
            pl.BlockSpec((block, flat), lambda n: (n, 0)),
            pl.BlockSpec((pieces, block, extent), lambda n: (0, n, 0)),
        ],
        out_specs=pl.BlockSpec((block, flat), lambda n: (n, 0)),
        out_shape=jax.ShapeDtypeStruct((rows, flat), jnp.float32),
        scratch_shapes=[
            pltpu.VMEM((extent, flat), jnp.bfloat16),
            pltpu.VMEM((extent, flat), jnp.bfloat16),
        ],
        cost_estimate=pl.CostEstimate(
            flops=2 * rows * extent * flat * (1 + 2 * steps),
            transcendentals=0,
            bytes_accessed=rows * (flat * 6 + pieces * extent * 2),
        ),
    )(moved_state, moved_terms)


def per_device(
    tier_feed_tensor,
    preceding_feed_each_stream,
    stream_kept_tableaux,
    position_mapping_target,
    lagging_mixture_weights,
    lagging_narrow_lowering,
    lagging_narrow_raising,
    fourfold_linear_maps,
    attenuation_narrow_lowering,
    attenuation_narrow_raising,
    attenuation_doublelog_anchor,
    instant_premium,
    norming_multiplier,
    norming_intercept,
    outgoing_linear_map,
):
    batch_count = lax.axis_size("batch")
    batch_index = lax.axis_index("batch")
    head_index = lax.axis_index("head")
    steps, sessions, feats = tier_feed_tensor.shape
    local_rows = sessions // batch_count
    heads_here = stream_kept_tableaux.shape[1]
    width = heads_here * SUBSPACE_EXTENT
    f32 = jnp.float32
    bf16 = jnp.bfloat16


    previous = jnp.concatenate([preceding_feed_each_stream[None], tier_feed_tensor[:-1]], axis=0)

    def by_block(value):
        return value.reshape(steps, batch_count, local_rows, feats).transpose(1, 0, 2, 3).reshape(
            batch_count * steps * local_rows, feats
        )

    x_float = by_block(tier_feed_tensor).astype(f32)
    shifted = by_block(previous).astype(f32) - x_float
    rows = x_float.shape[0]
    base_mix = (x_float + shifted * lagging_mixture_weights[0]).astype(bf16)
    partial_value = jnp.dot(base_mix, lagging_narrow_lowering, preferred_element_type=f32)
    hidden = jnp.tanh(
        jnp.sum(exchange_copies(partial_value.astype(bf16), "batch").astype(f32), axis=0)
    ).astype(bf16)
    hidden = hidden.reshape(rows, MIX_MAPS, lagging_narrow_raising.shape[1])
    offsets = jnp.einsum(
        "nim,imd->ind", hidden, lagging_narrow_raising, preferred_element_type=f32
    )
    mixed = (
        x_float[None] + shifted[None] * (lagging_mixture_weights[1:, None, :] + offsets)
    ).astype(bf16)
    main_part = jnp.einsum(
        "inf,ifc->inc", mixed[:4], fourfold_linear_maps, preferred_element_type=f32
    )
    decay_part = jnp.dot(mixed[4], attenuation_narrow_lowering, preferred_element_type=f32)
    main_sum, decay_sum = exchange_sum(
        (
            main_part.astype(bf16)
            .reshape(4, batch_count, steps * local_rows, width)
            .transpose(1, 0, 2, 3),
            decay_part.astype(bf16).reshape(batch_count, steps * local_rows, -1),
        ),
        "batch",
    )

    moved_state = route_to_slots(
        stream_kept_tableaux.astype(bf16),
        position_mapping_target,
        batch_index,
        head_index,
        after=(main_sum, decay_sum),
    )

    def heads_of(value):
        return value.reshape(steps, local_rows, heads_here, SUBSPACE_EXTENT)

    main_sum = main_sum.reshape(4, steps, local_rows, width)
    recept = heads_of(widen(main_sum[0]))
    key_vec = heads_of(widen(main_sum[1]))
    valued = heads_of(widen(main_sum[2]))
    gate_act = jax.nn.silu(main_sum[3])
    low_rank = jnp.tanh(decay_sum.reshape(steps, local_rows, -1)).astype(bf16)
    decay_rate = heads_of(
        jnp.exp(
            -jnp.exp(
                attenuation_doublelog_anchor
                + jnp.dot(low_rank, attenuation_narrow_raising, preferred_element_type=f32)
            )
        )
    )
    rows_here = local_rows * heads_here

    def by_row(value):
        return value.reshape(steps, rows_here, SUBSPACE_EXTENT)

    projected = tuple(by_row(value) for value in (recept, key_vec, valued, decay_rate, gate_act))
    params = jnp.tile(
        jnp.stack([instant_premium, norming_multiplier, norming_intercept]).reshape(
            3, heads_here, SUBSPACE_EXTENT
        ),
        (1, row_block(rows_here) // heads_here, 1),
    )
    mixed_rows, payload = run_recurrence(
        projected, params, stream_kept_tableaux.reshape(rows_here, -1)
    )
    moved_state, mixed_rows, payload = lax.optimization_barrier((moved_state, mixed_rows, payload))
    combined_response = mixed_rows.reshape(steps, local_rows, width)
    pieces = payload.shape[0]
    head_count = lax.axis_size("head")
    cluster_number = head_count // 4
    slots_dev = local_rows // cluster_number
    per_pair = slots_dev // batch_count
    quarter = heads_here // 4
    own_map = lax.dynamic_slice_in_dim(
        position_mapping_target, batch_index * local_rows, local_rows
    )
    dest_key = own_map // slots_dev
    positions = jnp.arange(local_rows, dtype=jnp.int32)
    ahead = (dest_key[None, :] < dest_key[:, None]) | (
        (dest_key[None, :] == dest_key[:, None]) & (positions[None, :] < positions[:, None])
    )
    send_order = index_of(jnp.sum(ahead.astype(jnp.int32), axis=1), local_rows)
    factors = jnp.take(
        payload.reshape(pieces, local_rows, heads_here, SUBSPACE_EXTENT),
        send_order,
        axis=1,
        mode="clip",
    ).reshape(pieces, batch_count, cluster_number * per_pair, heads_here, SUBSPACE_EXTENT)
    gathered, factors = gather_with_parts(
        combined_response, factors.transpose(1, 0, 2, 3, 4), "batch"
    )
    gathered = gathered.transpose(1, 0, 2, 3).reshape(steps, sessions, width)
    factors = factors.reshape(
        batch_count, pieces, cluster_number, per_pair, 4, quarter, SUBSPACE_EXTENT
    ).transpose(4, 2, 0, 1, 3, 5, 6)
    factors = factors.reshape(
        head_count, batch_count, pieces, per_pair, quarter, SUBSPACE_EXTENT
    )
    inverse = index_of(position_mapping_target, sessions)
    arranged = jnp.concatenate(
        [gathered[:STEPS_A], jnp.take(gathered[STEPS_A:], inverse, axis=1, mode="clip")], axis=0
    )
    partial_y = jnp.einsum(
        "tnf,fo->tno", arranged, outgoing_linear_map, preferred_element_type=f32
    ).astype(bf16)
    produced, factors = sum_with_parts(
        partial_y.reshape(steps, head_count, sessions // head_count, -1).transpose(1, 0, 2, 3),
        factors,
        "head",
    )
    produced = produced.astype(bf16)
    factors = factors.transpose(2, 1, 3, 0, 4, 5).reshape(
        pieces, batch_count * per_pair, head_count * quarter, SUBSPACE_EXTENT
    )
    target = batch_index * cluster_number + head_index % cluster_number
    chosen = lax.dynamic_slice_in_dim(inverse, target * slots_dev, slots_dev)
    every = jnp.arange(sessions, dtype=jnp.int32)
    coming = (position_mapping_target // slots_dev) == target
    placing = jnp.sum(
        ((every[None, :] < chosen[:, None]) & coming[None, :]).astype(jnp.int32), axis=1
    )
    moved_terms = jnp.take(factors, placing, axis=1, mode="clip").reshape(
        pieces, slots_dev * head_count * quarter, SUBSPACE_EXTENT
    )
    columns = head_count * quarter
    final_state = rebuild_state(
        moved_state.reshape(slots_dev * columns, -1), moved_terms, steps
    ).reshape(slots_dev, columns, -1)
    return (produced[:STEPS_A], produced[STEPS_A:], final_state)


def solution(mesh):
    in_specs = (
        P(None, "groups", "batch"),
        P("groups", "batch"),
        P(("groups", "batch"), "head", None),
        P("groups"),
        P(None, "batch"),
        P("batch", None),
        P(None, None, "batch"),
        P(None, "batch", "head"),
        P("batch", None),
        P(None, "head"),
        P("head"),
        P("head"),
        P("head"),
        P("head"),
        P("head", "batch"),
    )
    out_specs = (
        P(None, ("groups", "head"), "batch"),
        P(None, ("groups", "head"), "batch"),
        P(("groups", "batch", "head"), None, None),
    )
    return jax.shard_map(
        per_device, mesh=mesh, in_specs=in_specs, out_specs=out_specs, check_vma=False
    )
```

```python
import functools

import jax
import jax.numpy as jnp
from jax import lax
from jax.experimental import pallas as pl
from jax.experimental.pallas import tpu as pltpu
from jax.sharding import PartitionSpec as P

SUBSPACE_EXTENT = 64
STEPS_A = 2
MIX_MAPS = 5
NORMALIZER_GUARD = 0.00064


def index_of(values, count):
    positions = jnp.arange(values.shape[0], dtype=jnp.int32)
    wanted = jnp.arange(count, dtype=jnp.int32)
    return jnp.sum(jnp.where(values[None, :] == wanted[:, None], positions[None, :], 0), axis=1)


def route_to_slots(value, position_mapping_target, batch_index, head_index, after=None):
    batch_count = lax.axis_size("batch")
    head_count = lax.axis_size("head")
    local_rows, heads_here, width = value.shape
    cluster_number = head_count // 4
    slots_dev = local_rows // cluster_number
    per_pair = slots_dev // batch_count
    quarter = heads_here // 4
    own_map = lax.dynamic_slice_in_dim(
        position_mapping_target, batch_index * local_rows, local_rows
    )
    dest_key = own_map // slots_dev
    positions = jnp.arange(local_rows, dtype=jnp.int32)
    ahead = (dest_key[None, :] < dest_key[:, None]) | (
        (dest_key[None, :] == dest_key[:, None]) & (positions[None, :] < positions[:, None])
    )
    send_order = index_of(jnp.sum(ahead.astype(jnp.int32), axis=1), local_rows)
    dest = jnp.arange(batch_count * head_count, dtype=jnp.int32)
    dest_block = (dest // head_count) * cluster_number + dest % cluster_number
    quad = (dest % head_count) // cluster_number
    pair = jnp.arange(per_pair, dtype=jnp.int32)
    within = jnp.arange(quarter, dtype=jnp.int32)
    sent_sessions = jnp.take(
        send_order, dest_block[:, None] * per_pair + pair[None, :], mode="clip"
    )
    sent_rows = (
        sent_sessions[:, :, None] * heads_here
        + (quad * quarter)[:, None, None]
        + within[None, None, :]
    )
    packed = jnp.take(
        value.reshape(local_rows * heads_here, width), sent_rows.reshape(-1), axis=0, mode="clip"
    ).reshape(batch_count * head_count, per_pair * quarter, width)
    if after is not None:
        packed, after = lax.optimization_barrier((packed, after))
    arrived = lax.all_to_all(packed, ("batch", "head"), split_axis=0, concat_axis=0, tiled=True)
    target = batch_index * cluster_number + head_index % cluster_number
    sessions = position_mapping_target.shape[0]
    chosen = lax.dynamic_slice_in_dim(
        index_of(position_mapping_target, sessions), target * slots_dev, slots_dev
    )
    every = jnp.arange(sessions, dtype=jnp.int32)
    coming = (position_mapping_target // slots_dev) == target
    placing = jnp.sum(
        ((every[None, :] < chosen[:, None]) & coming[None, :]).astype(jnp.int32), axis=1
    )
    source_head = jnp.arange(head_count, dtype=jnp.int32)
    kept_rows = (
        (
            (placing[:, None, None] // per_pair) * head_count + source_head[None, :, None]
        )
        * per_pair
        + placing[:, None, None] % per_pair
    ) * quarter + within[None, None, :]
    return jnp.take(
        arrived.reshape(-1, width), kept_rows.reshape(-1), axis=0, mode="clip"
    ).reshape(slots_dev, head_count * quarter, width)

def exchange_sum(pieces, axis_name):
    count = lax.axis_size(axis_name)
    index = lax.axis_index(axis_name)

    def own(shift):
        return jax.tree.map(
            lambda value: lax.dynamic_index_in_dim(value, (index + shift) % count, keepdims=False),
            pieces,
        )

    total = jax.tree.map(lambda value: value.astype(jnp.float32), own(0))
    for shift in range(1, count):
        arrived = lax.ppermute(
            own(shift), axis_name, [(i, (i + shift) % count) for i in range(count)]
        )
        total = jax.tree.map(lambda acc, value: acc + value.astype(jnp.float32), total, arrived)
    return total

def exchange_copies(value, axis_name):
    count = lax.axis_size(axis_name)
    index = lax.axis_index(axis_name)
    received = [value]
    for shift in range(1, count):
        received.append(
            lax.ppermute(value, axis_name, [(i, (i + shift) % count) for i in range(count)])
        )
    shifts = (index - jnp.arange(count, dtype=jnp.int32)) % count
    return jnp.take(jnp.stack(received), shifts, axis=0, mode="clip")

def by_source(received, index, count):
    shifts = (index - jnp.arange(count, dtype=jnp.int32)) % count
    return jnp.take(jnp.stack(received), shifts, axis=0, mode="clip")


def gather_with_parts(value, parts, axis_name):
    count = lax.axis_size(axis_name)
    index = lax.axis_index(axis_name)
    copies = [value]
    moved = [lax.dynamic_index_in_dim(parts, index, keepdims=False)]
    for shift in range(1, count):
        sent = lax.dynamic_index_in_dim(parts, (index + shift) % count, keepdims=False)
        copy, part = lax.ppermute(
            (value, sent), axis_name, [(i, (i + shift) % count) for i in range(count)]
        )
        copies.append(copy)
        moved.append(part)
    return by_source(copies, index, count), by_source(moved, index, count)


def sum_with_parts(pieces, parts, axis_name):
    count = lax.axis_size(axis_name)
    index = lax.axis_index(axis_name)
    total = lax.dynamic_index_in_dim(pieces, index, keepdims=False).astype(jnp.float32)
    moved = [lax.dynamic_index_in_dim(parts, index, keepdims=False)]
    for shift in range(1, count):
        target = (index + shift) % count
        piece, part = lax.ppermute(
            (
                lax.dynamic_index_in_dim(pieces, target, keepdims=False),
                lax.dynamic_index_in_dim(parts, target, keepdims=False),
            ),
            axis_name,
            [(i, (i + shift) % count) for i in range(count)],
        )
        total = total + piece.astype(jnp.float32)
        moved.append(part)
    return total, by_source(moved, index, count)


def widen(value):
    return value.astype(jnp.bfloat16).astype(jnp.float32)


def fill_tables(spread_ref, tile_ref=None):
    extent = SUBSPACE_EXTENT

    @pl.when(pl.program_id(0) == 0)
    def _():
        lane = lax.broadcasted_iota(jnp.int32, spread_ref.shape, 1)
        row = lax.broadcasted_iota(jnp.int32, spread_ref.shape, 0)
        spread_ref[...] = (lane // extent == row).astype(spread_ref.dtype)
        if tile_ref is not None:
            tile_ref[...] = (lane % extent == row).astype(tile_ref.dtype)


def recurrence_kernel(
    steps,
    recept_ref,
    key_ref,
    value_ref,
    decay_ref,
    gate_ref,
    params_ref,
    state_ref,
    mixed_ref,
    payload_ref,
    spread_ref,
):
    extent = SUBSPACE_EXTENT
    fill_tables(spread_ref)
    spread = spread_ref[...]
    state = state_ref[...]
    premium = params_ref[0]
    gain = params_ref[1]
    bias = params_ref[2]
    recept = [recept_ref[t] for t in range(steps)]
    key_vec = [key_ref[t] for t in range(steps)]
    valued = [value_ref[t] for t in range(steps)]
    decay_rate = [decay_ref[t] for t in range(steps)]
    flat = state.shape[-1]
    prefix = jnp.ones_like(recept[0])
    for t in range(steps):
        query = recept[t] * prefix
        high = query.astype(jnp.bfloat16)
        rest = query - high.astype(jnp.float32)
        middle = rest.astype(jnp.bfloat16)
        low = (rest - middle.astype(jnp.float32)).astype(jnp.bfloat16)
        rows = query.shape[0]
        spread_parts = jnp.dot(
            jnp.concatenate([high, middle, low], axis=0), spread, preferred_element_type=jnp.float32
        )
        spread_query = (
            spread_parts[:rows] + spread_parts[rows : 2 * rows] + spread_parts[2 * rows :]
        )
        weighted = spread_query * state
        folded = weighted[:, 0:128]
        for c in range(1, flat // 128):
            folded = folded + weighted[:, 128 * c : 128 * (c + 1)]
        from_state = folded[:, :extent] + folded[:, extent:]
        bonus_term = jnp.sum(recept[t] * premium * key_vec[t], axis=-1, keepdims=True)
        total = bonus_term * valued[t] + from_state
        for s in range(t):
            factor = key_vec[s]
            for u in range(s + 1, t):
                factor = factor * decay_rate[u]
            total = total + jnp.sum(recept[t] * factor, axis=-1, keepdims=True) * valued[s]
        average = jnp.mean(total, axis=-1, keepdims=True)
        demeaned = total - average
        spread_squared = jnp.mean(demeaned * demeaned, axis=-1, keepdims=True)
        standardized = demeaned * lax.rsqrt(spread_squared + NORMALIZER_GUARD) * gain + bias
        mixed_ref[t] = (standardized * gate_ref[t]).astype(mixed_ref.dtype)
        prefix = prefix * decay_rate[t]
    payload_ref[0] = prefix.astype(payload_ref.dtype)
    for s in range(steps):
        factor = key_vec[s]
        for u in range(s + 1, steps):
            factor = factor * decay_rate[u]
        payload_ref[1 + s] = factor.astype(payload_ref.dtype)
        payload_ref[1 + steps + s] = valued[s].astype(payload_ref.dtype)


def row_block(rows):
    return 64 if rows % 64 == 0 else rows


def run_recurrence(projected, params, state):
    pieces = len(projected)
    steps, rows, extent = projected[0].shape
    flat = state.shape[-1]
    block = row_block(rows)
    return pl.pallas_call(
        functools.partial(recurrence_kernel, steps),
        grid=(rows // block,),
        in_specs=[
            *[pl.BlockSpec((steps, block, extent), lambda n: (0, n, 0))] * pieces,
            pl.BlockSpec((3, block, extent), lambda n: (0, 0, 0)),
            pl.BlockSpec((block, flat), lambda n: (n, 0)),
        ],
        out_specs=[
            pl.BlockSpec((steps, block, extent), lambda n: (0, n, 0)),
            pl.BlockSpec((1 + 2 * steps, block, extent), lambda n: (0, n, 0)),
        ],
        out_shape=[
            jax.ShapeDtypeStruct((steps, rows, extent), jnp.bfloat16),
            jax.ShapeDtypeStruct((1 + 2 * steps, rows, extent), jnp.bfloat16),
        ],
        scratch_shapes=[pltpu.VMEM((extent, flat), jnp.bfloat16)],
        cost_estimate=pl.CostEstimate(
            flops=2 * rows * extent * flat * 3 * steps,
            transcendentals=steps * rows,
            bytes_accessed=rows * (flat * 4 + extent * (pieces * steps * 4 + 3 * 4 + steps * 2 + (1 + 2 * steps) * 2)),
        ),
    )(*projected, params, state)


def rebuild_kernel(steps, state_ref, terms_ref, out_ref, spread_ref, tile_ref):
    fill_tables(spread_ref, tile_ref)
    spread = spread_ref[...]
    tile = tile_ref[...]
    total = jnp.dot(terms_ref[0], spread, preferred_element_type=jnp.float32) * state_ref[...].astype(
        jnp.float32
    )
    for s in range(steps):
        total = total + jnp.dot(
            terms_ref[1 + s], spread, preferred_element_type=jnp.float32
        ) * jnp.dot(terms_ref[1 + steps + s], tile, preferred_element_type=jnp.float32)
    out_ref[...] = total


def rebuild_state(moved_state, moved_terms, steps):
    rows, flat = moved_state.shape
    pieces = moved_terms.shape[0]
    extent = SUBSPACE_EXTENT
    block = row_block(rows)
    return pl.pallas_call(
        functools.partial(rebuild_kernel, steps),
        grid=(rows // block,),
        in_specs=[
            pl.BlockSpec((block, flat), lambda n: (n, 0)),
            pl.BlockSpec((pieces, block, extent), lambda n: (0, n, 0)),
        ],
        out_specs=pl.BlockSpec((block, flat), lambda n: (n, 0)),
        out_shape=jax.ShapeDtypeStruct((rows, flat), jnp.float32),
        scratch_shapes=[
            pltpu.VMEM((extent, flat), jnp.bfloat16),
            pltpu.VMEM((extent, flat), jnp.bfloat16),
        ],
        cost_estimate=pl.CostEstimate(
            flops=2 * rows * extent * flat * (1 + 2 * steps),
            transcendentals=0,
            bytes_accessed=rows * (flat * 6 + pieces * extent * 2),
        ),
    )(moved_state, moved_terms)


def per_device(
    tier_feed_tensor,
    preceding_feed_each_stream,
    stream_kept_tableaux,
    position_mapping_target,
    lagging_mixture_weights,
    lagging_narrow_lowering,
    lagging_narrow_raising,
    fourfold_linear_maps,
    attenuation_narrow_lowering,
    attenuation_narrow_raising,
    attenuation_doublelog_anchor,
    instant_premium,
    norming_multiplier,
    norming_intercept,
    outgoing_linear_map,
):
    batch_count = lax.axis_size("batch")
    batch_index = lax.axis_index("batch")
    head_index = lax.axis_index("head")
    steps, sessions, feats = tier_feed_tensor.shape
    local_rows = sessions // batch_count
    heads_here = stream_kept_tableaux.shape[1]
    width = heads_here * SUBSPACE_EXTENT
    f32 = jnp.float32
    bf16 = jnp.bfloat16


    previous = jnp.concatenate([preceding_feed_each_stream[None], tier_feed_tensor[:-1]], axis=0)

    def by_block(value):
        return value.reshape(steps, batch_count, local_rows, feats).transpose(1, 0, 2, 3).reshape(
            batch_count * steps * local_rows, feats
        )

    x_float = by_block(tier_feed_tensor).astype(f32)
    shifted = by_block(previous).astype(f32) - x_float
    rows = x_float.shape[0]
    base_mix = (x_float + shifted * lagging_mixture_weights[0]).astype(bf16)
    partial_value = jnp.dot(base_mix, lagging_narrow_lowering, preferred_element_type=f32)
    hidden = jnp.tanh(
        jnp.sum(exchange_copies(partial_value.astype(bf16), "batch").astype(f32), axis=0)
    ).astype(bf16)
    hidden = hidden.reshape(rows, MIX_MAPS, lagging_narrow_raising.shape[1])
    offsets = jnp.einsum(
        "nim,imd->ind", hidden, lagging_narrow_raising, preferred_element_type=f32
    )
    mixed = (
        x_float[None] + shifted[None] * (lagging_mixture_weights[1:, None, :] + offsets)
    ).astype(bf16)
    main_part = jnp.einsum(
        "inf,ifc->inc", mixed[:4], fourfold_linear_maps, preferred_element_type=f32
    )
    decay_part = jnp.dot(mixed[4], attenuation_narrow_lowering, preferred_element_type=f32)
    main_sum, decay_sum = exchange_sum(
        (
            main_part.astype(bf16)
            .reshape(4, batch_count, steps * local_rows, width)
            .transpose(1, 0, 2, 3),
            decay_part.astype(bf16).reshape(batch_count, steps * local_rows, -1),
        ),
        "batch",
    )

    moved_state = route_to_slots(
        stream_kept_tableaux.astype(bf16),
        position_mapping_target,
        batch_index,
        head_index,
        after=(main_sum, decay_sum),
    )

    def heads_of(value):
        return value.reshape(steps, local_rows, heads_here, SUBSPACE_EXTENT)

    main_sum = main_sum.reshape(4, steps, local_rows, width)
    recept = heads_of(widen(main_sum[0]))
    key_vec = heads_of(widen(main_sum[1]))
    valued = heads_of(widen(main_sum[2]))
    gate_act = jax.nn.silu(main_sum[3])
    low_rank = jnp.tanh(decay_sum.reshape(steps, local_rows, -1)).astype(bf16)
    decay_rate = heads_of(
        jnp.exp(
            -jnp.exp(
                attenuation_doublelog_anchor
                + jnp.dot(low_rank, attenuation_narrow_raising, preferred_element_type=f32)
            )
        )
    )
    rows_here = local_rows * heads_here

    def by_row(value):
        return value.reshape(steps, rows_here, SUBSPACE_EXTENT)

    projected = tuple(by_row(value) for value in (recept, key_vec, valued, decay_rate, gate_act))
    params = jnp.tile(
        jnp.stack([instant_premium, norming_multiplier, norming_intercept]).reshape(
            3, heads_here, SUBSPACE_EXTENT
        ),
        (1, row_block(rows_here) // heads_here, 1),
    )
    mixed_rows, payload = run_recurrence(
        projected, params, stream_kept_tableaux.reshape(rows_here, -1)
    )
    moved_state, mixed_rows, payload = lax.optimization_barrier((moved_state, mixed_rows, payload))
    combined_response = mixed_rows.reshape(steps, local_rows, width)
    pieces = payload.shape[0]
    head_count = lax.axis_size("head")
    cluster_number = head_count // 4
    slots_dev = local_rows // cluster_number
    per_pair = slots_dev // batch_count
    quarter = heads_here // 4
    own_map = lax.dynamic_slice_in_dim(
        position_mapping_target, batch_index * local_rows, local_rows
    )
    dest_key = own_map // slots_dev
    positions = jnp.arange(local_rows, dtype=jnp.int32)
    ahead = (dest_key[None, :] < dest_key[:, None]) | (
        (dest_key[None, :] == dest_key[:, None]) & (positions[None, :] < positions[:, None])
    )
    send_order = index_of(jnp.sum(ahead.astype(jnp.int32), axis=1), local_rows)
    factors = jnp.take(
        payload.reshape(pieces, local_rows, heads_here, SUBSPACE_EXTENT),
        send_order,
        axis=1,
        mode="clip",
    ).reshape(pieces, batch_count, cluster_number * per_pair, heads_here, SUBSPACE_EXTENT)
    gathered, factors = gather_with_parts(
        combined_response, factors.transpose(1, 0, 2, 3, 4), "batch"
    )
    gathered = gathered.transpose(1, 0, 2, 3).reshape(steps, sessions, width)
    factors = factors.reshape(
        batch_count, pieces, cluster_number, per_pair, 4, quarter, SUBSPACE_EXTENT
    ).transpose(4, 2, 0, 1, 3, 5, 6)
    factors = factors.reshape(
        head_count, batch_count, pieces, per_pair, quarter, SUBSPACE_EXTENT
    )
    inverse = index_of(position_mapping_target, sessions)
    arranged = jnp.concatenate(
        [gathered[:STEPS_A], jnp.take(gathered[STEPS_A:], inverse, axis=1, mode="clip")], axis=0
    )
    partial_y = jnp.einsum(
        "tnf,fo->tno", arranged, outgoing_linear_map, preferred_element_type=f32
    ).astype(bf16)
    produced, factors = sum_with_parts(
        partial_y.reshape(steps, head_count, sessions // head_count, -1).transpose(1, 0, 2, 3),
        factors,
        "head",
    )
    produced = produced.astype(bf16)
    factors = factors.transpose(2, 1, 3, 0, 4, 5).reshape(
        pieces, batch_count * per_pair, head_count * quarter, SUBSPACE_EXTENT
    )
    target = batch_index * cluster_number + head_index % cluster_number
    chosen = lax.dynamic_slice_in_dim(inverse, target * slots_dev, slots_dev)
    every = jnp.arange(sessions, dtype=jnp.int32)
    coming = (position_mapping_target // slots_dev) == target
    placing = jnp.sum(
        ((every[None, :] < chosen[:, None]) & coming[None, :]).astype(jnp.int32), axis=1
    )
    moved_terms = jnp.take(factors, placing, axis=1, mode="clip").reshape(
        pieces, slots_dev * head_count * quarter, SUBSPACE_EXTENT
    )
    columns = head_count * quarter
    final_state = rebuild_state(
        moved_state.reshape(slots_dev * columns, -1), moved_terms, steps
    ).reshape(slots_dev, columns, -1)
    return (produced[:STEPS_A], produced[STEPS_A:], final_state)


def solution(mesh):
    in_specs = (
        P(None, "groups", "batch"),
        P("groups", "batch"),
        P(("groups", "batch"), "head", None),
        P("groups"),
        P(None, "batch"),
        P("batch", None),
        P(None, None, "batch"),
        P(None, "batch", "head"),
        P("batch", None),
        P(None, "head"),
        P("head"),
        P("head"),
        P("head"),
        P("head"),
        P("head", "batch"),
    )
    out_specs = (
        P(None, ("groups", "head"), "batch"),
        P(None, ("groups", "head"), "batch"),
        P(("groups", "batch", "head"), None, None),
    )
    return jax.shard_map(
        per_device, mesh=mesh, in_specs=in_specs, out_specs=out_specs, check_vma=False
    )
```
